32 devices in a mesh: region: 8 (over z, y), station: 4 (over x, core).
Axes of the slice: x: 2, y: 2, z: 4, core: 2. Of those that a mesh axis runs over, the one named last changes fastest.
Arguments:
- waveforms: bfloat16 [128, 16, 3, 512], P('region', 'station'), may hold values from -6 to 6
- pair_lists: int32 [3, 256, 2], P(None, 'region'), may hold values from 0 to 15
- pair_counts: int32 [3, 8], P(None, 'region'), may hold values from 1 to 32, as said below
Outputs:
- correlations: float32 [3, 256, 256], P(None, ('region', 'station'))
The draws below stay inside these ranges and needn't reach their ends.
Inputs may be any that keep to these rules, and one draw needn't show every extreme that they name: `pair_counts`: in every round some region has all 32 slots live.
All inputs are finite; a program needn't handle non-finite values.
Results may differ from the reference program's by a relative error of at most 0.011.
Values may be sent and summed in bfloat16 or wider, within the bound.
No kernel may reach another device: no remote copies, remote signals or barrier semaphores. Data moves between devices by JAX's collectives and lax.ppermute only.
A program may use at most 64 MiB of HBM per device.

```python
import math
import jax
import jax.numpy as jnp
from jax import lax

STATIONS = 16
COMP = 3
SAMPLES = 512
ROUNDS = 3
EV_DEV = 16
PAIR_DEV = 32
LAGS = 256
REGIONS = 8
EVENTS = 128
PAIRS = 256
N_REGION = 8
N_STATION = 4


def draw_pair_counts(key, part):
    first_key, second_key = jax.random.split(jax.random.fold_in(key, 7))
    counts = jax.random.randint(first_key, (ROUNDS, REGIONS), 1, PAIR_DEV + 1)
    fullest = jax.random.randint(second_key, (ROUNDS, 1), 0, REGIONS)
    region_ids = jnp.arange(REGIONS, dtype=jnp.int32)[None, :]
    return jnp.where(region_ids == fullest, PAIR_DEV, counts).astype(jnp.int32)


def place_ends(drawn, key, smallest, top_value):
    shape = drawn.shape
    place = [jax.random.randint(jax.random.fold_in(key, axis), (), 0, shape[axis]) for axis in range(len(shape))]
    drawn = drawn.at[tuple(place)].set(smallest)
    longest = shape.index(max(shape))
    place[longest] = (place[longest] + 1) % shape[longest]
    return drawn.at[tuple(place)].set(top_value)


def block_levels(rng, shape, cuts, least, high):
    gain = 1.0
    for axis_at, shards_of in cuts:
        heights = jax.random.uniform(jax.random.fold_in(jax.random.fold_in(rng, 6), axis_at), (shards_of,), jnp.float32, least / len(cuts), high / len(cuts))
        gain = gain * jnp.repeat(jnp.exp(heights), shape[axis_at] // shards_of).reshape((-1,) + (1,) * (len(shape) - 1 - axis_at))
    return gain


def normal_values(key, dims, scale, limit, cuts=(), kind=jnp.bfloat16):
    values = scale * jax.random.normal(key, dims, jnp.float32)
    if cuts:
        values = values * block_levels(key, dims, cuts, -0.22, 0.18)
    return jnp.clip(values, -limit, limit).astype(kind)


def setup_inputs(seed: int = 0) -> dict:
    key_of = jax.random.split(jax.random.key(seed), 4)
    return {
        "waveforms": normal_values(key_of[0], (EVENTS, STATIONS, COMP, SAMPLES), 1.0, 6.0, ((0, 8), (1, 4))),
        "pair_lists": place_ends(jax.random.randint(key_of[1], (ROUNDS, PAIRS, 2), 0, EV_DEV), jax.random.fold_in(key_of[1], 1), 0, EV_DEV - 1).astype(jnp.int32),
        "pair_counts": draw_pair_counts(jax.random.fold_in(key_of[3], 71), 0),
    }


TWO_PI = 2.0 * math.pi
EPS = 1e-06

def forward_table(length):
    period = 2 * length
    times = jnp.arange(length, dtype=jnp.int32)[:, None]
    freqs = jnp.arange(period, dtype=jnp.int32)[None, :]
    angle = TWO_PI / period * (times * freqs % period).astype(jnp.float32)
    return jnp.concatenate([jnp.cos(angle), -jnp.sin(angle)], axis=1).astype(jnp.bfloat16)

def inverse_table(length, channels):
    period = 2 * length
    half = length // 2
    freqs = jnp.arange(period, dtype=jnp.int32)[:, None]
    lagged = jnp.arange(half, dtype=jnp.int32)[None, :] - half // 2
    angle = TWO_PI / period * (freqs * lagged % period).astype(jnp.float32)
    factor = 1.0 / (period * math.sqrt(channels * length))
    return (jnp.concatenate([jnp.cos(angle), -jnp.sin(angle)], axis=0) * factor).astype(jnp.bfloat16)

def spectra_of(block):
    events, stations, comps, length = block.shape
    traces = block.astype(jnp.float32)
    traces = traces - lax.optimization_barrier(jnp.mean(traces, axis=-1, keepdims=True))
    traces = traces * lax.rsqrt(lax.optimization_barrier(jnp.mean(traces * traces, axis=-1, keepdims=True)) + EPS)
    traces = traces.astype(jnp.bfloat16).reshape(events * stations * comps, length)
    spec = jnp.dot(traces, forward_table(length), preferred_element_type=jnp.float32)
    return spec.astype(jnp.bfloat16).reshape(events, stations * comps, 4 * length)

def cross_curves(left, right, groups, lag_table):
    slots, channels, width = left.shape
    period = width // 2
    left_parts = left.reshape(slots, groups, channels // groups, 2, period).astype(jnp.float32)
    right_parts = right.reshape(slots, groups, channels // groups, 2, period).astype(jnp.float32)
    rotated = jnp.stack([right_parts[:, :, :, 1], -right_parts[:, :, :, 0]], axis=3)
    real_part = jnp.einsum('pgchk,pgchk->pgk', left_parts, right_parts)
    imag_part = jnp.einsum('pgchk,pgchk->pgk', left_parts, rotated)
    cross = jnp.concatenate([real_part, imag_part], axis=-1).astype(jnp.bfloat16)
    return jnp.einsum('pgf,fl->pl', cross.astype(jnp.float32), lag_table.astype(jnp.float32))

def reference(waveforms, pair_lists, pair_counts):
    blocks = waveforms.reshape(N_REGION, EV_DEV, STATIONS, COMP, SAMPLES)
    spectra = lax.map(spectra_of, blocks)
    lag_table = inverse_table(SAMPLES, STATIONS * COMP)
    outputs = []
    for round_index in range(ROUNDS):

        def region_block(region_id, round_index=round_index):
            partner = jnp.bitwise_xor(region_id, jnp.int32(1 << round_index))
            pair_rows = lax.dynamic_slice_in_dim(pair_lists[round_index], (region_id * PAIR_DEV).astype(jnp.int32), PAIR_DEV, 0)
            left = jnp.take(spectra[region_id], pair_rows[:, 0], axis=0)
            right = jnp.take(spectra[partner], pair_rows[:, 1], axis=0)
            curves = cross_curves(left, right, N_STATION, lag_table)
            live = jnp.arange(PAIR_DEV, dtype=jnp.int32) < pair_counts[round_index, region_id]
            return jnp.where(live[:, None], curves, jnp.zeros_like(curves))
        result = lax.map(region_block, jnp.arange(N_REGION, dtype=jnp.int32))
        outputs.append(result.reshape(PAIRS, LAGS))
    return jnp.stack(outputs)
```

```python
import math

import ml_dtypes
import numpy as np

import jax
import jax.numpy as jnp
from jax import lax
from jax.experimental import pallas as pl
from jax.experimental.pallas import tpu as pltpu
from jax.sharding import PartitionSpec as P

EPS = 1e-06
LAGS = 256


def swapped(block, axis, bit):
    count = lax.axis_size(axis)
    route = []
    for low in range(count):
        high = low | 1 << bit
        if high != low and high < count:
            route += [(low, high), (high, low)]
    return lax.ppermute(block, axis, route)


def half_tables(length, channels, lags):
    period = 2 * length
    half = period // 2
    step = np.float32(2.0 * math.pi / period)
    times = np.arange(length, dtype=np.int64)[:, None]
    freqs = np.arange(half, dtype=np.int64)[None, :]
    angle = step * ((times * freqs) % period).astype(np.float32)
    fwd = np.concatenate([np.cos(angle), -np.sin(angle)], axis=1).astype(np.float32)
    fwd[:, half] = np.where(times[:, 0] % 2 == 0, 1.0, -1.0)
    fwd = fwd.astype(ml_dtypes.bfloat16)

    factor = np.float32(1.0 / (period * math.sqrt(channels * length)))
    rows = np.arange(half, dtype=np.int64)[:, None]
    lagged = np.arange(lags, dtype=np.int64)[None, :] - lags // 2
    angle = step * ((rows * lagged) % period).astype(np.float32)
    cos_t = (np.cos(angle).astype(np.float32) * factor).astype(ml_dtypes.bfloat16).astype(np.float32)
    sin_t = ((-np.sin(angle)).astype(np.float32) * factor).astype(ml_dtypes.bfloat16).astype(np.float32)
    inv = np.zeros((period, lags), np.float32)
    inv[0] = cos_t[0]
    inv[1:half] = 2.0 * cos_t[1:]
    nyq_angle = step * ((half * lagged[0]) % period).astype(np.float32)
    inv[half] = (np.cos(nyq_angle).astype(np.float32) * factor).astype(ml_dtypes.bfloat16).astype(np.float32)
    inv[half + 1:] = 2.0 * sin_t[1:]
    return fwd, inv.astype(ml_dtypes.bfloat16)


def make_round_kernel(events, chans, pad, length, slots, groups, share):
    half = length

    def kernel(pl_ref, cnt_ref, sid_ref, wl_ref, wp_ref, f_ref, g_ref, out_ref,
               nscr, xpad, specl, specp, cross):
        xpad[...] = jnp.zeros(xpad.shape, jnp.float32)

        def spectra(w_ref, spec_ref):
            x = w_ref[...].astype(jnp.float32)
            x = x - jnp.mean(x, axis=-1, keepdims=True)
            x = x * lax.rsqrt(jnp.mean(x * x, axis=-1, keepdims=True) + EPS)
            nscr[...] = x
            for e in range(events):
                xpad[e * pad:e * pad + chans, :] = nscr[e * chans:(e + 1) * chans, :]
            xb = xpad[...].astype(jnp.bfloat16)
            spec = jnp.dot(xb, f_ref[...], preferred_element_type=jnp.float32)
            spec_ref[...] = spec.astype(jnp.bfloat16).astype(jnp.float32)

        spectra(wl_ref, specl)
        spectra(wp_ref, specp)

        sid = sid_ref[0]
        lane = lax.broadcasted_iota(jnp.int32, (1, 128), 1)
        for r in range(slots):
            d, ip = divmod(r, share)
            slot = ((sid + d) % groups) * share + ip
            a = jnp.minimum(jnp.maximum(pl_ref[2 * slot], 0), events - 1)
            b = jnp.minimum(jnp.maximum(pl_ref[2 * slot + 1], 0), events - 1)
            left = specl[pl.ds(pl.multiple_of(a * pad, pad), pad), :]
            right = specp[pl.ds(pl.multiple_of(b * pad, pad), pad), :]
            lr, li = left[:, :half], left[:, half:]
            rr, ri = right[:, :half], right[:, half:]
            pp = lr * rr
            qq = li * ri
            re = jnp.sum(pp + qq, axis=0, keepdims=True)
            im = jnp.sum(lr * ri - li * rr, axis=0, keepdims=True)
            p0 = jnp.sum(pp[:, :128], axis=0, keepdims=True)
            q0 = jnp.sum(qq[:, :128], axis=0, keepdims=True)
            cross[r:r + 1, 0:128] = jnp.where(lane == 0, p0, re[:, :128])
            cross[r:r + 1, 128:half] = re[:, 128:]
            cross[r:r + 1, half:half + 128] = jnp.where(lane == 0, q0, im[:, :128])
            cross[r:r + 1, half + 128:] = im[:, 128:]

        cb = cross[...].astype(jnp.bfloat16)
        corr = jnp.dot(cb, g_ref[...], preferred_element_type=jnp.float32)
        rows = lax.broadcasted_iota(jnp.int32, corr.shape, 0)
        slot_of = ((sid + rows // share) % groups) * share + rows % share
        out_ref[...] = jnp.where(slot_of < cnt_ref[0], corr, 0.0)

    return kernel


def round_call(pairs, count, sid, local, partner, fwd, inv, events, chans, slots, groups):
    length = fwd.shape[0]
    pad = 16
    share = slots // groups
    kernel = make_round_kernel(events, chans, pad, length, slots, groups, share)
    smem = pl.BlockSpec(memory_space=pltpu.SMEM)
    vmem = pl.BlockSpec(memory_space=pltpu.VMEM)
    return pl.pallas_call(
        kernel,
        out_shape=jax.ShapeDtypeStruct((slots, inv.shape[1]), jnp.float32),
        in_specs=[smem, smem, smem, vmem, vmem, vmem, vmem],
        out_specs=vmem,
        scratch_shapes=[
            pltpu.VMEM((events * chans, length), jnp.float32),
            pltpu.VMEM((events * pad, length), jnp.float32),
            pltpu.VMEM((events * pad, 2 * length), jnp.float32),
            pltpu.VMEM((events * pad, 2 * length), jnp.float32),
            pltpu.VMEM((slots, 2 * length), jnp.float32),
        ],
    )(pairs, count, sid, local, partner, fwd, inv)


def shards(waveforms, pair_lists, pair_counts):
    events, stations, comps, length = waveforms.shape
    groups = lax.axis_size("station")
    rounds, slots, _ = pair_lists.shape
    chans = stations * comps
    fwd_np, inv_np = half_tables(length, stations * groups * comps, LAGS)
    fwd = jnp.asarray(fwd_np)
    inv = jnp.asarray(inv_np)
    flat = waveforms.reshape(events * chans, length)
    sid = lax.axis_index("station").astype(jnp.int32).reshape(1)
    share = slots // groups
    outs = []
    for q in range(rounds):
        partner = swapped(flat, "region", q)
        outs.append(
            round_call(pair_lists[q].reshape(-1), pair_counts[q], sid, flat, partner, fwd, inv,
                       events, chans, slots, groups)
        )
    stacked = jnp.stack(outs).reshape(rounds, groups, share, LAGS)
    total = stacked[:, 0]
    for d in range(1, groups):
        perm = [(s, (s + d) % groups) for s in range(groups)]
        got = lax.ppermute(stacked[:, d].astype(jnp.bfloat16), "station", perm)
        total = total + got.astype(jnp.float32)
    return total


def solution(mesh):
    return jax.shard_map(
        shards,
        mesh=mesh,
        in_specs=(P("region", "station", None, None), P(None, "region", None), P(None, "region")),
        out_specs=P(None, ("region", "station"), None),
        check_vma=False,
    )
```

```python
import math

import ml_dtypes
import numpy as np

import jax
import jax.numpy as jnp
from jax import lax
from jax.experimental import pallas as pl
from jax.experimental.pallas import tpu as pltpu
from jax.sharding import PartitionSpec as P

EPS = 1e-06
LAGS = 256


def swapped(block, axis, bit):
    count = lax.axis_size(axis)
    route = []
    for low in range(count):
        high = low | 1 << bit
        if high != low and high < count:
            route += [(low, high), (high, low)]
    return lax.ppermute(block, axis, route)


def half_tables(length, channels, lags):
    period = 2 * length
    half = period // 2
    step = np.float32(2.0 * math.pi / period)
    times = np.arange(length, dtype=np.int64)[:, None]
    freqs = np.arange(half, dtype=np.int64)[None, :]
    angle = step * ((times * freqs) % period).astype(np.float32)
    fwd = np.concatenate([np.cos(angle), -np.sin(angle)], axis=1).astype(np.float32)
    fwd[:, half] = np.where(times[:, 0] % 2 == 0, 1.0, -1.0)
    fwd = fwd.astype(ml_dtypes.bfloat16)

    factor = np.float32(1.0 / (period * math.sqrt(channels * length)))
    rows = np.arange(half, dtype=np.int64)[:, None]
    lagged = np.arange(lags, dtype=np.int64)[None, :] - lags // 2
    angle = step * ((rows * lagged) % period).astype(np.float32)
    cos_t = (np.cos(angle).astype(np.float32) * factor).astype(ml_dtypes.bfloat16).astype(np.float32)
    sin_t = ((-np.sin(angle)).astype(np.float32) * factor).astype(ml_dtypes.bfloat16).astype(np.float32)
    inv = np.zeros((period, lags), np.float32)
    inv[0] = cos_t[0]
    inv[1:half] = 2.0 * cos_t[1:]
    nyq_angle = step * ((half * lagged[0]) % period).astype(np.float32)
    inv[half] = (np.cos(nyq_angle).astype(np.float32) * factor).astype(ml_dtypes.bfloat16).astype(np.float32)
    inv[half + 1:] = 2.0 * sin_t[1:]
    return fwd, inv.astype(ml_dtypes.bfloat16)


def make_kernel(events, chans, pad, length, slots, groups, share, rounds, first, from_waves):
    half = length
    n_part = len(rounds)

    def kernel(*refs):
        pl_ref, cnt_ref, sid_ref, own_ref = refs[:4]
        part_refs = refs[4:4 + n_part]
        f_ref, g_ref = refs[4 + n_part:6 + n_part]
        outs = refs[6 + n_part:]
        out_ref = outs[0]
        spec_out = outs[1] if from_waves else None
        nscr, xpad, specl, specp, cross = outs[1 + int(from_waves):]

        def spectra(w_ref, spec_ref):
            x = w_ref[...].astype(jnp.float32)
            x = x - jnp.mean(x, axis=-1, keepdims=True)
            x = x * lax.rsqrt(jnp.mean(x * x, axis=-1, keepdims=True) + EPS)
            nscr[...] = x
            for e in range(events):
                xpad[e * pad:e * pad + chans, :] = nscr[e * chans:(e + 1) * chans, :]
            xb = xpad[...].astype(jnp.bfloat16)
            spec = jnp.dot(xb, f_ref[...], preferred_element_type=jnp.float32)
            spec_ref[...] = spec.astype(jnp.bfloat16).astype(jnp.float32)

        xpad[...] = jnp.zeros(xpad.shape, jnp.float32)
        if from_waves:
            spectra(own_ref, specl)
            spec_out[...] = specl[...].astype(jnp.bfloat16)
        else:
            specl[...] = own_ref[...].astype(jnp.float32)

        sid = sid_ref[0]
        lane = lax.broadcasted_iota(jnp.int32, (1, 128), 1)
        for n, q in enumerate(rounds):
            spectra(part_refs[n], specp)
            base = q * slots * 2
            for r in range(slots):
                d, ip = divmod(r, share)
                slot = ((sid + d) % groups) * share + ip
                a = jnp.minimum(jnp.maximum(pl_ref[base + 2 * slot], 0), events - 1)
                b = jnp.minimum(jnp.maximum(pl_ref[base + 2 * slot + 1], 0), events - 1)
                left = specl[pl.ds(pl.multiple_of(a * pad, pad), pad), :]
                right = specp[pl.ds(pl.multiple_of(b * pad, pad), pad), :]
                lr, li = left[:, :half], left[:, half:]
                rr, ri = right[:, :half], right[:, half:]
                pp = lr * rr
                qq = li * ri
                re = jnp.sum(pp + qq, axis=0, keepdims=True)
                im = jnp.sum(lr * ri - li * rr, axis=0, keepdims=True)
                p0 = jnp.sum(pp[:, :128], axis=0, keepdims=True)
                q0 = jnp.sum(qq[:, :128], axis=0, keepdims=True)
                cross[r:r + 1, 0:128] = jnp.where(lane == 0, p0, re[:, :128])
                cross[r:r + 1, 128:half] = re[:, 128:]
                cross[r:r + 1, half:half + 128] = jnp.where(lane == 0, q0, im[:, :128])
                cross[r:r + 1, half + 128:] = im[:, 128:]

            cb = cross[...].astype(jnp.bfloat16)
            corr = jnp.dot(cb, g_ref[...], preferred_element_type=jnp.float32)
            rows = lax.broadcasted_iota(jnp.int32, corr.shape, 0)
            slot_of = ((sid + rows // share) % groups) * share + rows % share
            out_ref[n] = jnp.where(slot_of < cnt_ref[q], corr, 0.0)

    return kernel


def rounds_call(pairs, counts, sid, own, partners, fwd, inv, rounds, events, chans, slots, groups, from_waves):
    length = fwd.shape[0]
    pad = 16
    share = slots // groups
    kernel = make_kernel(events, chans, pad, length, slots, groups, share, rounds, rounds[0], from_waves)
    smem = pl.BlockSpec(memory_space=pltpu.SMEM)
    vmem = pl.BlockSpec(memory_space=pltpu.VMEM)
    out_shape = [jax.ShapeDtypeStruct((len(rounds), slots, inv.shape[1]), jnp.float32)]
    out_specs = [vmem]
    if from_waves:
        out_shape.append(jax.ShapeDtypeStruct((events * pad, 2 * length), jnp.bfloat16))
        out_specs.append(vmem)
    res = pl.pallas_call(
        kernel,
        out_shape=tuple(out_shape),
        in_specs=[smem, smem, smem] + [vmem] * (3 + len(partners)),
        out_specs=tuple(out_specs),
        scratch_shapes=[
            pltpu.VMEM((events * chans, length), jnp.float32),
            pltpu.VMEM((events * pad, length), jnp.float32),
            pltpu.VMEM((events * pad, 2 * length), jnp.float32),
            pltpu.VMEM((events * pad, 2 * length), jnp.float32),
            pltpu.VMEM((slots, 2 * length), jnp.float32),
        ],
    )(pairs, counts, sid, own, *partners, fwd, inv)
    return res


def station_sum(block, groups):
    total = block[:, 0]
    for d in range(1, groups):
        perm = [(s, (s + d) % groups) for s in range(groups)]
        got = lax.ppermute(block[:, d].astype(jnp.bfloat16), "station", perm)
        total = total + got.astype(jnp.float32)
    return total


def shards(waveforms, pair_lists, pair_counts):
    events, stations, comps, length = waveforms.shape
    groups = lax.axis_size("station")
    rounds, slots, _ = pair_lists.shape
    chans = stations * comps
    share = slots // groups
    fwd_np, inv_np = half_tables(length, stations * groups * comps, LAGS)
    fwd = jnp.asarray(fwd_np)
    inv = jnp.asarray(inv_np)
    flat = waveforms.reshape(events * chans, length)
    sid = lax.axis_index("station").astype(jnp.int32).reshape(1)
    pairs = pair_lists.reshape(-1)
    counts = pair_counts.reshape(-1)
    partners = [swapped(flat, "region", q) for q in range(rounds)]
    early = list(range(rounds - 1))
    corr_a, spec = rounds_call(pairs, counts, sid, flat, [partners[q] for q in early], fwd, inv,
                               early, events, chans, slots, groups, True)
    sum_a = station_sum(corr_a.reshape(len(early), groups, share, LAGS), groups)
    (corr_b,) = rounds_call(pairs, counts, sid, spec, [partners[-1]], fwd, inv,
                            [rounds - 1], events, chans, slots, groups, False)
    sum_b = station_sum(corr_b.reshape(1, groups, share, LAGS), groups)
    return jnp.concatenate([sum_a, sum_b], axis=0)


def solution(mesh):
    return jax.shard_map(
        shards,
        mesh=mesh,
        in_specs=(P("region", "station", None, None), P(None, "region", None), P(None, "region")),
        out_specs=P(None, ("region", "station"), None),
        check_vma=False,
    )
```

```python
import math

import ml_dtypes
import numpy as np

import jax
import jax.numpy as jnp
from jax import lax
from jax.experimental import pallas as pl
from jax.experimental.pallas import tpu as pltpu
from jax.sharding import PartitionSpec as P

EPS = 1e-06
LAGS = 256


def swapped(block, axis, bit):
    count = lax.axis_size(axis)
    route = []
    for low in range(count):
        high = low | 1 << bit
        if high != low and high < count:
            route += [(low, high), (high, low)]
    return lax.ppermute(block, axis, route)


def half_tables(length, channels, lags):
    period = 2 * length
    half = period // 2
    step = np.float32(2.0 * math.pi / period)
    times = np.arange(length, dtype=np.int64)[:, None]
    freqs = np.arange(half, dtype=np.int64)[None, :]
    angle = step * ((times * freqs) % period).astype(np.float32)
    fwd = np.concatenate([np.cos(angle), -np.sin(angle)], axis=1).astype(np.float32)
    fwd[:, half] = np.where(times[:, 0] % 2 == 0, 1.0, -1.0)
    fwd = fwd.astype(ml_dtypes.bfloat16)

    factor = np.float32(1.0 / (period * math.sqrt(channels * length)))
    rows = np.arange(half, dtype=np.int64)[:, None]
    lagged = np.arange(lags, dtype=np.int64)[None, :] - lags // 2
    angle = step * ((rows * lagged) % period).astype(np.float32)
    cos_t = (np.cos(angle).astype(np.float32) * factor).astype(ml_dtypes.bfloat16).astype(np.float32)
    sin_t = ((-np.sin(angle)).astype(np.float32) * factor).astype(ml_dtypes.bfloat16).astype(np.float32)
    inv = np.zeros((period, lags), np.float32)
    inv[0] = cos_t[0]
    inv[1:half] = 2.0 * cos_t[1:]
    nyq_angle = step * ((half * lagged[0]) % period).astype(np.float32)
    inv[half] = (np.cos(nyq_angle).astype(np.float32) * factor).astype(ml_dtypes.bfloat16).astype(np.float32)
    inv[half + 1:] = 2.0 * sin_t[1:]
    return fwd, inv.astype(ml_dtypes.bfloat16)


def make_kernel(events, chans, pad, length, slots, groups, share, rounds, n_prev, from_waves):
    half = length
    n_part = len(rounds)

    def kernel(*refs):
        pl_ref, cnt_ref, own_ref = refs[:3]
        part_refs = refs[3:3 + n_part]
        f_ref, g_ref = refs[3 + n_part:5 + n_part]
        rest = refs[5 + n_part:]
        if from_waves:
            out_ref, spec_out = rest[:2]
            rest = rest[2:]
        else:
            prev_ref, out_ref = rest[:2]
            rest = rest[2:]
        nscr, xpad, specl, specp, cross = rest

        def spectra(w_ref, spec_ref):
            x = w_ref[...].astype(jnp.float32)
            x = x - jnp.mean(x, axis=-1, keepdims=True)
            x = x * lax.rsqrt(jnp.mean(x * x, axis=-1, keepdims=True) + EPS)
            nscr[...] = x
            for e in range(events):
                xpad[e * pad:e * pad + chans, :] = nscr[e * chans:(e + 1) * chans, :]
            xb = xpad[...].astype(jnp.bfloat16)
            spec = jnp.dot(xb, f_ref[...], preferred_element_type=jnp.float32)
            spec_ref[...] = spec.astype(jnp.bfloat16).astype(jnp.float32)

        xpad[...] = jnp.zeros(xpad.shape, jnp.float32)
        if from_waves:
            spectra(own_ref, specl)
            spec_out[...] = specl[...].astype(jnp.bfloat16)
        else:
            specl[...] = own_ref[...].astype(jnp.float32)
            for n in range(n_prev):
                prev = prev_ref[n]
                for i in range(groups):
                    out_ref[i, n] = prev[i * share:(i + 1) * share].astype(jnp.bfloat16)

        lane = lax.broadcasted_iota(jnp.int32, (1, 128), 1)
        for n, q in enumerate(rounds):
            spectra(part_refs[n], specp)
            base = q * slots * 2
            for r in range(slots):
                a = jnp.minimum(jnp.maximum(pl_ref[base + 2 * r], 0), events - 1)
                b = jnp.minimum(jnp.maximum(pl_ref[base + 2 * r + 1], 0), events - 1)
                left = specl[pl.ds(pl.multiple_of(a * pad, pad), pad), :]
                right = specp[pl.ds(pl.multiple_of(b * pad, pad), pad), :]
                lr, li = left[:, :half], left[:, half:]
                rr, ri = right[:, :half], right[:, half:]
                pp = lr * rr
                qq = li * ri
                re = jnp.sum(pp + qq, axis=0, keepdims=True)
                im = jnp.sum(lr * ri - li * rr, axis=0, keepdims=True)
                p0 = jnp.sum(pp[:, :128], axis=0, keepdims=True)
                q0 = jnp.sum(qq[:, :128], axis=0, keepdims=True)
                cross[r:r + 1, 0:128] = jnp.where(lane == 0, p0, re[:, :128])
                cross[r:r + 1, 128:half] = re[:, 128:]
                cross[r:r + 1, half:half + 128] = jnp.where(lane == 0, q0, im[:, :128])
                cross[r:r + 1, half + 128:] = im[:, 128:]

            cb = cross[...].astype(jnp.bfloat16)
            corr = jnp.dot(cb, g_ref[...], preferred_element_type=jnp.float32)
            rows = lax.broadcasted_iota(jnp.int32, corr.shape, 0)
            corr = jnp.where(rows < cnt_ref[q], corr, 0.0)
            if from_waves:
                out_ref[n] = corr
            else:
                for i in range(groups):
                    out_ref[i, n_prev + n] = corr[i * share:(i + 1) * share].astype(jnp.bfloat16)

    return kernel


def rounds_call(pairs, counts, own, partners, fwd, inv, rounds, events, chans, slots, groups, prev=None):
    length = fwd.shape[0]
    lags = inv.shape[1]
    pad = 16
    share = slots // groups
    from_waves = prev is None
    n_prev = 0 if from_waves else prev.shape[0]
    kernel = make_kernel(events, chans, pad, length, slots, groups, share, rounds, n_prev, from_waves)
    smem = pl.BlockSpec(memory_space=pltpu.SMEM)
    vmem = pl.BlockSpec(memory_space=pltpu.VMEM)
    if from_waves:
        out_shape = (jax.ShapeDtypeStruct((len(rounds), slots, lags), jnp.float32),
                     jax.ShapeDtypeStruct((events * pad, 2 * length), jnp.bfloat16))
        extra = []
    else:
        out_shape = (jax.ShapeDtypeStruct((groups, n_prev + len(rounds), share, lags), jnp.bfloat16),)
        extra = [prev]
    return pl.pallas_call(
        kernel,
        out_shape=out_shape,
        in_specs=[smem, smem] + [vmem] * (3 + len(partners) + len(extra)),
        out_specs=tuple(vmem for _ in out_shape),
        scratch_shapes=[
            pltpu.VMEM((events * chans, length), jnp.float32),
            pltpu.VMEM((events * pad, length), jnp.float32),
            pltpu.VMEM((events * pad, 2 * length), jnp.float32),
            pltpu.VMEM((events * pad, 2 * length), jnp.float32),
            pltpu.VMEM((slots, 2 * length), jnp.float32),
        ],
    )(pairs, counts, own, *partners, fwd, inv, *extra)


def shards(waveforms, pair_lists, pair_counts):
    events, stations, comps, length = waveforms.shape
    groups = lax.axis_size("station")
    rounds, slots, _ = pair_lists.shape
    chans = stations * comps
    fwd_np, inv_np = half_tables(length, stations * groups * comps, LAGS)
    fwd = jnp.asarray(fwd_np)
    inv = jnp.asarray(inv_np)
    flat = waveforms.reshape(events * chans, length)
    pairs = pair_lists.reshape(-1)
    counts = pair_counts.reshape(-1)
    partners = [swapped(flat, "region", q) for q in range(rounds)]
    early = list(range(rounds - 1))
    corr_a, spec = rounds_call(pairs, counts, flat, [partners[q] for q in early], fwd, inv,
                               early, events, chans, slots, groups)
    (blocks,) = rounds_call(pairs, counts, spec, [partners[-1]], fwd, inv,
                            [rounds - 1], events, chans, slots, groups, prev=corr_a)
    got = lax.all_to_all(blocks, "station", 0, 0, tiled=True)
    return jnp.sum(got.astype(jnp.float32), axis=0)


def solution(mesh):
    return jax.shard_map(
        shards,
        mesh=mesh,
        in_specs=(P("region", "station", None, None), P(None, "region", None), P(None, "region")),
        out_specs=P(None, ("region", "station"), None),
        check_vma=False,
    )
```

```python
import math

import ml_dtypes
import numpy as np

import jax
import jax.numpy as jnp
from jax import lax
from jax.experimental import pallas as pl
from jax.experimental.pallas import tpu as pltpu
from jax.sharding import PartitionSpec as P

EPS = 1e-06
LAGS = 256


def swapped(block, axis, bit):
    count = lax.axis_size(axis)
    route = []
    for low in range(count):
        high = low | 1 << bit
        if high != low and high < count:
            route += [(low, high), (high, low)]
    return lax.ppermute(block, axis, route)


def half_tables(length, channels, lags):
    period = 2 * length
    half = period // 2
    step = np.float32(2.0 * math.pi / period)
    times = np.arange(length, dtype=np.int64)[:, None]
    freqs = np.arange(half, dtype=np.int64)[None, :]
    angle = step * ((times * freqs) % period).astype(np.float32)
    fwd = np.concatenate([np.cos(angle), -np.sin(angle)], axis=1).astype(np.float32)
    fwd[:, half] = np.where(times[:, 0] % 2 == 0, 1.0, -1.0)
    fwd = fwd.astype(ml_dtypes.bfloat16)

    factor = np.float32(1.0 / (period * math.sqrt(channels * length)))
    rows = np.arange(half, dtype=np.int64)[:, None]
    lagged = np.arange(lags, dtype=np.int64)[None, :] - lags // 2
    angle = step * ((rows * lagged) % period).astype(np.float32)
    cos_t = (np.cos(angle).astype(np.float32) * factor).astype(ml_dtypes.bfloat16).astype(np.float32)
    sin_t = ((-np.sin(angle)).astype(np.float32) * factor).astype(ml_dtypes.bfloat16).astype(np.float32)
    inv = np.zeros((period, lags), np.float32)
    inv[0] = cos_t[0]
    inv[1:half] = 2.0 * cos_t[1:]
    nyq_angle = step * ((half * lagged[0]) % period).astype(np.float32)
    inv[half] = (np.cos(nyq_angle).astype(np.float32) * factor).astype(ml_dtypes.bfloat16).astype(np.float32)
    inv[half + 1:] = 2.0 * sin_t[1:]
    return fwd, inv.astype(ml_dtypes.bfloat16)


def make_kernel(events, chans, pad, length, slots, groups, share, rounds, n_prev, from_waves):
    half = length
    n_part = len(rounds)

    def kernel(*refs):
        pl_ref, cnt_ref, sid_ref, own_ref = refs[:4]
        part_refs = refs[4:4 + n_part]
        f_ref, g_ref = refs[4 + n_part:6 + n_part]
        rest = refs[6 + n_part:]
        if from_waves:
            out_ref, spec_out = rest[:2]
            rest = rest[2:]
        else:
            prev_ref, out_ref = rest[:2]
            rest = rest[2:]
        nscr, xpad, specl, specp, cross = rest

        def spectra(w_ref, spec_ref):
            x = w_ref[...].astype(jnp.float32)
            x = x - jnp.mean(x, axis=-1, keepdims=True)
            x = x * lax.rsqrt(jnp.mean(x * x, axis=-1, keepdims=True) + EPS)
            nscr[...] = x
            for e in range(events):
                xpad[e * pad:e * pad + chans, :] = nscr[e * chans:(e + 1) * chans, :]
            xb = xpad[...].astype(jnp.bfloat16)
            spec = jnp.dot(xb, f_ref[...], preferred_element_type=jnp.float32)
            spec_ref[...] = spec.astype(jnp.bfloat16).astype(jnp.float32)

        xpad[...] = jnp.zeros(xpad.shape, jnp.float32)
        if from_waves:
            spectra(own_ref, specl)
            spec_out[...] = specl[...].astype(jnp.bfloat16)
        else:
            specl[...] = own_ref[...].astype(jnp.float32)
            for n in range(n_prev):
                out_ref[n] = prev_ref[n]

        sid = sid_ref[0]
        lane = lax.broadcasted_iota(jnp.int32, (1, 128), 1)
        for n, q in enumerate(rounds):
            spectra(part_refs[n], specp)
            base = q * slots * 2
            for r in range(slots):
                slot = (sid ^ (r // share)) * share + r % share
                a = jnp.minimum(jnp.maximum(pl_ref[base + 2 * slot], 0), events - 1)
                b = jnp.minimum(jnp.maximum(pl_ref[base + 2 * slot + 1], 0), events - 1)
                left = specl[pl.ds(pl.multiple_of(a * pad, pad), pad), :]
                right = specp[pl.ds(pl.multiple_of(b * pad, pad), pad), :]
                lr, li = left[:, :half], left[:, half:]
                rr, ri = right[:, :half], right[:, half:]
                pp = lr * rr
                qq = li * ri
                re = jnp.sum(pp + qq, axis=0, keepdims=True)
                im = jnp.sum(lr * ri - li * rr, axis=0, keepdims=True)
                p0 = jnp.sum(pp[:, :128], axis=0, keepdims=True)
                q0 = jnp.sum(qq[:, :128], axis=0, keepdims=True)
                cross[r:r + 1, 0:128] = jnp.where(lane == 0, p0, re[:, :128])
                cross[r:r + 1, 128:half] = re[:, 128:]
                cross[r:r + 1, half:half + 128] = jnp.where(lane == 0, q0, im[:, :128])
                cross[r:r + 1, half + 128:] = im[:, 128:]

            cb = cross[...].astype(jnp.bfloat16)
            corr = jnp.dot(cb, g_ref[...], preferred_element_type=jnp.float32)
            rows = lax.broadcasted_iota(jnp.int32, corr.shape, 0)
            slot_of = (sid ^ (rows // share)) * share + rows % share
            out_ref[n_prev + n] = jnp.where(slot_of < cnt_ref[q], corr, 0.0)

    return kernel


def rounds_call(pairs, counts, sid, own, partners, fwd, inv, rounds, events, chans, slots, groups, prev=None):
    length = fwd.shape[0]
    lags = inv.shape[1]
    pad = 16
    share = slots // groups
    from_waves = prev is None
    n_prev = 0 if from_waves else prev.shape[0]
    kernel = make_kernel(events, chans, pad, length, slots, groups, share, rounds, n_prev, from_waves)
    smem = pl.BlockSpec(memory_space=pltpu.SMEM)
    vmem = pl.BlockSpec(memory_space=pltpu.VMEM)
    if from_waves:
        out_shape = (jax.ShapeDtypeStruct((len(rounds), slots, lags), jnp.float32),
                     jax.ShapeDtypeStruct((events * pad, 2 * length), jnp.bfloat16))
        extra = []
    else:
        out_shape = (jax.ShapeDtypeStruct((n_prev + len(rounds), slots, lags), jnp.float32),)
        extra = [prev]
    return pl.pallas_call(
        kernel,
        out_shape=out_shape,
        in_specs=[smem, smem, smem] + [vmem] * (3 + len(partners) + len(extra)),
        out_specs=tuple(vmem for _ in out_shape),
        scratch_shapes=[
            pltpu.VMEM((events * chans, length), jnp.float32),
            pltpu.VMEM((events * pad, length), jnp.float32),
            pltpu.VMEM((events * pad, 2 * length), jnp.float32),
            pltpu.VMEM((events * pad, 2 * length), jnp.float32),
            pltpu.VMEM((slots, 2 * length), jnp.float32),
        ],
    )(pairs, counts, sid, own, *partners, fwd, inv, *extra)


def station_sum(block, groups):
    total = block
    bit = groups // 2
    while bit:
        rows = total.shape[1] // 2
        perm = [(s, s ^ bit) for s in range(groups)]
        got = lax.ppermute(total[:, rows:].astype(jnp.bfloat16), "station", perm)
        total = total[:, :rows] + got.astype(jnp.float32)
        bit //= 2
    return total


def shards(waveforms, pair_lists, pair_counts):
    events, stations, comps, length = waveforms.shape
    groups = lax.axis_size("station")
    rounds, slots, _ = pair_lists.shape
    chans = stations * comps
    fwd_np, inv_np = half_tables(length, stations * groups * comps, LAGS)
    fwd = jnp.asarray(fwd_np)
    inv = jnp.asarray(inv_np)
    flat = waveforms.reshape(events * chans, length)
    sid = lax.axis_index("station").astype(jnp.int32).reshape(1)
    pairs = pair_lists.reshape(-1)
    counts = pair_counts.reshape(-1)
    partners = {q: swapped(flat, "region", q) for q in reversed(range(rounds))}
    early = list(range(rounds - 1))
    corr_a, spec = rounds_call(pairs, counts, sid, flat, [partners[q] for q in early], fwd, inv,
                               early, events, chans, slots, groups)
    (corr,) = rounds_call(pairs, counts, sid, spec, [partners[rounds - 1]], fwd, inv,
                          [rounds - 1], events, chans, slots, groups, prev=corr_a)
    return station_sum(corr, groups)


def solution(mesh):
    return jax.shard_map(
        shards,
        mesh=mesh,
        in_specs=(P("region", "station", None, None), P(None, "region", None), P(None, "region")),
        out_specs=P(None, ("region", "station"), None),
        check_vma=False,
    )
```

```python
import math

import ml_dtypes
import numpy as np

import jax
import jax.numpy as jnp
from jax import lax
from jax.experimental import pallas as pl
from jax.experimental.pallas import tpu as pltpu
from jax.sharding import PartitionSpec as P

EPS = 1e-06
LAGS = 256


def swapped(block, axis, bit):
    count = lax.axis_size(axis)
    route = []
    for low in range(count):
        high = low | 1 << bit
        if high != low and high < count:
            route += [(low, high), (high, low)]
    return lax.ppermute(block, axis, route)


def half_tables(length, channels, lags):
    period = 2 * length
    half = period // 2
    step = np.float32(2.0 * math.pi / period)
    times = np.arange(length, dtype=np.int64)[:, None]
    freqs = np.arange(half, dtype=np.int64)[None, :]
    angle = step * ((times * freqs) % period).astype(np.float32)
    fwd = np.concatenate([np.cos(angle), -np.sin(angle)], axis=1).astype(np.float32)
    fwd[:, half] = np.where(times[:, 0] % 2 == 0, 1.0, -1.0)
    fwd = fwd.astype(ml_dtypes.bfloat16)

    factor = np.float32(1.0 / (period * math.sqrt(channels * length)))
    rows = np.arange(half, dtype=np.int64)[:, None]
    lagged = np.arange(lags, dtype=np.int64)[None, :] - lags // 2
    angle = step * ((rows * lagged) % period).astype(np.float32)
    cos_t = (np.cos(angle).astype(np.float32) * factor).astype(ml_dtypes.bfloat16).astype(np.float32)
    sin_t = ((-np.sin(angle)).astype(np.float32) * factor).astype(ml_dtypes.bfloat16).astype(np.float32)
    inv = np.zeros((period, lags), np.float32)
    inv[0] = cos_t[0]
    inv[1:half] = 2.0 * cos_t[1:]
    nyq_angle = step * ((half * lagged[0]) % period).astype(np.float32)
    inv[half] = (np.cos(nyq_angle).astype(np.float32) * factor).astype(ml_dtypes.bfloat16).astype(np.float32)
    inv[half + 1:] = 2.0 * sin_t[1:]
    return fwd, inv.astype(ml_dtypes.bfloat16)


def make_kernel(events, chans, pad, length, slots, groups, share, rounds, n_prev, from_waves):
    half = length
    n_part = len(rounds)

    def kernel(*refs):
        pl_ref, cnt_ref, sid_ref, own_ref = refs[:4]
        part_refs = refs[4:4 + n_part]
        f_ref, g_ref = refs[4 + n_part:6 + n_part]
        rest = refs[6 + n_part:]
        if from_waves:
            out_ref, spec_out = rest[:2]
            rest = rest[2:]
        else:
            prev_ref, keep_ref, send_ref = rest[:3]
            rest = rest[3:]
        nscr, xpad, specl, specp, cross = rest

        def spectra(w_ref, spec_ref):
            x = w_ref[...].astype(jnp.float32)
            x = x - jnp.mean(x, axis=-1, keepdims=True)
            x = x * lax.rsqrt(jnp.mean(x * x, axis=-1, keepdims=True) + EPS)
            nscr[...] = x
            for e in range(events):
                xpad[e * pad:e * pad + chans, :] = nscr[e * chans:(e + 1) * chans, :]
            xb = xpad[...].astype(jnp.bfloat16)
            spec = jnp.dot(xb, f_ref[...], preferred_element_type=jnp.float32)
            spec_ref[...] = spec.astype(jnp.bfloat16).astype(jnp.float32)

        xpad[...] = jnp.zeros(xpad.shape, jnp.float32)
        if from_waves:
            spectra(own_ref, specl)
            spec_out[...] = specl[...].astype(jnp.bfloat16)
        else:
            specl[...] = own_ref[...].astype(jnp.float32)
            for n in range(n_prev):
                prev = prev_ref[n]
                keep_ref[n] = prev[:slots // 2]
                send_ref[n] = prev[slots // 2:].astype(jnp.bfloat16)

        sid = sid_ref[0]
        lane = lax.broadcasted_iota(jnp.int32, (1, 128), 1)
        for n, q in enumerate(rounds):
            spectra(part_refs[n], specp)
            base = q * slots * 2
            for r in range(slots):
                slot = (sid ^ (r // share)) * share + r % share
                a = jnp.minimum(jnp.maximum(pl_ref[base + 2 * slot], 0), events - 1)
                b = jnp.minimum(jnp.maximum(pl_ref[base + 2 * slot + 1], 0), events - 1)
                left = specl[pl.ds(pl.multiple_of(a * pad, pad), pad), :]
                right = specp[pl.ds(pl.multiple_of(b * pad, pad), pad), :]
                lr, li = left[:, :half], left[:, half:]
                rr, ri = right[:, :half], right[:, half:]
                pp = lr * rr
                qq = li * ri
                re = jnp.sum(pp + qq, axis=0, keepdims=True)
                im = jnp.sum(lr * ri - li * rr, axis=0, keepdims=True)
                p0 = jnp.sum(pp[:, :128], axis=0, keepdims=True)
                q0 = jnp.sum(qq[:, :128], axis=0, keepdims=True)
                cross[r:r + 1, 0:128] = jnp.where(lane == 0, p0, re[:, :128])
                cross[r:r + 1, 128:half] = re[:, 128:]
                cross[r:r + 1, half:half + 128] = jnp.where(lane == 0, q0, im[:, :128])
                cross[r:r + 1, half + 128:] = im[:, 128:]

            cb = cross[...].astype(jnp.bfloat16)
            corr = jnp.dot(cb, g_ref[...], preferred_element_type=jnp.float32)
            rows = lax.broadcasted_iota(jnp.int32, corr.shape, 0)
            slot_of = (sid ^ (rows // share)) * share + rows % share
            corr = jnp.where(slot_of < cnt_ref[q], corr, 0.0)
            if from_waves:
                out_ref[n] = corr
            else:
                keep_ref[n_prev + n] = corr[:slots // 2]
                send_ref[n_prev + n] = corr[slots // 2:].astype(jnp.bfloat16)

    return kernel


def rounds_call(pairs, counts, sid, own, partners, fwd, inv, rounds, events, chans, slots, groups, prev=None):
    length = fwd.shape[0]
    lags = inv.shape[1]
    pad = 16
    share = slots // groups
    from_waves = prev is None
    n_prev = 0 if from_waves else prev.shape[0]
    kernel = make_kernel(events, chans, pad, length, slots, groups, share, rounds, n_prev, from_waves)
    smem = pl.BlockSpec(memory_space=pltpu.SMEM)
    vmem = pl.BlockSpec(memory_space=pltpu.VMEM)
    if from_waves:
        out_shape = (jax.ShapeDtypeStruct((len(rounds), slots, lags), jnp.float32),
                     jax.ShapeDtypeStruct((events * pad, 2 * length), jnp.bfloat16))
        extra = []
    else:
        out_shape = (jax.ShapeDtypeStruct((n_prev + len(rounds), slots // 2, lags), jnp.float32),
                     jax.ShapeDtypeStruct((n_prev + len(rounds), slots // 2, lags), jnp.bfloat16))
        extra = [prev]
    return pl.pallas_call(
        kernel,
        out_shape=out_shape,
        in_specs=[smem, smem, smem] + [vmem] * (3 + len(partners) + len(extra)),
        out_specs=tuple(vmem for _ in out_shape),
        scratch_shapes=[
            pltpu.VMEM((events * chans, length), jnp.float32),
            pltpu.VMEM((events * pad, length), jnp.float32),
            pltpu.VMEM((events * pad, 2 * length), jnp.float32),
            pltpu.VMEM((events * pad, 2 * length), jnp.float32),
            pltpu.VMEM((slots, 2 * length), jnp.float32),
        ],
    )(pairs, counts, sid, own, *partners, fwd, inv, *extra)


def station_sum(keep, send, groups):
    bit = groups // 2
    while True:
        perm = [(s, s ^ bit) for s in range(groups)]
        total = keep + lax.ppermute(send, "station", perm).astype(jnp.float32)
        bit //= 2
        if not bit:
            return total
        rows = total.shape[1] // 2
        keep, send = total[:, :rows], total[:, rows:].astype(jnp.bfloat16)


def shards(waveforms, pair_lists, pair_counts):
    events, stations, comps, length = waveforms.shape
    groups = lax.axis_size("station")
    rounds, slots, _ = pair_lists.shape
    chans = stations * comps
    fwd_np, inv_np = half_tables(length, stations * groups * comps, LAGS)
    fwd = jnp.asarray(fwd_np)
    inv = jnp.asarray(inv_np)
    flat = waveforms.reshape(events * chans, length)
    sid = lax.axis_index("station").astype(jnp.int32).reshape(1)
    pairs = pair_lists.reshape(-1)
    counts = pair_counts.reshape(-1)
    partners = {q: swapped(flat, "region", q) for q in reversed(range(rounds))}
    early = list(range(rounds - 1))
    corr_a, spec = rounds_call(pairs, counts, sid, flat, [partners[q] for q in early], fwd, inv,
                               early, events, chans, slots, groups)
    keep, send = rounds_call(pairs, counts, sid, spec, [partners[rounds - 1]], fwd, inv,
                          [rounds - 1], events, chans, slots, groups, prev=corr_a)
    return station_sum(keep, send, groups)


def solution(mesh):
    return jax.shard_map(
        shards,
        mesh=mesh,
        in_specs=(P("region", "station", None, None), P(None, "region", None), P(None, "region")),
        out_specs=P(None, ("region", "station"), None),
        check_vma=False,
    )
```

```python
import math

import ml_dtypes
import numpy as np

import jax
import jax.numpy as jnp
from jax import lax
from jax.experimental import pallas as pl
from jax.experimental.pallas import tpu as pltpu
from jax.sharding import PartitionSpec as P

EPS = 1e-06
LAGS = 256


def swapped(block, axis, bit):
    count = lax.axis_size(axis)
    route = []
    for low in range(count):
        high = low | 1 << bit
        if high != low and high < count:
            route += [(low, high), (high, low)]
    return lax.ppermute(block, axis, route)


def half_tables(length, channels, lags):
    period = 2 * length
    half = period // 2
    step = np.float32(2.0 * math.pi / period)
    times = np.arange(length, dtype=np.int64)[:, None]
    freqs = np.arange(half, dtype=np.int64)[None, :]
    angle = step * ((times * freqs) % period).astype(np.float32)
    fwd = np.concatenate([np.cos(angle), -np.sin(angle)], axis=1).astype(np.float32)
    fwd[:, half] = np.where(times[:, 0] % 2 == 0, 1.0, -1.0)
    fwd = fwd.astype(ml_dtypes.bfloat16)

    factor = np.float32(1.0 / (period * math.sqrt(channels * length)))
    rows = np.arange(half, dtype=np.int64)[:, None]
    lagged = np.arange(lags, dtype=np.int64)[None, :] - lags // 2
    angle = step * ((rows * lagged) % period).astype(np.float32)
    cos_t = (np.cos(angle).astype(np.float32) * factor).astype(ml_dtypes.bfloat16).astype(np.float32)
    sin_t = ((-np.sin(angle)).astype(np.float32) * factor).astype(ml_dtypes.bfloat16).astype(np.float32)
    inv = np.zeros((period, lags), np.float32)
    inv[0] = cos_t[0]
    inv[1:half] = 2.0 * cos_t[1:]
    nyq_angle = step * ((half * lagged[0]) % period).astype(np.float32)
    inv[half] = (np.cos(nyq_angle).astype(np.float32) * factor).astype(ml_dtypes.bfloat16).astype(np.float32)
    inv[half + 1:] = 2.0 * sin_t[1:]
    return fwd, inv.astype(ml_dtypes.bfloat16)


def make_kernel(events, chans, pad, length, slots, groups, share, rounds, prev_rounds, from_waves):
    half = length
    n_part = len(rounds)

    def kernel(*refs):
        pl_ref, cnt_ref, sid_ref, own_ref = refs[:4]
        part_refs = refs[4:4 + n_part]
        f_ref, g_ref = refs[4 + n_part:6 + n_part]
        rest = refs[6 + n_part:]
        if from_waves:
            out_ref, spec_out = rest[:2]
            rest = rest[2:]
        else:
            prev_ref, keep_ref, send_ref = rest[:3]
            rest = rest[3:]
        nscr, xpad, specl, specp, cross = rest

        def spectra(w_ref, spec_ref):
            x = w_ref[...].astype(jnp.float32)
            x = x - jnp.mean(x, axis=-1, keepdims=True)
            x = x * lax.rsqrt(jnp.mean(x * x, axis=-1, keepdims=True) + EPS)
            nscr[...] = x
            for e in range(events):
                xpad[e * pad:e * pad + chans, :] = nscr[e * chans:(e + 1) * chans, :]
            xb = xpad[...].astype(jnp.bfloat16)
            spec = jnp.dot(xb, f_ref[...], preferred_element_type=jnp.float32)
            spec_ref[...] = spec.astype(jnp.bfloat16).astype(jnp.float32)

        xpad[...] = jnp.zeros(xpad.shape, jnp.float32)
        if from_waves:
            spectra(own_ref, specl)
            spec_out[...] = specl[...].astype(jnp.bfloat16)
        else:
            specl[...] = own_ref[...].astype(jnp.float32)
            for n, q in enumerate(prev_rounds):
                prev = prev_ref[n]
                keep_ref[q] = prev[:slots // 2]
                send_ref[q] = prev[slots // 2:].astype(jnp.bfloat16)

        sid = sid_ref[0]
        lane = lax.broadcasted_iota(jnp.int32, (1, 128), 1)
        for n, q in enumerate(rounds):
            spectra(part_refs[n], specp)
            base = q * slots * 2
            for r in range(slots):
                slot = (sid ^ (r // share)) * share + r % share
                a = jnp.minimum(jnp.maximum(pl_ref[base + 2 * slot], 0), events - 1)
                b = jnp.minimum(jnp.maximum(pl_ref[base + 2 * slot + 1], 0), events - 1)
                left = specl[pl.ds(pl.multiple_of(a * pad, pad), pad), :]
                right = specp[pl.ds(pl.multiple_of(b * pad, pad), pad), :]
                lr, li = left[:, :half], left[:, half:]
                rr, ri = right[:, :half], right[:, half:]
                pp = lr * rr
                qq = li * ri
                re = jnp.sum(pp + qq, axis=0, keepdims=True)
                im = jnp.sum(lr * ri - li * rr, axis=0, keepdims=True)
                p0 = jnp.sum(pp[:, :128], axis=0, keepdims=True)
                q0 = jnp.sum(qq[:, :128], axis=0, keepdims=True)
                cross[r:r + 1, 0:128] = jnp.where(lane == 0, p0, re[:, :128])
                cross[r:r + 1, 128:half] = re[:, 128:]
                cross[r:r + 1, half:half + 128] = jnp.where(lane == 0, q0, im[:, :128])
                cross[r:r + 1, half + 128:] = im[:, 128:]

            cb = cross[...].astype(jnp.bfloat16)
            corr = jnp.dot(cb, g_ref[...], preferred_element_type=jnp.float32)
            rows = lax.broadcasted_iota(jnp.int32, corr.shape, 0)
            slot_of = (sid ^ (rows // share)) * share + rows % share
            corr = jnp.where(slot_of < cnt_ref[q], corr, 0.0)
            if from_waves:
                out_ref[n] = corr
            else:
                keep_ref[q] = corr[:slots // 2]
                send_ref[q] = corr[slots // 2:].astype(jnp.bfloat16)

    return kernel


def rounds_call(pairs, counts, sid, own, partners, fwd, inv, rounds, events, chans, slots, groups,
                prev=None, prev_rounds=()):
    length = fwd.shape[0]
    lags = inv.shape[1]
    pad = 16
    share = slots // groups
    from_waves = prev is None
    n_prev = 0 if from_waves else prev.shape[0]
    kernel = make_kernel(events, chans, pad, length, slots, groups, share, rounds, list(prev_rounds), from_waves)
    smem = pl.BlockSpec(memory_space=pltpu.SMEM)
    vmem = pl.BlockSpec(memory_space=pltpu.VMEM)
    if from_waves:
        out_shape = (jax.ShapeDtypeStruct((len(rounds), slots, lags), jnp.float32),
                     jax.ShapeDtypeStruct((events * pad, 2 * length), jnp.bfloat16))
        extra = []
    else:
        out_shape = (jax.ShapeDtypeStruct((n_prev + len(rounds), slots // 2, lags), jnp.float32),
                     jax.ShapeDtypeStruct((n_prev + len(rounds), slots // 2, lags), jnp.bfloat16))
        extra = [prev]
    return pl.pallas_call(
        kernel,
        out_shape=out_shape,
        in_specs=[smem, smem, smem] + [vmem] * (3 + len(partners) + len(extra)),
        out_specs=tuple(vmem for _ in out_shape),
        scratch_shapes=[
            pltpu.VMEM((events * chans, length), jnp.float32),
            pltpu.VMEM((events * pad, length), jnp.float32),
            pltpu.VMEM((events * pad, 2 * length), jnp.float32),
            pltpu.VMEM((events * pad, 2 * length), jnp.float32),
            pltpu.VMEM((slots, 2 * length), jnp.float32),
        ],
    )(pairs, counts, sid, own, *partners, fwd, inv, *extra)


def station_sum(keep, send, groups):
    bit = groups // 2
    while True:
        perm = [(s, s ^ bit) for s in range(groups)]
        total = keep + lax.ppermute(send, "station", perm).astype(jnp.float32)
        bit //= 2
        if not bit:
            return total
        rows = total.shape[1] // 2
        keep, send = total[:, :rows], total[:, rows:].astype(jnp.bfloat16)


def shards(waveforms, pair_lists, pair_counts):
    events, stations, comps, length = waveforms.shape
    groups = lax.axis_size("station")
    rounds, slots, _ = pair_lists.shape
    chans = stations * comps
    fwd_np, inv_np = half_tables(length, stations * groups * comps, LAGS)
    fwd = jnp.asarray(fwd_np)
    inv = jnp.asarray(inv_np)
    flat = waveforms.reshape(events * chans, length)
    sid = lax.axis_index("station").astype(jnp.int32).reshape(1)
    pairs = pair_lists.reshape(-1)
    counts = pair_counts.reshape(-1)
    partners = {q: swapped(flat, "region", q) for q in reversed(range(rounds))}
    late = 1 if rounds > 2 else rounds - 1
    early = [q for q in range(rounds) if q != late]
    corr_a, spec = rounds_call(pairs, counts, sid, flat, [partners[q] for q in early], fwd, inv,
                               early, events, chans, slots, groups)
    keep, send = rounds_call(pairs, counts, sid, spec, [partners[late]], fwd, inv,
                             [late], events, chans, slots, groups, prev=corr_a, prev_rounds=early)
    return station_sum(keep, send, groups)


def solution(mesh):
    return jax.shard_map(
        shards,
        mesh=mesh,
        in_specs=(P("region", "station", None, None), P(None, "region", None), P(None, "region")),
        out_specs=P(None, ("region", "station"), None),
        check_vma=False,
    )
```

```python
import math

import ml_dtypes
import numpy as np

import jax
import jax.numpy as jnp
from jax import lax
from jax.experimental import pallas as pl
from jax.experimental.pallas import tpu as pltpu
from jax.sharding import PartitionSpec as P

EPS = 1e-06
LAGS = 256


def swapped(block, axis, bit):
    count = lax.axis_size(axis)
    route = []
    for low in range(count):
        high = low | 1 << bit
        if high != low and high < count:
            route += [(low, high), (high, low)]
    return lax.ppermute(block, axis, route)


def half_tables(length, channels, lags):
    period = 2 * length
    half = period // 2
    step = np.float32(2.0 * math.pi / period)
    times = np.arange(length, dtype=np.int64)[:, None]
    freqs = np.arange(half, dtype=np.int64)[None, :]
    angle = step * ((times * freqs) % period).astype(np.float32)
    fwd = np.concatenate([np.cos(angle), -np.sin(angle)], axis=1).astype(np.float32)
    fwd[:, half] = np.where(times[:, 0] % 2 == 0, 1.0, -1.0)
    fwd = fwd.astype(ml_dtypes.bfloat16)

    factor = np.float32(1.0 / (period * math.sqrt(channels * length)))
    rows = np.arange(half, dtype=np.int64)[:, None]
    lagged = np.arange(lags, dtype=np.int64)[None, :] - lags // 2
    angle = step * ((rows * lagged) % period).astype(np.float32)
    cos_t = (np.cos(angle).astype(np.float32) * factor).astype(ml_dtypes.bfloat16).astype(np.float32)
    sin_t = ((-np.sin(angle)).astype(np.float32) * factor).astype(ml_dtypes.bfloat16).astype(np.float32)
    inv = np.zeros((period, lags), np.float32)
    inv[0] = cos_t[0]
    inv[1:half] = 2.0 * cos_t[1:]
    nyq_angle = step * ((half * lagged[0]) % period).astype(np.float32)
    inv[half] = (np.cos(nyq_angle).astype(np.float32) * factor).astype(ml_dtypes.bfloat16).astype(np.float32)
    inv[half + 1:] = 2.0 * sin_t[1:]
    return fwd, inv.astype(ml_dtypes.bfloat16)


def make_kernel(events, chans, pad, length, slots, groups, share, rounds, n_prev, from_waves, final):
    half = length
    n_part = len(rounds)

    def kernel(*refs):
        pl_ref, cnt_ref, sid_ref, own_ref = refs[:4]
        part_refs = refs[4:4 + n_part]
        f_ref, g_ref = refs[4 + n_part:6 + n_part]
        rest = refs[6 + n_part:]
        if from_waves:
            out_ref, spec_out = rest[:2]
            rest = rest[2:]
        elif final:
            prev_ref, keep_ref, send_ref = rest[:3]
            rest = rest[3:]
        else:
            prev_ref, out_ref = rest[:2]
            rest = rest[2:]
        nscr, xpad, specl, specp, cross = rest

        def spectra(w_ref, spec_ref):
            x = w_ref[...].astype(jnp.float32)
            x = x - jnp.mean(x, axis=-1, keepdims=True)
            x = x * lax.rsqrt(jnp.mean(x * x, axis=-1, keepdims=True) + EPS)
            nscr[...] = x
            for e in range(events):
                xpad[e * pad:e * pad + chans, :] = nscr[e * chans:(e + 1) * chans, :]
            xb = xpad[...].astype(jnp.bfloat16)
            spec = jnp.dot(xb, f_ref[...], preferred_element_type=jnp.float32)
            spec_ref[...] = spec.astype(jnp.bfloat16).astype(jnp.float32)

        xpad[...] = jnp.zeros(xpad.shape, jnp.float32)
        if from_waves:
            spectra(own_ref, specl)
            spec_out[...] = specl[...].astype(jnp.bfloat16)
        else:
            specl[...] = own_ref[...].astype(jnp.float32)
            for n in range(n_prev):
                prev = prev_ref[n]
                if final:
                    keep_ref[n] = prev[:slots // 2]
                    send_ref[n] = prev[slots // 2:].astype(jnp.bfloat16)
                else:
                    out_ref[n] = prev

        sid = sid_ref[0]
        lane = lax.broadcasted_iota(jnp.int32, (1, 128), 1)
        for n, q in enumerate(rounds):
            spectra(part_refs[n], specp)
            base = q * slots * 2
            for r in range(slots):
                slot = (sid ^ (r // share)) * share + r % share
                a = jnp.minimum(jnp.maximum(pl_ref[base + 2 * slot], 0), events - 1)
                b = jnp.minimum(jnp.maximum(pl_ref[base + 2 * slot + 1], 0), events - 1)
                left = specl[pl.ds(pl.multiple_of(a * pad, pad), pad), :]
                right = specp[pl.ds(pl.multiple_of(b * pad, pad), pad), :]
                lr, li = left[:, :half], left[:, half:]
                rr, ri = right[:, :half], right[:, half:]
                pp = lr * rr
                qq = li * ri
                re = jnp.sum(pp + qq, axis=0, keepdims=True)
                im = jnp.sum(lr * ri - li * rr, axis=0, keepdims=True)
                p0 = jnp.sum(pp[:, :128], axis=0, keepdims=True)
                q0 = jnp.sum(qq[:, :128], axis=0, keepdims=True)
                cross[r:r + 1, 0:128] = jnp.where(lane == 0, p0, re[:, :128])
                cross[r:r + 1, 128:half] = re[:, 128:]
                cross[r:r + 1, half:half + 128] = jnp.where(lane == 0, q0, im[:, :128])
                cross[r:r + 1, half + 128:] = im[:, 128:]

            cb = cross[...].astype(jnp.bfloat16)
            corr = jnp.dot(cb, g_ref[...], preferred_element_type=jnp.float32)
            rows = lax.broadcasted_iota(jnp.int32, corr.shape, 0)
            slot_of = (sid ^ (rows // share)) * share + rows % share
            corr = jnp.where(slot_of < cnt_ref[q], corr, 0.0)
            if not final:
                out_ref[n_prev + n] = corr
            else:
                keep_ref[n_prev + n] = corr[:slots // 2]
                send_ref[n_prev + n] = corr[slots // 2:].astype(jnp.bfloat16)

    return kernel


def rounds_call(pairs, counts, sid, own, partners, fwd, inv, rounds, events, chans, slots, groups,
                prev=None, final=False):
    length = fwd.shape[0]
    lags = inv.shape[1]
    pad = 16
    share = slots // groups
    from_waves = prev is None
    n_prev = 0 if from_waves else prev.shape[0]
    kernel = make_kernel(events, chans, pad, length, slots, groups, share, rounds, n_prev, from_waves, final)
    smem = pl.BlockSpec(memory_space=pltpu.SMEM)
    vmem = pl.BlockSpec(memory_space=pltpu.VMEM)
    if from_waves:
        out_shape = (jax.ShapeDtypeStruct((len(rounds), slots, lags), jnp.float32),
                     jax.ShapeDtypeStruct((events * pad, 2 * length), jnp.bfloat16))
        extra = []
    elif not final:
        out_shape = (jax.ShapeDtypeStruct((n_prev + len(rounds), slots, lags), jnp.float32),)
        extra = [prev]
    else:
        out_shape = (jax.ShapeDtypeStruct((n_prev + len(rounds), slots // 2, lags), jnp.float32),
                     jax.ShapeDtypeStruct((n_prev + len(rounds), slots // 2, lags), jnp.bfloat16))
        extra = [prev]
    return pl.pallas_call(
        kernel,
        out_shape=out_shape,
        in_specs=[smem, smem, smem] + [vmem] * (3 + len(partners) + len(extra)),
        out_specs=tuple(vmem for _ in out_shape),
        scratch_shapes=[
            pltpu.VMEM((events * chans, length), jnp.float32),
            pltpu.VMEM((events * pad, length), jnp.float32),
            pltpu.VMEM((events * pad, 2 * length), jnp.float32),
            pltpu.VMEM((events * pad, 2 * length), jnp.float32),
            pltpu.VMEM((slots, 2 * length), jnp.float32),
        ],
    )(pairs, counts, sid, own, *partners, fwd, inv, *extra)


def station_sum(keep, send, groups):
    bit = groups // 2
    while True:
        perm = [(s, s ^ bit) for s in range(groups)]
        total = keep + lax.ppermute(send, "station", perm).astype(jnp.float32)
        bit //= 2
        if not bit:
            return total
        rows = total.shape[1] // 2
        keep, send = total[:, :rows], total[:, rows:].astype(jnp.bfloat16)


def shards(waveforms, pair_lists, pair_counts):
    events, stations, comps, length = waveforms.shape
    groups = lax.axis_size("station")
    rounds, slots, _ = pair_lists.shape
    chans = stations * comps
    fwd_np, inv_np = half_tables(length, stations * groups * comps, LAGS)
    fwd = jnp.asarray(fwd_np)
    inv = jnp.asarray(inv_np)
    flat = waveforms.reshape(events * chans, length)
    sid = lax.axis_index("station").astype(jnp.int32).reshape(1)
    pairs = pair_lists.reshape(-1)
    counts = pair_counts.reshape(-1)
    partners = {q: swapped(flat, "region", q) for q in reversed(range(rounds))}
    corr, spec = rounds_call(pairs, counts, sid, flat, [partners[0]], fwd, inv,
                             [0], events, chans, slots, groups)
    for q in range(1, rounds - 1):
        (corr,) = rounds_call(pairs, counts, sid, spec, [partners[q]], fwd, inv,
                              [q], events, chans, slots, groups, prev=corr)
    keep, send = rounds_call(pairs, counts, sid, spec, [partners[rounds - 1]], fwd, inv,
                             [rounds - 1], events, chans, slots, groups, prev=corr, final=True)
    return station_sum(keep, send, groups)


def solution(mesh):
    return jax.shard_map(
        shards,
        mesh=mesh,
        in_specs=(P("region", "station", None, None), P(None, "region", None), P(None, "region")),
        out_specs=P(None, ("region", "station"), None),
        check_vma=False,
    )
```

```python
import math

import ml_dtypes
import numpy as np

import jax
import jax.numpy as jnp
from jax import lax
from jax.experimental import pallas as pl
from jax.experimental.pallas import tpu as pltpu
from jax.sharding import PartitionSpec as P

EPS = 1e-06
LAGS = 256


def swapped(block, axis, bit):
    count = lax.axis_size(axis)
    route = []
    for low in range(count):
        high = low | 1 << bit
        if high != low and high < count:
            route += [(low, high), (high, low)]
    return lax.ppermute(block, axis, route)


def half_tables(length, channels, lags):
    period = 2 * length
    half = period // 2
    step = np.float32(2.0 * math.pi / period)
    times = np.arange(length, dtype=np.int64)[:, None]
    freqs = np.arange(half, dtype=np.int64)[None, :]
    angle = step * ((times * freqs) % period).astype(np.float32)
    fwd = np.concatenate([np.cos(angle), -np.sin(angle)], axis=1).astype(np.float32)
    fwd[:, half] = np.where(times[:, 0] % 2 == 0, 1.0, -1.0)
    fwd = fwd.astype(ml_dtypes.bfloat16)

    factor = np.float32(1.0 / (period * math.sqrt(channels * length)))
    rows = np.arange(half, dtype=np.int64)[:, None]
    lagged = np.arange(lags, dtype=np.int64)[None, :] - lags // 2
    angle = step * ((rows * lagged) % period).astype(np.float32)
    cos_t = (np.cos(angle).astype(np.float32) * factor).astype(ml_dtypes.bfloat16).astype(np.float32)
    sin_t = ((-np.sin(angle)).astype(np.float32) * factor).astype(ml_dtypes.bfloat16).astype(np.float32)
    inv = np.zeros((period, lags), np.float32)
    inv[0] = cos_t[0]
    inv[1:half] = 2.0 * cos_t[1:]
    nyq_angle = step * ((half * lagged[0]) % period).astype(np.float32)
    inv[half] = (np.cos(nyq_angle).astype(np.float32) * factor).astype(ml_dtypes.bfloat16).astype(np.float32)
    inv[half + 1:] = 2.0 * sin_t[1:]
    return fwd, inv.astype(ml_dtypes.bfloat16)


def make_kernel(events, chans, pad, length, slots, groups, share, rounds, n_prev, from_waves, final):
    half = length
    n_part = len(rounds)

    def kernel(*refs):
        pl_ref, cnt_ref, sid_ref, own_ref = refs[:4]
        part_refs = refs[4:4 + n_part]
        f_ref, g_ref = refs[4 + n_part:6 + n_part]
        rest = refs[6 + n_part:]
        if from_waves:
            out_ref, spec_out = rest[:2]
            rest = rest[2:]
        elif final:
            prev_ref, keep_ref, send_ref = rest[:3]
            rest = rest[3:]
        else:
            prev_ref, out_ref = rest[:2]
            rest = rest[2:]
        nscr, xpad, specl, specp, cross, wbuf, sems = rest
        copies = [pltpu.make_async_copy(part_refs[n], wbuf.at[n], sems.at[n]) for n in range(n_part)]
        for c in copies:
            c.start()

        def spectra(w_ref, spec_ref):
            x = w_ref[...].astype(jnp.float32)
            x = x - jnp.mean(x, axis=-1, keepdims=True)
            x = x * lax.rsqrt(jnp.mean(x * x, axis=-1, keepdims=True) + EPS)
            nscr[...] = x
            for e in range(events):
                xpad[e * pad:e * pad + chans, :] = nscr[e * chans:(e + 1) * chans, :]
            xb = xpad[...].astype(jnp.bfloat16)
            spec = jnp.dot(xb, f_ref[...], preferred_element_type=jnp.float32)
            spec_ref[...] = spec.astype(jnp.bfloat16).astype(jnp.float32)

        xpad[...] = jnp.zeros(xpad.shape, jnp.float32)
        if from_waves:
            spectra(own_ref, specl)
            spec_out[...] = specl[...].astype(jnp.bfloat16)
        else:
            specl[...] = own_ref[...].astype(jnp.float32)
            for n in range(n_prev):
                prev = prev_ref[n]
                if final:
                    keep_ref[n] = prev[:slots // 2]
                    send_ref[n] = prev[slots // 2:].astype(jnp.bfloat16)
                else:
                    out_ref[n] = prev

        sid = sid_ref[0]
        lane = lax.broadcasted_iota(jnp.int32, (1, 128), 1)
        for n, q in enumerate(rounds):
            copies[n].wait()
            spectra(wbuf.at[n], specp)
            base = q * slots * 2
            for r in range(slots):
                slot = (sid ^ (r // share)) * share + r % share
                a = jnp.minimum(jnp.maximum(pl_ref[base + 2 * slot], 0), events - 1)
                b = jnp.minimum(jnp.maximum(pl_ref[base + 2 * slot + 1], 0), events - 1)
                left = specl[pl.ds(pl.multiple_of(a * pad, pad), pad), :]
                right = specp[pl.ds(pl.multiple_of(b * pad, pad), pad), :]
                lr, li = left[:, :half], left[:, half:]
                rr, ri = right[:, :half], right[:, half:]
                pp = lr * rr
                qq = li * ri
                re = jnp.sum(pp + qq, axis=0, keepdims=True)
                im = jnp.sum(lr * ri - li * rr, axis=0, keepdims=True)
                p0 = jnp.sum(pp[:, :128], axis=0, keepdims=True)
                q0 = jnp.sum(qq[:, :128], axis=0, keepdims=True)
                cross[r:r + 1, 0:128] = jnp.where(lane == 0, p0, re[:, :128])
                cross[r:r + 1, 128:half] = re[:, 128:]
                cross[r:r + 1, half:half + 128] = jnp.where(lane == 0, q0, im[:, :128])
                cross[r:r + 1, half + 128:] = im[:, 128:]

            cb = cross[...].astype(jnp.bfloat16)
            corr = jnp.dot(cb, g_ref[...], preferred_element_type=jnp.float32)
            rows = lax.broadcasted_iota(jnp.int32, corr.shape, 0)
            slot_of = (sid ^ (rows // share)) * share + rows % share
            corr = jnp.where(slot_of < cnt_ref[q], corr, 0.0)
            if not final:
                out_ref[n_prev + n] = corr
            else:
                keep_ref[n_prev + n] = corr[:slots // 2]
                send_ref[n_prev + n] = corr[slots // 2:].astype(jnp.bfloat16)

    return kernel


def rounds_call(pairs, counts, sid, own, partners, fwd, inv, rounds, events, chans, slots, groups,
                prev=None, final=False):
    length = fwd.shape[0]
    lags = inv.shape[1]
    pad = 16
    share = slots // groups
    from_waves = prev is None
    n_prev = 0 if from_waves else prev.shape[0]
    kernel = make_kernel(events, chans, pad, length, slots, groups, share, rounds, n_prev, from_waves, final)
    smem = pl.BlockSpec(memory_space=pltpu.SMEM)
    vmem = pl.BlockSpec(memory_space=pltpu.VMEM)
    anyspace = pl.BlockSpec(memory_space=pl.ANY)
    if from_waves:
        out_shape = (jax.ShapeDtypeStruct((len(rounds), slots, lags), jnp.float32),
                     jax.ShapeDtypeStruct((events * pad, 2 * length), jnp.bfloat16))
        extra = []
    elif not final:
        out_shape = (jax.ShapeDtypeStruct((n_prev + len(rounds), slots, lags), jnp.float32),)
        extra = [prev]
    else:
        out_shape = (jax.ShapeDtypeStruct((n_prev + len(rounds), slots // 2, lags), jnp.float32),
                     jax.ShapeDtypeStruct((n_prev + len(rounds), slots // 2, lags), jnp.bfloat16))
        extra = [prev]
    return pl.pallas_call(
        kernel,
        out_shape=out_shape,
        in_specs=[smem, smem, smem, vmem] + [anyspace] * len(partners) + [vmem] * (2 + len(extra)),
        out_specs=tuple(vmem for _ in out_shape),
        scratch_shapes=[
            pltpu.VMEM((events * chans, length), jnp.float32),
            pltpu.VMEM((events * pad, length), jnp.float32),
            pltpu.VMEM((events * pad, 2 * length), jnp.float32),
            pltpu.VMEM((events * pad, 2 * length), jnp.float32),
            pltpu.VMEM((slots, 2 * length), jnp.float32),
            pltpu.VMEM((len(partners),) + partners[0].shape, partners[0].dtype),
            pltpu.SemaphoreType.DMA((len(partners),)),
        ],
    )(pairs, counts, sid, own, *partners, fwd, inv, *extra)


def station_sum(keep, send, groups):
    bit = groups // 2
    while True:
        perm = [(s, s ^ bit) for s in range(groups)]
        total = keep + lax.ppermute(send, "station", perm).astype(jnp.float32)
        bit //= 2
        if not bit:
            return total
        rows = total.shape[1] // 2
        keep, send = total[:, :rows], total[:, rows:].astype(jnp.bfloat16)


def shards(waveforms, pair_lists, pair_counts):
    events, stations, comps, length = waveforms.shape
    groups = lax.axis_size("station")
    rounds, slots, _ = pair_lists.shape
    chans = stations * comps
    fwd_np, inv_np = half_tables(length, stations * groups * comps, LAGS)
    fwd = jnp.asarray(fwd_np)
    inv = jnp.asarray(inv_np)
    flat = waveforms.reshape(events * chans, length)
    sid = lax.axis_index("station").astype(jnp.int32).reshape(1)
    pairs = pair_lists.reshape(-1)
    counts = pair_counts.reshape(-1)
    partners = {q: swapped(flat, "region", q) for q in reversed(range(rounds))}
    corr, spec = rounds_call(pairs, counts, sid, flat, [partners[0]], fwd, inv,
                             [0], events, chans, slots, groups)
    for q in range(1, rounds - 1):
        (corr,) = rounds_call(pairs, counts, sid, spec, [partners[q]], fwd, inv,
                              [q], events, chans, slots, groups, prev=corr)
    keep, send = rounds_call(pairs, counts, sid, spec, [partners[rounds - 1]], fwd, inv,
                             [rounds - 1], events, chans, slots, groups, prev=corr, final=True)
    return station_sum(keep, send, groups)


def solution(mesh):
    return jax.shard_map(
        shards,
        mesh=mesh,
        in_specs=(P("region", "station", None, None), P(None, "region", None), P(None, "region")),
        out_specs=P(None, ("region", "station"), None),
        check_vma=False,
    )
```

```python
import math

import ml_dtypes
import numpy as np

import jax
import jax.numpy as jnp
from jax import lax
from jax.experimental import pallas as pl
from jax.experimental.pallas import tpu as pltpu
from jax.sharding import PartitionSpec as P

EPS = 1e-06
LAGS = 256


def swapped(block, axis, bit):
    count = lax.axis_size(axis)
    route = []
    for low in range(count):
        high = low | 1 << bit
        if high != low and high < count:
            route += [(low, high), (high, low)]
    return lax.ppermute(block, axis, route)


def half_tables(length, channels, lags):
    period = 2 * length
    half = period // 2
    step = np.float32(2.0 * math.pi / period)
    times = np.arange(length, dtype=np.int64)[:, None]
    freqs = np.arange(half, dtype=np.int64)[None, :]
    angle = step * ((times * freqs) % period).astype(np.float32)
    fwd = np.concatenate([np.cos(angle), -np.sin(angle)], axis=1).astype(np.float32)
    fwd[:, half] = np.where(times[:, 0] % 2 == 0, 1.0, -1.0)
    fwd = fwd.astype(ml_dtypes.bfloat16)

    factor = np.float32(1.0 / (period * math.sqrt(channels * length)))
    rows = np.arange(half, dtype=np.int64)[:, None]
    lagged = np.arange(lags, dtype=np.int64)[None, :] - lags // 2
    angle = step * ((rows * lagged) % period).astype(np.float32)
    cos_t = (np.cos(angle).astype(np.float32) * factor).astype(ml_dtypes.bfloat16).astype(np.float32)
    sin_t = ((-np.sin(angle)).astype(np.float32) * factor).astype(ml_dtypes.bfloat16).astype(np.float32)
    inv = np.zeros((period, lags), np.float32)
    inv[0] = cos_t[0]
    inv[1:half] = 2.0 * cos_t[1:]
    nyq_angle = step * ((half * lagged[0]) % period).astype(np.float32)
    inv[half] = (np.cos(nyq_angle).astype(np.float32) * factor).astype(ml_dtypes.bfloat16).astype(np.float32)
    inv[half + 1:] = 2.0 * sin_t[1:]
    return fwd, inv.astype(ml_dtypes.bfloat16)


def make_kernel(events, chans, pad, length, slots, groups, share, rounds, n_prev, from_waves, final):
    half = length
    n_part = len(rounds)

    def kernel(*refs):
        pl_ref, cnt_ref, sid_ref, own_ref = refs[:4]
        part_refs = refs[4:4 + n_part]
        f_ref, g_ref = refs[4 + n_part:6 + n_part]
        rest = refs[6 + n_part:]
        if from_waves:
            out_ref, spec_out = rest[:2]
            rest = rest[2:]
        elif final:
            prev_ref, keep_ref, send_ref = rest[:3]
            rest = rest[3:]
        else:
            prev_ref, out_ref = rest[:2]
            rest = rest[2:]
        nscr, xpad, specl, specp, cross = rest

        def spectra(w_ref, spec_ref):
            x = w_ref[...].astype(jnp.float32)
            x = x - jnp.mean(x, axis=-1, keepdims=True)
            x = x * lax.rsqrt(jnp.mean(x * x, axis=-1, keepdims=True) + EPS)
            nscr[...] = x
            for e in range(events):
                xpad[e * pad:e * pad + chans, :] = nscr[e * chans:(e + 1) * chans, :]
            xb = xpad[...].astype(jnp.bfloat16)
            spec = jnp.dot(xb, f_ref[...], preferred_element_type=jnp.float32)
            spec_ref[...] = spec.astype(jnp.bfloat16).astype(jnp.float32)

        xpad[...] = jnp.zeros(xpad.shape, jnp.float32)
        if from_waves:
            spectra(own_ref, specl)
            spec_out[...] = specl[...].astype(jnp.bfloat16)
        else:
            specl[...] = own_ref[...].astype(jnp.float32)
            for n in range(n_prev):
                prev = prev_ref[n]
                if final:
                    keep_ref[n] = prev[:share]
                    for j in range(1, groups):
                        send_ref[j - 1, n] = prev[j * share:(j + 1) * share].astype(jnp.bfloat16)
                else:
                    out_ref[n] = prev

        sid = sid_ref[0]
        lane = lax.broadcasted_iota(jnp.int32, (1, 128), 1)
        for n, q in enumerate(rounds):
            spectra(part_refs[n], specp)
            base = q * slots * 2
            for r in range(slots):
                slot = (sid ^ (r // share)) * share + r % share
                a = jnp.minimum(jnp.maximum(pl_ref[base + 2 * slot], 0), events - 1)
                b = jnp.minimum(jnp.maximum(pl_ref[base + 2 * slot + 1], 0), events - 1)
                left = specl[pl.ds(pl.multiple_of(a * pad, pad), pad), :]
                right = specp[pl.ds(pl.multiple_of(b * pad, pad), pad), :]
                lr, li = left[:, :half], left[:, half:]
                rr, ri = right[:, :half], right[:, half:]
                pp = lr * rr
                qq = li * ri
                re = jnp.sum(pp + qq, axis=0, keepdims=True)
                im = jnp.sum(lr * ri - li * rr, axis=0, keepdims=True)
                p0 = jnp.sum(pp[:, :128], axis=0, keepdims=True)
                q0 = jnp.sum(qq[:, :128], axis=0, keepdims=True)
                cross[r:r + 1, 0:128] = jnp.where(lane == 0, p0, re[:, :128])
                cross[r:r + 1, 128:half] = re[:, 128:]
                cross[r:r + 1, half:half + 128] = jnp.where(lane == 0, q0, im[:, :128])
                cross[r:r + 1, half + 128:] = im[:, 128:]

            cb = cross[...].astype(jnp.bfloat16)
            corr = jnp.dot(cb, g_ref[...], preferred_element_type=jnp.float32)
            rows = lax.broadcasted_iota(jnp.int32, corr.shape, 0)
            slot_of = (sid ^ (rows // share)) * share + rows % share
            corr = jnp.where(slot_of < cnt_ref[q], corr, 0.0)
            if not final:
                out_ref[n_prev + n] = corr
            else:
                keep_ref[n_prev + n] = corr[:share]
                for j in range(1, groups):
                    send_ref[j - 1, n_prev + n] = corr[j * share:(j + 1) * share].astype(jnp.bfloat16)

    return kernel


def rounds_call(pairs, counts, sid, own, partners, fwd, inv, rounds, events, chans, slots, groups,
                prev=None, final=False):
    length = fwd.shape[0]
    lags = inv.shape[1]
    pad = 16
    share = slots // groups
    from_waves = prev is None
    n_prev = 0 if from_waves else prev.shape[0]
    kernel = make_kernel(events, chans, pad, length, slots, groups, share, rounds, n_prev, from_waves, final)
    smem = pl.BlockSpec(memory_space=pltpu.SMEM)
    vmem = pl.BlockSpec(memory_space=pltpu.VMEM)
    if from_waves:
        out_shape = (jax.ShapeDtypeStruct((len(rounds), slots, lags), jnp.float32),
                     jax.ShapeDtypeStruct((events * pad, 2 * length), jnp.bfloat16))
        extra = []
    elif not final:
        out_shape = (jax.ShapeDtypeStruct((n_prev + len(rounds), slots, lags), jnp.float32),)
        extra = [prev]
    else:
        out_shape = (jax.ShapeDtypeStruct((n_prev + len(rounds), share, lags), jnp.float32),
                     jax.ShapeDtypeStruct((groups - 1, n_prev + len(rounds), share, lags), jnp.bfloat16))
        extra = [prev]
    return pl.pallas_call(
        kernel,
        out_shape=out_shape,
        in_specs=[smem, smem, smem] + [vmem] * (3 + len(partners) + len(extra)),
        out_specs=tuple(vmem for _ in out_shape),
        scratch_shapes=[
            pltpu.VMEM((events * chans, length), jnp.float32),
            pltpu.VMEM((events * pad, length), jnp.float32),
            pltpu.VMEM((events * pad, 2 * length), jnp.float32),
            pltpu.VMEM((events * pad, 2 * length), jnp.float32),
            pltpu.VMEM((slots, 2 * length), jnp.float32),
        ],
    )(pairs, counts, sid, own, *partners, fwd, inv, *extra)


def station_sum(keep, send, groups):
    total = keep
    for j in range(1, groups):
        perm = [(s, s ^ j) for s in range(groups)]
        total = total + lax.ppermute(send[j - 1], "station", perm).astype(jnp.float32)
    return total


def shards(waveforms, pair_lists, pair_counts):
    events, stations, comps, length = waveforms.shape
    groups = lax.axis_size("station")
    rounds, slots, _ = pair_lists.shape
    chans = stations * comps
    fwd_np, inv_np = half_tables(length, stations * groups * comps, LAGS)
    fwd = jnp.asarray(fwd_np)
    inv = jnp.asarray(inv_np)
    flat = waveforms.reshape(events * chans, length)
    sid = lax.axis_index("station").astype(jnp.int32).reshape(1)
    pairs = pair_lists.reshape(-1)
    counts = pair_counts.reshape(-1)
    partners = {q: swapped(flat, "region", q) for q in reversed(range(rounds))}
    corr, spec = rounds_call(pairs, counts, sid, flat, [partners[0]], fwd, inv,
                             [0], events, chans, slots, groups)
    for q in range(1, rounds - 1):
        (corr,) = rounds_call(pairs, counts, sid, spec, [partners[q]], fwd, inv,
                              [q], events, chans, slots, groups, prev=corr)
    keep, send = rounds_call(pairs, counts, sid, spec, [partners[rounds - 1]], fwd, inv,
                             [rounds - 1], events, chans, slots, groups, prev=corr, final=True)
    return station_sum(keep, send, groups)


def solution(mesh):
    return jax.shard_map(
        shards,
        mesh=mesh,
        in_specs=(P("region", "station", None, None), P(None, "region", None), P(None, "region")),
        out_specs=P(None, ("region", "station"), None),
        check_vma=False,
    )
```

```python
import math

import ml_dtypes
import numpy as np

import jax
import jax.numpy as jnp
from jax import lax
from jax.experimental import pallas as pl
from jax.experimental.pallas import tpu as pltpu
from jax.sharding import PartitionSpec as P

EPS = 1e-06
LAGS = 256


def swapped(block, axis, bit):
    count = lax.axis_size(axis)
    route = []
    for low in range(count):
        high = low | 1 << bit
        if high != low and high < count:
            route += [(low, high), (high, low)]
    return lax.ppermute(block, axis, route)


def half_tables(length, channels, lags):
    period = 2 * length
    half = period // 2
    step = np.float32(2.0 * math.pi / period)
    times = np.arange(length, dtype=np.int64)[:, None]
    freqs = np.arange(half, dtype=np.int64)[None, :]
    angle = step * ((times * freqs) % period).astype(np.float32)
    fwd = np.concatenate([np.cos(angle), -np.sin(angle)], axis=1).astype(np.float32)
    fwd[:, half] = np.where(times[:, 0] % 2 == 0, 1.0, -1.0)
    fwd = fwd.astype(ml_dtypes.bfloat16)

    factor = np.float32(1.0 / (period * math.sqrt(channels * length)))
    rows = np.arange(half, dtype=np.int64)[:, None]
    lagged = np.arange(lags, dtype=np.int64)[None, :] - lags // 2
    angle = step * ((rows * lagged) % period).astype(np.float32)
    cos_t = (np.cos(angle).astype(np.float32) * factor).astype(ml_dtypes.bfloat16).astype(np.float32)
    sin_t = ((-np.sin(angle)).astype(np.float32) * factor).astype(ml_dtypes.bfloat16).astype(np.float32)
    inv = np.zeros((period, lags), np.float32)
    inv[0] = cos_t[0]
    inv[1:half] = 2.0 * cos_t[1:]
    nyq_angle = step * ((half * lagged[0]) % period).astype(np.float32)
    inv[half] = (np.cos(nyq_angle).astype(np.float32) * factor).astype(ml_dtypes.bfloat16).astype(np.float32)
    inv[half + 1:] = 2.0 * sin_t[1:]
    return fwd, inv.astype(ml_dtypes.bfloat16)


def make_kernel(events, chans, pad, length, slots, groups, share, rounds, n_prev, from_waves, final):
    half = length
    n_part = len(rounds)

    def kernel(*refs):
        pl_ref, cnt_ref, sid_ref, own_ref = refs[:4]
        part_refs = refs[4:4 + n_part]
        f_ref, g_ref = refs[4 + n_part:6 + n_part]
        rest = refs[6 + n_part:]
        if from_waves:
            out_ref, spec_out = rest[:2]
            rest = rest[2:]
        elif final:
            prev_ref, keep_ref = rest[:2]
            send_refs = rest[2:2 + groups - 1]
            rest = rest[2 + groups - 1:]
        else:
            prev_ref, out_ref = rest[:2]
            rest = rest[2:]
        nscr, xpad, specl, specp, cross = rest

        def spectra(w_ref, spec_ref):
            x = w_ref[...].astype(jnp.float32)
            x = x - jnp.mean(x, axis=-1, keepdims=True)
            x = x * lax.rsqrt(jnp.mean(x * x, axis=-1, keepdims=True) + EPS)
            nscr[...] = x
            for e in range(events):
                xpad[e * pad:e * pad + chans, :] = nscr[e * chans:(e + 1) * chans, :]
            xb = xpad[...].astype(jnp.bfloat16)
            spec = jnp.dot(xb, f_ref[...], preferred_element_type=jnp.float32)
            spec_ref[...] = spec.astype(jnp.bfloat16).astype(jnp.float32)

        xpad[...] = jnp.zeros(xpad.shape, jnp.float32)
        if from_waves:
            spectra(own_ref, specl)
            spec_out[...] = specl[...].astype(jnp.bfloat16)
        else:
            specl[...] = own_ref[...].astype(jnp.float32)
            for n in range(n_prev):
                prev = prev_ref[n]
                if final:
                    keep_ref[n] = prev[:share]
                    for j in range(1, groups):
                        send_refs[j - 1][n] = prev[j * share:(j + 1) * share].astype(jnp.bfloat16)
                else:
                    out_ref[n] = prev

        sid = sid_ref[0]
        lane = lax.broadcasted_iota(jnp.int32, (1, 128), 1)
        for n, q in enumerate(rounds):
            spectra(part_refs[n], specp)
            base = q * slots * 2
            for r in range(slots):
                slot = (sid ^ (r // share)) * share + r % share
                a = jnp.minimum(jnp.maximum(pl_ref[base + 2 * slot], 0), events - 1)
                b = jnp.minimum(jnp.maximum(pl_ref[base + 2 * slot + 1], 0), events - 1)
                left = specl[pl.ds(pl.multiple_of(a * pad, pad), pad), :]
                right = specp[pl.ds(pl.multiple_of(b * pad, pad), pad), :]
                lr, li = left[:, :half], left[:, half:]
                rr, ri = right[:, :half], right[:, half:]
                pp = lr * rr
                qq = li * ri
                re = jnp.sum(pp + qq, axis=0, keepdims=True)
                im = jnp.sum(lr * ri - li * rr, axis=0, keepdims=True)
                p0 = jnp.sum(pp[:, :128], axis=0, keepdims=True)
                q0 = jnp.sum(qq[:, :128], axis=0, keepdims=True)
                cross[r:r + 1, 0:128] = jnp.where(lane == 0, p0, re[:, :128])
                cross[r:r + 1, 128:half] = re[:, 128:]
                cross[r:r + 1, half:half + 128] = jnp.where(lane == 0, q0, im[:, :128])
                cross[r:r + 1, half + 128:] = im[:, 128:]

            cb = cross[...].astype(jnp.bfloat16)
            corr = jnp.dot(cb, g_ref[...], preferred_element_type=jnp.float32)
            rows = lax.broadcasted_iota(jnp.int32, corr.shape, 0)
            slot_of = (sid ^ (rows // share)) * share + rows % share
            corr = jnp.where(slot_of < cnt_ref[q], corr, 0.0)
            if not final:
                out_ref[n_prev + n] = corr
            else:
                keep_ref[n_prev + n] = corr[:share]
                for j in range(1, groups):
                    send_refs[j - 1][n_prev + n] = corr[j * share:(j + 1) * share].astype(jnp.bfloat16)

    return kernel


def rounds_call(pairs, counts, sid, own, partners, fwd, inv, rounds, events, chans, slots, groups,
                prev=None, final=False):
    length = fwd.shape[0]
    lags = inv.shape[1]
    pad = 16
    share = slots // groups
    from_waves = prev is None
    n_prev = 0 if from_waves else prev.shape[0]
    kernel = make_kernel(events, chans, pad, length, slots, groups, share, rounds, n_prev, from_waves, final)
    smem = pl.BlockSpec(memory_space=pltpu.SMEM)
    vmem = pl.BlockSpec(memory_space=pltpu.VMEM)
    if from_waves:
        out_shape = (jax.ShapeDtypeStruct((len(rounds), slots, lags), jnp.float32),
                     jax.ShapeDtypeStruct((events * pad, 2 * length), jnp.bfloat16))
        extra = []
    elif not final:
        out_shape = (jax.ShapeDtypeStruct((n_prev + len(rounds), slots, lags), jnp.float32),)
        extra = [prev]
    else:
        out_shape = (jax.ShapeDtypeStruct((n_prev + len(rounds), share, lags), jnp.float32),
                     ) + tuple(jax.ShapeDtypeStruct((n_prev + len(rounds), share, lags), jnp.bfloat16)
                               for _ in range(groups - 1))
        extra = [prev]
    return pl.pallas_call(
        kernel,
        out_shape=out_shape,
        in_specs=[smem, smem, smem] + [vmem] * (3 + len(partners) + len(extra)),
        out_specs=tuple(vmem for _ in out_shape),
        scratch_shapes=[
            pltpu.VMEM((events * chans, length), jnp.float32),
            pltpu.VMEM((events * pad, length), jnp.float32),
            pltpu.VMEM((events * pad, 2 * length), jnp.float32),
            pltpu.VMEM((events * pad, 2 * length), jnp.float32),
            pltpu.VMEM((slots, 2 * length), jnp.float32),
        ],
    )(pairs, counts, sid, own, *partners, fwd, inv, *extra)


def station_sum(keep, send, groups):
    total = keep
    for j in range(1, groups):
        perm = [(s, s ^ j) for s in range(groups)]
        total = total + lax.ppermute(send[j - 1], "station", perm).astype(jnp.float32)
    return total


def shards(waveforms, pair_lists, pair_counts):
    events, stations, comps, length = waveforms.shape
    groups = lax.axis_size("station")
    rounds, slots, _ = pair_lists.shape
    chans = stations * comps
    fwd_np, inv_np = half_tables(length, stations * groups * comps, LAGS)
    fwd = jnp.asarray(fwd_np)
    inv = jnp.asarray(inv_np)
    flat = waveforms.reshape(events * chans, length)
    sid = lax.axis_index("station").astype(jnp.int32).reshape(1)
    pairs = pair_lists.reshape(-1)
    counts = pair_counts.reshape(-1)
    partners = {q: swapped(flat, "region", q) for q in reversed(range(rounds))}
    corr, spec = rounds_call(pairs, counts, sid, flat, [partners[0]], fwd, inv,
                             [0], events, chans, slots, groups)
    for q in range(1, rounds - 1):
        (corr,) = rounds_call(pairs, counts, sid, spec, [partners[q]], fwd, inv,
                              [q], events, chans, slots, groups, prev=corr)
    keep, *send = rounds_call(pairs, counts, sid, spec, [partners[rounds - 1]], fwd, inv,
                             [rounds - 1], events, chans, slots, groups, prev=corr, final=True)
    return station_sum(keep, send, groups)


def solution(mesh):
    return jax.shard_map(
        shards,
        mesh=mesh,
        in_specs=(P("region", "station", None, None), P(None, "region", None), P(None, "region")),
        out_specs=P(None, ("region", "station"), None),
        check_vma=False,
    )
```

```python
import math

import ml_dtypes
import numpy as np

import jax
import jax.numpy as jnp
from jax import lax
from jax.experimental import pallas as pl
from jax.experimental.pallas import tpu as pltpu
from jax.sharding import PartitionSpec as P

EPS = 1e-06
LAGS = 256


def swapped(block, axis, bit):
    count = lax.axis_size(axis)
    route = []
    for low in range(count):
        high = low | 1 << bit
        if high != low and high < count:
            route += [(low, high), (high, low)]
    return lax.ppermute(block, axis, route)


def half_tables(length, channels, lags):
    period = 2 * length
    half = period // 2
    step = np.float32(2.0 * math.pi / period)
    times = np.arange(length, dtype=np.int64)[:, None]
    freqs = np.arange(half, dtype=np.int64)[None, :]
    angle = step * ((times * freqs) % period).astype(np.float32)
    fwd = np.concatenate([np.cos(angle), -np.sin(angle)], axis=1).astype(np.float32)
    fwd[:, half] = np.where(times[:, 0] % 2 == 0, 1.0, -1.0)
    fwd = fwd.astype(ml_dtypes.bfloat16)

    factor = np.float32(1.0 / (period * math.sqrt(channels * length)))
    rows = np.arange(half, dtype=np.int64)[:, None]
    lagged = np.arange(lags, dtype=np.int64)[None, :] - lags // 2
    angle = step * ((rows * lagged) % period).astype(np.float32)
    cos_t = (np.cos(angle).astype(np.float32) * factor).astype(ml_dtypes.bfloat16).astype(np.float32)
    sin_t = ((-np.sin(angle)).astype(np.float32) * factor).astype(ml_dtypes.bfloat16).astype(np.float32)
    inv = np.zeros((period, lags), np.float32)
    inv[0] = cos_t[0]
    inv[1:half] = 2.0 * cos_t[1:]
    nyq_angle = step * ((half * lagged[0]) % period).astype(np.float32)
    inv[half] = (np.cos(nyq_angle).astype(np.float32) * factor).astype(ml_dtypes.bfloat16).astype(np.float32)
    inv[half + 1:] = 2.0 * sin_t[1:]
    return fwd, inv.astype(ml_dtypes.bfloat16)


def make_kernel(events, chans, pad, length, slots, groups, share, rounds, n_prev, from_waves, final):
    half = length
    n_part = len(rounds)

    def kernel(*refs):
        pl_ref, cnt_ref, sid_ref, own_ref = refs[:4]
        part_refs = refs[4:4 + n_part]
        f_ref, g_ref = refs[4 + n_part:6 + n_part]
        rest = refs[6 + n_part:]
        if from_waves:
            out_ref, spec_out = rest[:2]
            rest = rest[2:]
        elif final:
            prev_ref, keep_ref, send_ref = rest[:3]
            rest = rest[3:]
        else:
            prev_ref, out_ref = rest[:2]
            rest = rest[2:]
        nscr, xpad, specl, specp, cross, fbuf, gbuf, sems = rest
        f_copy = pltpu.make_async_copy(f_ref, fbuf, sems.at[0])
        g_copy = pltpu.make_async_copy(g_ref, gbuf, sems.at[1])
        f_copy.start()
        g_copy.start()
        pending = {"f": f_copy, "g": g_copy}

        def table(name, buf):
            if name in pending:
                pending.pop(name).wait()
            return buf[...]

        def spectra(w_ref, spec_ref):
            x = w_ref[...].astype(jnp.float32)
            x = x - jnp.mean(x, axis=-1, keepdims=True)
            x = x * lax.rsqrt(jnp.mean(x * x, axis=-1, keepdims=True) + EPS)
            nscr[...] = x
            for e in range(events):
                xpad[e * pad:e * pad + chans, :] = nscr[e * chans:(e + 1) * chans, :]
            xb = xpad[...].astype(jnp.bfloat16)
            spec = jnp.dot(xb, table("f", fbuf), preferred_element_type=jnp.float32)
            spec_ref[...] = spec.astype(jnp.bfloat16).astype(jnp.float32)

        xpad[...] = jnp.zeros(xpad.shape, jnp.float32)
        if from_waves:
            spectra(own_ref, specl)
            spec_out[...] = specl[...].astype(jnp.bfloat16)
        else:
            specl[...] = own_ref[...].astype(jnp.float32)
            for n in range(n_prev):
                prev = prev_ref[n]
                if final:
                    keep_ref[n] = prev[:share]
                    for j in range(1, groups):
                        send_ref[j - 1, n] = prev[j * share:(j + 1) * share].astype(jnp.bfloat16)
                else:
                    out_ref[n] = prev

        sid = sid_ref[0]
        lane = lax.broadcasted_iota(jnp.int32, (1, 128), 1)
        for n, q in enumerate(rounds):
            spectra(part_refs[n], specp)
            base = q * slots * 2
            for r in range(slots):
                slot = (sid ^ (r // share)) * share + r % share
                a = jnp.minimum(jnp.maximum(pl_ref[base + 2 * slot], 0), events - 1)
                b = jnp.minimum(jnp.maximum(pl_ref[base + 2 * slot + 1], 0), events - 1)
                left = specl[pl.ds(pl.multiple_of(a * pad, pad), pad), :]
                right = specp[pl.ds(pl.multiple_of(b * pad, pad), pad), :]
                lr, li = left[:, :half], left[:, half:]
                rr, ri = right[:, :half], right[:, half:]
                pp = lr * rr
                qq = li * ri
                re = jnp.sum(pp + qq, axis=0, keepdims=True)
                im = jnp.sum(lr * ri - li * rr, axis=0, keepdims=True)
                p0 = jnp.sum(pp[:, :128], axis=0, keepdims=True)
                q0 = jnp.sum(qq[:, :128], axis=0, keepdims=True)
                cross[r:r + 1, 0:128] = jnp.where(lane == 0, p0, re[:, :128])
                cross[r:r + 1, 128:half] = re[:, 128:]
                cross[r:r + 1, half:half + 128] = jnp.where(lane == 0, q0, im[:, :128])
                cross[r:r + 1, half + 128:] = im[:, 128:]

            cb = cross[...].astype(jnp.bfloat16)
            corr = jnp.dot(cb, table("g", gbuf), preferred_element_type=jnp.float32)
            rows = lax.broadcasted_iota(jnp.int32, corr.shape, 0)
            slot_of = (sid ^ (rows // share)) * share + rows % share
            corr = jnp.where(slot_of < cnt_ref[q], corr, 0.0)
            if not final:
                out_ref[n_prev + n] = corr
            else:
                keep_ref[n_prev + n] = corr[:share]
                for j in range(1, groups):
                    send_ref[j - 1, n_prev + n] = corr[j * share:(j + 1) * share].astype(jnp.bfloat16)

    return kernel


def rounds_call(pairs, counts, sid, own, partners, fwd, inv, rounds, events, chans, slots, groups,
                prev=None, final=False):
    length = fwd.shape[0]
    lags = inv.shape[1]
    pad = 16
    share = slots // groups
    from_waves = prev is None
    n_prev = 0 if from_waves else prev.shape[0]
    kernel = make_kernel(events, chans, pad, length, slots, groups, share, rounds, n_prev, from_waves, final)
    smem = pl.BlockSpec(memory_space=pltpu.SMEM)
    vmem = pl.BlockSpec(memory_space=pltpu.VMEM)
    anyspace = pl.BlockSpec(memory_space=pl.ANY)
    if from_waves:
        out_shape = (jax.ShapeDtypeStruct((len(rounds), slots, lags), jnp.float32),
                     jax.ShapeDtypeStruct((events * pad, 2 * length), jnp.bfloat16))
        extra = []
    elif not final:
        out_shape = (jax.ShapeDtypeStruct((n_prev + len(rounds), slots, lags), jnp.float32),)
        extra = [prev]
    else:
        out_shape = (jax.ShapeDtypeStruct((n_prev + len(rounds), share, lags), jnp.float32),
                     jax.ShapeDtypeStruct((groups - 1, n_prev + len(rounds), share, lags), jnp.bfloat16))
        extra = [prev]
    return pl.pallas_call(
        kernel,
        out_shape=out_shape,
        in_specs=[smem, smem, smem] + [vmem] * (1 + len(partners)) + [anyspace] * 2 + [vmem] * len(extra),
        out_specs=tuple(vmem for _ in out_shape),
        scratch_shapes=[
            pltpu.VMEM((events * chans, length), jnp.float32),
            pltpu.VMEM((events * pad, length), jnp.float32),
            pltpu.VMEM((events * pad, 2 * length), jnp.float32),
            pltpu.VMEM((events * pad, 2 * length), jnp.float32),
            pltpu.VMEM((slots, 2 * length), jnp.float32),
            pltpu.VMEM(fwd.shape, fwd.dtype),
            pltpu.VMEM(inv.shape, inv.dtype),
            pltpu.SemaphoreType.DMA((2,)),
        ],
    )(pairs, counts, sid, own, *partners, fwd, inv, *extra)


def station_sum(keep, send, groups):
    total = keep
    for j in range(1, groups):
        perm = [(s, s ^ j) for s in range(groups)]
        total = total + lax.ppermute(send[j - 1], "station", perm).astype(jnp.float32)
    return total


def shards(waveforms, pair_lists, pair_counts):
    events, stations, comps, length = waveforms.shape
    groups = lax.axis_size("station")
    rounds, slots, _ = pair_lists.shape
    chans = stations * comps
    fwd_np, inv_np = half_tables(length, stations * groups * comps, LAGS)
    fwd = jnp.asarray(fwd_np)
    inv = jnp.asarray(inv_np)
    flat = waveforms.reshape(events * chans, length)
    sid = lax.axis_index("station").astype(jnp.int32).reshape(1)
    pairs = pair_lists.reshape(-1)
    counts = pair_counts.reshape(-1)
    partners = {q: swapped(flat, "region", q) for q in reversed(range(rounds))}
    corr, spec = rounds_call(pairs, counts, sid, flat, [partners[0]], fwd, inv,
                             [0], events, chans, slots, groups)
    for q in range(1, rounds - 1):
        (corr,) = rounds_call(pairs, counts, sid, spec, [partners[q]], fwd, inv,
                              [q], events, chans, slots, groups, prev=corr)
    keep, send = rounds_call(pairs, counts, sid, spec, [partners[rounds - 1]], fwd, inv,
                             [rounds - 1], events, chans, slots, groups, prev=corr, final=True)
    return station_sum(keep, send, groups)


def solution(mesh):
    return jax.shard_map(
        shards,
        mesh=mesh,
        in_specs=(P("region", "station", None, None), P(None, "region", None), P(None, "region")),
        out_specs=P(None, ("region", "station"), None),
        check_vma=False,
    )
```

```python
import math

import ml_dtypes
import numpy as np

import jax
import jax.numpy as jnp
from jax import lax
from jax.experimental import pallas as pl
from jax.experimental.pallas import tpu as pltpu
from jax.sharding import PartitionSpec as P

EPS = 1e-06
LAGS = 256


def swapped(block, axis, bit):
    count = lax.axis_size(axis)
    route = []
    for low in range(count):
        high = low | 1 << bit
        if high != low and high < count:
            route += [(low, high), (high, low)]
    return lax.ppermute(block, axis, route)


def half_tables(length, channels, lags):
    period = 2 * length
    half = period // 2
    step = np.float32(2.0 * math.pi / period)
    times = np.arange(length, dtype=np.int64)[:, None]
    freqs = np.arange(half, dtype=np.int64)[None, :]
    angle = step * ((times * freqs) % period).astype(np.float32)
    fwd = np.concatenate([np.cos(angle), -np.sin(angle)], axis=1).astype(np.float32)
    fwd[:, half] = np.where(times[:, 0] % 2 == 0, 1.0, -1.0)
    fwd = fwd.astype(ml_dtypes.bfloat16)

    factor = np.float32(1.0 / (period * math.sqrt(channels * length)))
    rows = np.arange(half, dtype=np.int64)[:, None]
    lagged = np.arange(lags, dtype=np.int64)[None, :] - lags // 2
    angle = step * ((rows * lagged) % period).astype(np.float32)
    cos_t = (np.cos(angle).astype(np.float32) * factor).astype(ml_dtypes.bfloat16).astype(np.float32)
    sin_t = ((-np.sin(angle)).astype(np.float32) * factor).astype(ml_dtypes.bfloat16).astype(np.float32)
    inv = np.zeros((period, lags), np.float32)
    inv[0] = cos_t[0]
    inv[1:half] = 2.0 * cos_t[1:]
    nyq_angle = step * ((half * lagged[0]) % period).astype(np.float32)
    inv[half] = (np.cos(nyq_angle).astype(np.float32) * factor).astype(ml_dtypes.bfloat16).astype(np.float32)
    inv[half + 1:] = 2.0 * sin_t[1:]
    return fwd, inv.astype(ml_dtypes.bfloat16)


def make_kernel(events, chans, pad, length, slots, groups, share, rounds, n_prev, from_waves, final):
    half = length
    n_part = len(rounds)
    total_rounds = n_prev + n_part

    def kernel(*refs):
        pl_ref, cnt_ref, sid_ref, own_ref = refs[:4]
        part_refs = refs[4:4 + n_part]
        rest = list(refs[4 + n_part:])
        f_ref = rest.pop(0)
        g_ref = rest.pop(0) if final else None
        prev_ref = rest.pop(0) if n_prev else None
        if final:
            keep_ref, send_ref = rest.pop(0), rest.pop(0)
        else:
            xout = rest.pop(0)
            spec_out = rest.pop(0) if from_waves else None
        nscr, xpad, specl, specp, cross = rest[:5]
        allx = rest[5] if final else None

        def spectra(w_ref, spec_ref):
            x = w_ref[...].astype(jnp.float32)
            x = x - jnp.mean(x, axis=-1, keepdims=True)
            x = x * lax.rsqrt(jnp.mean(x * x, axis=-1, keepdims=True) + EPS)
            nscr[...] = x
            for e in range(events):
                xpad[e * pad:e * pad + chans, :] = nscr[e * chans:(e + 1) * chans, :]
            xb = xpad[...].astype(jnp.bfloat16)
            spec = jnp.dot(xb, f_ref[...], preferred_element_type=jnp.float32)
            spec_ref[...] = spec.astype(jnp.bfloat16).astype(jnp.float32)

        xpad[...] = jnp.zeros(xpad.shape, jnp.float32)
        if from_waves:
            spectra(own_ref, specl)
            spec_out[...] = specl[...].astype(jnp.bfloat16)
        else:
            specl[...] = own_ref[...].astype(jnp.float32)
            for n in range(n_prev):
                if final:
                    allx[n * slots:(n + 1) * slots, :] = prev_ref[n]
                else:
                    xout[n] = prev_ref[n]

        sid = sid_ref[0]
        lane = lax.broadcasted_iota(jnp.int32, (1, 128), 1)
        for n, q in enumerate(rounds):
            spectra(part_refs[n], specp)
            base = q * slots * 2
            for r in range(slots):
                slot = (sid ^ (r // share)) * share + r % share
                a = jnp.minimum(jnp.maximum(pl_ref[base + 2 * slot], 0), events - 1)
                b = jnp.minimum(jnp.maximum(pl_ref[base + 2 * slot + 1], 0), events - 1)
                left = specl[pl.ds(pl.multiple_of(a * pad, pad), pad), :]
                right = specp[pl.ds(pl.multiple_of(b * pad, pad), pad), :]
                lr, li = left[:, :half], left[:, half:]
                rr, ri = right[:, :half], right[:, half:]
                pp = lr * rr
                qq = li * ri
                re = jnp.sum(pp + qq, axis=0, keepdims=True)
                im = jnp.sum(lr * ri - li * rr, axis=0, keepdims=True)
                p0 = jnp.sum(pp[:, :128], axis=0, keepdims=True)
                q0 = jnp.sum(qq[:, :128], axis=0, keepdims=True)
                cross[r:r + 1, 0:128] = jnp.where(lane == 0, p0, re[:, :128])
                cross[r:r + 1, 128:half] = re[:, 128:]
                cross[r:r + 1, half:half + 128] = jnp.where(lane == 0, q0, im[:, :128])
                cross[r:r + 1, half + 128:] = im[:, 128:]
            cb = cross[...].astype(jnp.bfloat16)
            if final:
                allx[(n_prev + n) * slots:(n_prev + n + 1) * slots, :] = cb
            else:
                xout[n_prev + n] = cb

        if final:
            corr = jnp.dot(allx[...], g_ref[...], preferred_element_type=jnp.float32)
            rows = lax.broadcasted_iota(jnp.int32, corr.shape, 0)
            rnd = rows // slots
            rr_ = rows % slots
            slot_of = (sid ^ (rr_ // share)) * share + rr_ % share
            limit = jnp.zeros(corr.shape, jnp.int32)
            for q in range(total_rounds):
                limit = jnp.where(rnd == q, cnt_ref[q], limit)
            corr = jnp.where(slot_of < limit, corr, 0.0)
            for q in range(total_rounds):
                keep_ref[q] = corr[q * slots:q * slots + share]
                for j in range(1, groups):
                    lo = q * slots + j * share
                    send_ref[j - 1, q] = corr[lo:lo + share].astype(jnp.bfloat16)

    return kernel


def rounds_call(pairs, counts, sid, own, partners, fwd, inv, rounds, events, chans, slots, groups,
                prev=None, final=False):
    length = fwd.shape[0]
    lags = inv.shape[1]
    pad = 16
    share = slots // groups
    from_waves = prev is None and own.shape[0] == events * chans
    n_prev = 0 if prev is None else prev.shape[0]
    total = n_prev + len(rounds)
    kernel = make_kernel(events, chans, pad, length, slots, groups, share, rounds, n_prev, from_waves, final)
    smem = pl.BlockSpec(memory_space=pltpu.SMEM)
    vmem = pl.BlockSpec(memory_space=pltpu.VMEM)
    inputs = [pairs, counts, sid, own, *partners, fwd]
    if final:
        inputs.append(inv)
        out_shape = (jax.ShapeDtypeStruct((total, share, lags), jnp.float32),
                     jax.ShapeDtypeStruct((groups - 1, total, share, lags), jnp.bfloat16))
    else:
        out_shape = (jax.ShapeDtypeStruct((total, slots, 2 * length), jnp.bfloat16),)
        if from_waves:
            out_shape += (jax.ShapeDtypeStruct((events * pad, 2 * length), jnp.bfloat16),)
    if prev is not None:
        inputs.append(prev)
    scratch = [
        pltpu.VMEM((events * chans, length), jnp.float32),
        pltpu.VMEM((events * pad, length), jnp.float32),
        pltpu.VMEM((events * pad, 2 * length), jnp.float32),
        pltpu.VMEM((events * pad, 2 * length), jnp.float32),
        pltpu.VMEM((slots, 2 * length), jnp.float32),
    ]
    if final:
        scratch.append(pltpu.VMEM((total * slots, 2 * length), jnp.bfloat16))
    return pl.pallas_call(
        kernel,
        out_shape=out_shape,
        in_specs=[smem, smem, smem] + [vmem] * (len(inputs) - 3),
        out_specs=tuple(vmem for _ in out_shape),
        scratch_shapes=scratch,
    )(*inputs)


def station_sum(keep, send, groups):
    total = keep
    for j in range(1, groups):
        perm = [(s, s ^ j) for s in range(groups)]
        total = total + lax.ppermute(send[j - 1], "station", perm).astype(jnp.float32)
    return total


def shards(waveforms, pair_lists, pair_counts):
    events, stations, comps, length = waveforms.shape
    groups = lax.axis_size("station")
    rounds, slots, _ = pair_lists.shape
    chans = stations * comps
    fwd_np, inv_np = half_tables(length, stations * groups * comps, LAGS)
    fwd = jnp.asarray(fwd_np)
    inv = jnp.asarray(inv_np)
    flat = waveforms.reshape(events * chans, length)
    sid = lax.axis_index("station").astype(jnp.int32).reshape(1)
    pairs = pair_lists.reshape(-1)
    counts = pair_counts.reshape(-1)
    partners = {q: swapped(flat, "region", q) for q in reversed(range(rounds))}
    crosses, spec = rounds_call(pairs, counts, sid, flat, [partners[0]], fwd, inv,
                                [0], events, chans, slots, groups)
    for q in range(1, rounds - 1):
        (crosses,) = rounds_call(pairs, counts, sid, spec, [partners[q]], fwd, inv,
                                 [q], events, chans, slots, groups, prev=crosses)
    keep, send = rounds_call(pairs, counts, sid, spec, [partners[rounds - 1]], fwd, inv,
                             [rounds - 1], events, chans, slots, groups, prev=crosses, final=True)
    return station_sum(keep, send, groups)


def solution(mesh):
    return jax.shard_map(
        shards,
        mesh=mesh,
        in_specs=(P("region", "station", None, None), P(None, "region", None), P(None, "region")),
        out_specs=P(None, ("region", "station"), None),
        check_vma=False,
    )
```

```python
import math

import ml_dtypes
import numpy as np

import jax
import jax.numpy as jnp
from jax import lax
from jax.experimental import pallas as pl
from jax.experimental.pallas import tpu as pltpu
from jax.sharding import PartitionSpec as P

EPS = 1e-06
LAGS = 256


def swapped(block, axis, bit):
    count = lax.axis_size(axis)
    route = []
    for low in range(count):
        high = low | 1 << bit
        if high != low and high < count:
            route += [(low, high), (high, low)]
    return lax.ppermute(block, axis, route)


def half_tables(length, channels, lags):
    period = 2 * length
    half = period // 2
    step = np.float32(2.0 * math.pi / period)
    times = np.arange(length, dtype=np.int64)[:, None]
    freqs = np.arange(half, dtype=np.int64)[None, :]
    angle = step * ((times * freqs) % period).astype(np.float32)
    fwd = np.concatenate([np.cos(angle), -np.sin(angle)], axis=1).astype(np.float32)
    fwd[:, half] = np.where(times[:, 0] % 2 == 0, 1.0, -1.0)
    fwd = fwd.astype(ml_dtypes.bfloat16)

    factor = np.float32(1.0 / (period * math.sqrt(channels * length)))
    rows = np.arange(half, dtype=np.int64)[:, None]
    lagged = np.arange(lags, dtype=np.int64)[None, :] - lags // 2
    angle = step * ((rows * lagged) % period).astype(np.float32)
    cos_t = (np.cos(angle).astype(np.float32) * factor).astype(ml_dtypes.bfloat16).astype(np.float32)
    sin_t = ((-np.sin(angle)).astype(np.float32) * factor).astype(ml_dtypes.bfloat16).astype(np.float32)
    inv = np.zeros((period, lags), np.float32)
    inv[0] = cos_t[0]
    inv[1:half] = 2.0 * cos_t[1:]
    nyq_angle = step * ((half * lagged[0]) % period).astype(np.float32)
    inv[half] = (np.cos(nyq_angle).astype(np.float32) * factor).astype(ml_dtypes.bfloat16).astype(np.float32)
    inv[half + 1:] = 2.0 * sin_t[1:]
    return fwd, inv.astype(ml_dtypes.bfloat16)


def make_kernel(events, chans, pad, length, slots, groups, share, rounds, n_prev, from_waves, final):
    half = length
    n_part = len(rounds)
    total_rounds = n_prev + n_part

    def kernel(*refs):
        pl_ref, cnt_ref, sid_ref, own_ref = refs[:4]
        part_refs = refs[4:4 + n_part]
        rest = list(refs[4 + n_part:])
        f_ref = rest.pop(0)
        g_ref = rest.pop(0) if final else None
        prev_ref = rest.pop(0) if n_prev else None
        if final:
            keep_ref, send_ref = rest.pop(0), rest.pop(0)
        else:
            xout = rest.pop(0)
            spec_out = rest.pop(0) if from_waves else None
        nscr, xpad, specl, specp, cross = rest[:5]
        allx = rest[5] if final else None

        def spectra(w_ref, spec_ref):
            x = w_ref[...].astype(jnp.float32)
            x = x - jnp.mean(x, axis=-1, keepdims=True)
            x = x * lax.rsqrt(jnp.mean(x * x, axis=-1, keepdims=True) + EPS)
            nscr[...] = x
            for e in range(events):
                xpad[e * pad:e * pad + chans, :] = nscr[e * chans:(e + 1) * chans, :]
            xb = xpad[...].astype(jnp.bfloat16)
            spec = jnp.dot(xb, f_ref[...], preferred_element_type=jnp.float32)
            spec_ref[...] = spec.astype(jnp.bfloat16).astype(jnp.float32)

        xpad[...] = jnp.zeros(xpad.shape, jnp.float32)
        if from_waves:
            spectra(own_ref, specl)
            spec_out[...] = specl[...].astype(jnp.bfloat16)
        else:
            specl[...] = own_ref[...].astype(jnp.float32)
            for n in range(n_prev):
                if final:
                    allx[n * slots:(n + 1) * slots, :] = prev_ref[n]
                else:
                    xout[n] = prev_ref[n]

        sid = sid_ref[0]
        lane = lax.broadcasted_iota(jnp.int32, (1, 128), 1)
        for n, q in enumerate(rounds):
            spectra(part_refs[n], specp)
            for r in range(slots):
                slot = (sid ^ (r // share)) * share + r % share
                a = jnp.minimum(jnp.maximum(pl_ref[q, slot, 0], 0), events - 1)
                b = jnp.minimum(jnp.maximum(pl_ref[q, slot, 1], 0), events - 1)
                left = specl[pl.ds(pl.multiple_of(a * pad, pad), pad), :]
                right = specp[pl.ds(pl.multiple_of(b * pad, pad), pad), :]
                lr, li = left[:, :half], left[:, half:]
                rr, ri = right[:, :half], right[:, half:]
                pp = lr * rr
                qq = li * ri
                re = jnp.sum(pp + qq, axis=0, keepdims=True)
                im = jnp.sum(lr * ri - li * rr, axis=0, keepdims=True)
                p0 = jnp.sum(pp[:, :128], axis=0, keepdims=True)
                q0 = jnp.sum(qq[:, :128], axis=0, keepdims=True)
                cross[r:r + 1, 0:128] = jnp.where(lane == 0, p0, re[:, :128])
                cross[r:r + 1, 128:half] = re[:, 128:]
                cross[r:r + 1, half:half + 128] = jnp.where(lane == 0, q0, im[:, :128])
                cross[r:r + 1, half + 128:] = im[:, 128:]
            cb = cross[...].astype(jnp.bfloat16)
            if final:
                allx[(n_prev + n) * slots:(n_prev + n + 1) * slots, :] = cb
            else:
                xout[n_prev + n] = cb

        if final:
            corr = jnp.dot(allx[...], g_ref[...], preferred_element_type=jnp.float32)
            rows = lax.broadcasted_iota(jnp.int32, corr.shape, 0)
            rnd = rows // slots
            rr_ = rows % slots
            slot_of = (sid ^ (rr_ // share)) * share + rr_ % share
            limit = jnp.zeros(corr.shape, jnp.int32)
            for q in range(total_rounds):
                limit = jnp.where(rnd == q, cnt_ref[q], limit)
            corr = jnp.where(slot_of < limit, corr, 0.0)
            for q in range(total_rounds):
                keep_ref[q] = corr[q * slots:q * slots + share]
                for j in range(1, groups):
                    lo = q * slots + j * share
                    send_ref[j - 1, q] = corr[lo:lo + share].astype(jnp.bfloat16)

    return kernel


def rounds_call(pairs, counts, sid, own, partners, fwd, inv, rounds, events, chans, slots, groups,
                prev=None, final=False):
    length = fwd.shape[0]
    lags = inv.shape[1]
    pad = 16
    share = slots // groups
    from_waves = prev is None and own.shape[0] == events * chans
    n_prev = 0 if prev is None else prev.shape[0]
    total = n_prev + len(rounds)
    kernel = make_kernel(events, chans, pad, length, slots, groups, share, rounds, n_prev, from_waves, final)
    smem = pl.BlockSpec(memory_space=pltpu.SMEM)
    vmem = pl.BlockSpec(memory_space=pltpu.VMEM)
    inputs = [pairs, counts, sid, own, *partners, fwd]
    if final:
        inputs.append(inv)
        out_shape = (jax.ShapeDtypeStruct((total, share, lags), jnp.float32),
                     jax.ShapeDtypeStruct((groups - 1, total, share, lags), jnp.bfloat16))
    else:
        out_shape = (jax.ShapeDtypeStruct((total, slots, 2 * length), jnp.bfloat16),)
        if from_waves:
            out_shape += (jax.ShapeDtypeStruct((events * pad, 2 * length), jnp.bfloat16),)
    if prev is not None:
        inputs.append(prev)
    scratch = [
        pltpu.VMEM((events * chans, length), jnp.float32),
        pltpu.VMEM((events * pad, length), jnp.float32),
        pltpu.VMEM((events * pad, 2 * length), jnp.float32),
        pltpu.VMEM((events * pad, 2 * length), jnp.float32),
        pltpu.VMEM((slots, 2 * length), jnp.float32),
    ]
    if final:
        scratch.append(pltpu.VMEM((total * slots, 2 * length), jnp.bfloat16))
    return pl.pallas_call(
        kernel,
        out_shape=out_shape,
        in_specs=[smem, smem, smem] + [vmem] * (len(inputs) - 3),
        out_specs=tuple(vmem for _ in out_shape),
        scratch_shapes=scratch,
    )(*inputs)


def station_sum(keep, send, groups):
    total = keep
    for j in range(1, groups):
        perm = [(s, s ^ j) for s in range(groups)]
        total = total + lax.ppermute(send[j - 1], "station", perm).astype(jnp.float32)
    return total


def shards(waveforms, pair_lists, pair_counts):
    events, stations, comps, length = waveforms.shape
    groups = lax.axis_size("station")
    rounds, slots, _ = pair_lists.shape
    chans = stations * comps
    fwd_np, inv_np = half_tables(length, stations * groups * comps, LAGS)
    fwd = jnp.asarray(fwd_np)
    inv = jnp.asarray(inv_np)
    flat = waveforms.reshape(events * chans, length)
    sid = lax.axis_index("station").astype(jnp.int32).reshape(1)
    pairs = pair_lists
    counts = pair_counts.reshape(-1)
    partners = {q: swapped(flat, "region", q) for q in reversed(range(rounds))}
    crosses, spec = rounds_call(pairs, counts, sid, flat, [partners[0]], fwd, inv,
                                [0], events, chans, slots, groups)
    for q in range(1, rounds - 1):
        (crosses,) = rounds_call(pairs, counts, sid, spec, [partners[q]], fwd, inv,
                                 [q], events, chans, slots, groups, prev=crosses)
    keep, send = rounds_call(pairs, counts, sid, spec, [partners[rounds - 1]], fwd, inv,
                             [rounds - 1], events, chans, slots, groups, prev=crosses, final=True)
    return station_sum(keep, send, groups)


def solution(mesh):
    return jax.shard_map(
        shards,
        mesh=mesh,
        in_specs=(P("region", "station", None, None), P(None, "region", None), P(None, "region")),
        out_specs=P(None, ("region", "station"), None),
        check_vma=False,
    )
```

```python
import math

import ml_dtypes
import numpy as np

import jax
import jax.numpy as jnp
from jax import lax
from jax.experimental import pallas as pl
from jax.experimental.pallas import tpu as pltpu
from jax.sharding import PartitionSpec as P

EPS = 1e-06
LAGS = 256


def swapped(block, axis, bit):
    count = lax.axis_size(axis)
    route = []
    for low in range(count):
        high = low | 1 << bit
        if high != low and high < count:
            route += [(low, high), (high, low)]
    return lax.ppermute(block, axis, route)


def half_tables(length, channels, lags):
    period = 2 * length
    half = period // 2
    step = np.float32(2.0 * math.pi / period)
    times = np.arange(length, dtype=np.int64)[:, None]
    freqs = np.arange(half, dtype=np.int64)[None, :]
    angle = step * ((times * freqs) % period).astype(np.float32)
    fwd = np.concatenate([np.cos(angle), -np.sin(angle)], axis=1).astype(np.float32)
    fwd[:, half] = np.where(times[:, 0] % 2 == 0, 1.0, -1.0)
    fwd = fwd.astype(ml_dtypes.bfloat16)

    factor = np.float32(1.0 / (period * math.sqrt(channels * length)))
    rows = np.arange(half, dtype=np.int64)[:, None]
    lagged = np.arange(lags, dtype=np.int64)[None, :] - lags // 2
    angle = step * ((rows * lagged) % period).astype(np.float32)
    cos_t = (np.cos(angle).astype(np.float32) * factor).astype(ml_dtypes.bfloat16).astype(np.float32)
    sin_t = ((-np.sin(angle)).astype(np.float32) * factor).astype(ml_dtypes.bfloat16).astype(np.float32)
    inv = np.zeros((period, lags), np.float32)
    inv[0] = cos_t[0]
    inv[1:half] = 2.0 * cos_t[1:]
    nyq_angle = step * ((half * lagged[0]) % period).astype(np.float32)
    inv[half] = (np.cos(nyq_angle).astype(np.float32) * factor).astype(ml_dtypes.bfloat16).astype(np.float32)
    inv[half + 1:] = 2.0 * sin_t[1:]
    return fwd, inv.astype(ml_dtypes.bfloat16)


def make_kernel(events, chans, pad, length, slots, groups, share, rounds, n_prev, from_waves, final):
    half = length
    n_part = len(rounds)
    total_rounds = n_prev + n_part

    def kernel(*refs):
        pl_ref, cnt_ref, sid_ref, own_ref = refs[:4]
        part_refs = refs[4:4 + n_part]
        rest = list(refs[4 + n_part:])
        f_ref = rest.pop(0)
        g_ref = rest.pop(0) if final else None
        prev_ref = rest.pop(0) if n_prev else None
        if final:
            keep_ref, send_ref = rest.pop(0), rest.pop(0)
        else:
            xout = rest.pop(0)
            spec_out = rest.pop(0) if from_waves else None
        nscr, xpad, specl, specp, cross = rest[:5]
        allx = rest[5] if final else None

        def spectra(w_ref, spec_ref):
            x = w_ref[...].astype(jnp.float32)
            x = x - jnp.mean(x, axis=-1, keepdims=True)
            x = x * lax.rsqrt(jnp.mean(x * x, axis=-1, keepdims=True) + EPS)
            nscr[...] = x
            for e in range(events):
                xpad[e * pad:e * pad + chans, :] = nscr[e * chans:(e + 1) * chans, :]
            xb = xpad[...].astype(jnp.bfloat16)
            spec = jnp.dot(xb, f_ref[...], preferred_element_type=jnp.float32)
            spec_ref[...] = spec.astype(jnp.bfloat16).astype(jnp.float32)

        xpad[...] = jnp.zeros(xpad.shape, jnp.float32)
        if from_waves:
            spectra(own_ref, specl)
            spec_out[...] = specl[...].astype(jnp.bfloat16)
        else:
            specl[...] = own_ref[...].astype(jnp.float32)
            for n in range(n_prev):
                if final:
                    allx[n * slots:(n + 1) * slots, :] = prev_ref[n]
                else:
                    xout[n] = prev_ref[n]

        sid = sid_ref[0]
        lane = lax.broadcasted_iota(jnp.int32, (1, 128), 1)
        for n, q in enumerate(rounds):
            spectra(part_refs[n], specp)
            for r in range(slots):
                slot = (sid ^ (r // share)) * share + r % share
                a = jnp.minimum(jnp.maximum(pl_ref[q, 0, slot], 0), events - 1)
                b = jnp.minimum(jnp.maximum(pl_ref[q, 1, slot], 0), events - 1)
                left = specl[pl.ds(pl.multiple_of(a * pad, pad), pad), :]
                right = specp[pl.ds(pl.multiple_of(b * pad, pad), pad), :]
                lr, li = left[:, :half], left[:, half:]
                rr, ri = right[:, :half], right[:, half:]
                pp = lr * rr
                qq = li * ri
                re = jnp.sum(pp + qq, axis=0, keepdims=True)
                im = jnp.sum(lr * ri - li * rr, axis=0, keepdims=True)
                p0 = jnp.sum(pp[:, :128], axis=0, keepdims=True)
                q0 = jnp.sum(qq[:, :128], axis=0, keepdims=True)
                cross[r:r + 1, 0:128] = jnp.where(lane == 0, p0, re[:, :128])
                cross[r:r + 1, 128:half] = re[:, 128:]
                cross[r:r + 1, half:half + 128] = jnp.where(lane == 0, q0, im[:, :128])
                cross[r:r + 1, half + 128:] = im[:, 128:]
            cb = cross[...].astype(jnp.bfloat16)
            if final:
                allx[(n_prev + n) * slots:(n_prev + n + 1) * slots, :] = cb
            else:
                xout[n_prev + n] = cb

        if final:
            corr = jnp.dot(allx[...], g_ref[...], preferred_element_type=jnp.float32)
            rows = lax.broadcasted_iota(jnp.int32, corr.shape, 0)
            rnd = rows // slots
            rr_ = rows % slots
            slot_of = (sid ^ (rr_ // share)) * share + rr_ % share
            limit = jnp.zeros(corr.shape, jnp.int32)
            for q in range(total_rounds):
                limit = jnp.where(rnd == q, cnt_ref[q], limit)
            corr = jnp.where(slot_of < limit, corr, 0.0)
            for q in range(total_rounds):
                keep_ref[q] = corr[q * slots:q * slots + share]
                for j in range(1, groups):
                    lo = q * slots + j * share
                    send_ref[j - 1, q] = corr[lo:lo + share].astype(jnp.bfloat16)

    return kernel


def rounds_call(pairs, counts, sid, own, partners, fwd, inv, rounds, events, chans, slots, groups,
                prev=None, final=False):
    length = fwd.shape[0]
    lags = inv.shape[1]
    pad = 16
    share = slots // groups
    from_waves = prev is None and own.shape[0] == events * chans
    n_prev = 0 if prev is None else prev.shape[0]
    total = n_prev + len(rounds)
    kernel = make_kernel(events, chans, pad, length, slots, groups, share, rounds, n_prev, from_waves, final)
    smem = pl.BlockSpec(memory_space=pltpu.SMEM)
    vmem = pl.BlockSpec(memory_space=pltpu.VMEM)
    inputs = [pairs, counts, sid, own, *partners, fwd]
    if final:
        inputs.append(inv)
        out_shape = (jax.ShapeDtypeStruct((total, share, lags), jnp.float32),
                     jax.ShapeDtypeStruct((groups - 1, total, share, lags), jnp.bfloat16))
    else:
        out_shape = (jax.ShapeDtypeStruct((total, slots, 2 * length), jnp.bfloat16),)
        if from_waves:
            out_shape += (jax.ShapeDtypeStruct((events * pad, 2 * length), jnp.bfloat16),)
    if prev is not None:
        inputs.append(prev)
    scratch = [
        pltpu.VMEM((events * chans, length), jnp.float32),
        pltpu.VMEM((events * pad, length), jnp.float32),
        pltpu.VMEM((events * pad, 2 * length), jnp.float32),
        pltpu.VMEM((events * pad, 2 * length), jnp.float32),
        pltpu.VMEM((slots, 2 * length), jnp.float32),
    ]
    if final:
        scratch.append(pltpu.VMEM((total * slots, 2 * length), jnp.bfloat16))
    return pl.pallas_call(
        kernel,
        out_shape=out_shape,
        in_specs=[smem, smem, smem] + [vmem] * (len(inputs) - 3),
        out_specs=tuple(vmem for _ in out_shape),
        scratch_shapes=scratch,
    )(*inputs)


def station_sum(keep, send, groups):
    total = keep
    for j in range(1, groups):
        perm = [(s, s ^ j) for s in range(groups)]
        total = total + lax.ppermute(send[j - 1], "station", perm).astype(jnp.float32)
    return total


def shards(waveforms, pair_lists, pair_counts):
    events, stations, comps, length = waveforms.shape
    groups = lax.axis_size("station")
    rounds, slots, _ = pair_lists.shape
    chans = stations * comps
    fwd_np, inv_np = half_tables(length, stations * groups * comps, LAGS)
    fwd = jnp.asarray(fwd_np)
    inv = jnp.asarray(inv_np)
    flat = waveforms.reshape(events * chans, length)
    sid = lax.axis_index("station").astype(jnp.int32).reshape(1)
    pairs = jnp.transpose(pair_lists, (0, 2, 1))
    counts = pair_counts.reshape(-1)
    partners = {q: swapped(flat, "region", q) for q in reversed(range(rounds))}
    crosses, spec = rounds_call(pairs, counts, sid, flat, [partners[0]], fwd, inv,
                                [0], events, chans, slots, groups)
    for q in range(1, rounds - 1):
        (crosses,) = rounds_call(pairs, counts, sid, spec, [partners[q]], fwd, inv,
                                 [q], events, chans, slots, groups, prev=crosses)
    keep, send = rounds_call(pairs, counts, sid, spec, [partners[rounds - 1]], fwd, inv,
                             [rounds - 1], events, chans, slots, groups, prev=crosses, final=True)
    return station_sum(keep, send, groups)


def solution(mesh):
    return jax.shard_map(
        shards,
        mesh=mesh,
        in_specs=(P("region", "station", None, None), P(None, "region", None), P(None, "region")),
        out_specs=P(None, ("region", "station"), None),
        check_vma=False,
    )
```

```python
import math

import ml_dtypes
import numpy as np

import jax
import jax.numpy as jnp
from jax import lax
from jax.experimental import pallas as pl
from jax.experimental.pallas import tpu as pltpu
from jax.sharding import PartitionSpec as P

EPS = 1e-06
LAGS = 256


def swapped(block, axis, bit):
    count = lax.axis_size(axis)
    route = []
    for low in range(count):
        high = low | 1 << bit
        if high != low and high < count:
            route += [(low, high), (high, low)]
    return lax.ppermute(block, axis, route)


def half_tables(length, channels, lags):
    period = 2 * length
    half = period // 2
    step = np.float32(2.0 * math.pi / period)
    times = np.arange(length, dtype=np.int64)[:, None]
    freqs = np.arange(half, dtype=np.int64)[None, :]
    angle = step * ((times * freqs) % period).astype(np.float32)
    fwd = np.concatenate([np.cos(angle), -np.sin(angle)], axis=1).astype(np.float32)
    fwd[:, half] = np.where(times[:, 0] % 2 == 0, 1.0, -1.0)
    fwd = fwd.astype(ml_dtypes.bfloat16)

    factor = np.float32(1.0 / (period * math.sqrt(channels * length)))
    rows = np.arange(half, dtype=np.int64)[:, None]
    lagged = np.arange(lags, dtype=np.int64)[None, :] - lags // 2
    angle = step * ((rows * lagged) % period).astype(np.float32)
    cos_t = (np.cos(angle).astype(np.float32) * factor).astype(ml_dtypes.bfloat16).astype(np.float32)
    sin_t = ((-np.sin(angle)).astype(np.float32) * factor).astype(ml_dtypes.bfloat16).astype(np.float32)
    inv = np.zeros((period, lags), np.float32)
    inv[0] = cos_t[0]
    inv[1:half] = 2.0 * cos_t[1:]
    nyq_angle = step * ((half * lagged[0]) % period).astype(np.float32)
    inv[half] = (np.cos(nyq_angle).astype(np.float32) * factor).astype(ml_dtypes.bfloat16).astype(np.float32)
    inv[half + 1:] = 2.0 * sin_t[1:]
    return fwd, inv.astype(ml_dtypes.bfloat16)


def make_kernel(events, chans, pad, length, slots, groups, share, rounds, n_prev, from_waves, final):
    half = length
    n_part = len(rounds)
    total_rounds = n_prev + n_part

    def kernel(*refs):
        pl_ref, cnt_ref, sid_ref, own_ref = refs[:4]
        part_refs = refs[4:4 + n_part]
        rest = list(refs[4 + n_part:])
        f_ref = rest.pop(0)
        g_ref = rest.pop(0) if final else None
        prev_ref = rest.pop(0) if n_prev else None
        if final:
            keep_ref, send_ref = rest.pop(0), rest.pop(0)
        else:
            xout = rest.pop(0)
            spec_out = rest.pop(0) if from_waves else None
        nscr, xpad, specl, specp, cross = rest[:5]
        allx = rest[5] if final else None

        def spectra(w_ref, spec_ref):
            x = w_ref[...].astype(jnp.float32)
            x = x - jnp.mean(x, axis=-1, keepdims=True)
            x = x * lax.rsqrt(jnp.mean(x * x, axis=-1, keepdims=True) + EPS)
            nscr[...] = x
            for e in range(events):
                xpad[e * pad:e * pad + chans, :] = nscr[e * chans:(e + 1) * chans, :]
            xb = xpad[...].astype(jnp.bfloat16)
            spec = jnp.dot(xb, f_ref[...], preferred_element_type=jnp.float32)
            spec_ref[...] = spec.astype(jnp.bfloat16).astype(jnp.float32)

        xpad[...] = jnp.zeros(xpad.shape, jnp.float32)
        if from_waves:
            spectra(own_ref, specl)
            spec_out[...] = specl[...].astype(jnp.bfloat16)
        else:
            specl[...] = own_ref[...].astype(jnp.float32)
            for n in range(n_prev):
                if final:
                    allx[n * slots:(n + 1) * slots, :] = prev_ref[n]
                else:
                    xout[n] = prev_ref[n]

        sid = sid_ref[0]
        lane = lax.broadcasted_iota(jnp.int32, (1, 128), 1)
        for n, q in enumerate(rounds):
            spectra(part_refs[n], specp)
            for r in range(slots):
                slot = (sid ^ (r // share)) * share + r % share
                a = jnp.minimum(jnp.maximum(pl_ref[q, 0, slot], 0), events - 1)
                b = jnp.minimum(jnp.maximum(pl_ref[q, 1, slot], 0), events - 1)
                left = specl[pl.ds(pl.multiple_of(a * pad, pad), pad), :]
                right = specp[pl.ds(pl.multiple_of(b * pad, pad), pad), :]
                lr, li = left[:, :half], left[:, half:]
                rr, ri = right[:, :half], right[:, half:]
                pp = lr * rr
                qq = li * ri
                re = jnp.sum(pp + qq, axis=0, keepdims=True)
                im = jnp.sum(lr * ri - li * rr, axis=0, keepdims=True)
                p0 = jnp.sum(pp[:, :128], axis=0, keepdims=True)
                q0 = jnp.sum(qq[:, :128], axis=0, keepdims=True)
                cross[r:r + 1, 0:128] = jnp.where(lane == 0, p0, re[:, :128])
                cross[r:r + 1, 128:half] = re[:, 128:]
                cross[r:r + 1, half:half + 128] = jnp.where(lane == 0, q0, im[:, :128])
                cross[r:r + 1, half + 128:] = im[:, 128:]
            cb = cross[...].astype(jnp.bfloat16)
            if final:
                allx[(n_prev + n) * slots:(n_prev + n + 1) * slots, :] = cb
            else:
                xout[n_prev + n] = cb

        if final:
            corr = jnp.dot(allx[...], g_ref[...], preferred_element_type=jnp.float32)
            rows = lax.broadcasted_iota(jnp.int32, corr.shape, 0)
            rnd = rows // slots
            rr_ = rows % slots
            slot_of = (sid ^ (rr_ // share)) * share + rr_ % share
            limit = jnp.zeros(corr.shape, jnp.int32)
            for q in range(total_rounds):
                limit = jnp.where(rnd == q, cnt_ref[q], limit)
            corr = jnp.where(slot_of < limit, corr, 0.0)
            for q in range(total_rounds):
                keep_ref[q] = corr[q * slots:q * slots + share]
                for j in range(1, groups):
                    lo = q * slots + j * share
                    send_ref[j - 1, q] = corr[lo:lo + share].astype(jnp.bfloat16)

    return kernel


def rounds_call(pairs, counts, sid, own, partners, fwd, inv, rounds, events, chans, slots, groups,
                prev=None, final=False):
    length = fwd.shape[0]
    lags = inv.shape[1]
    pad = 16
    share = slots // groups
    from_waves = prev is None and own.shape[0] == events * chans
    n_prev = 0 if prev is None else prev.shape[0]
    total = n_prev + len(rounds)
    kernel = make_kernel(events, chans, pad, length, slots, groups, share, rounds, n_prev, from_waves, final)
    smem = pl.BlockSpec(memory_space=pltpu.SMEM)
    vmem = pl.BlockSpec(memory_space=pltpu.VMEM)
    inputs = [pairs, counts, sid, own, *partners, fwd]
    if final:
        inputs.append(inv)
        out_shape = (jax.ShapeDtypeStruct((total, share, lags), jnp.float32),
                     jax.ShapeDtypeStruct((groups - 1, total, share, lags), jnp.bfloat16))
    else:
        out_shape = (jax.ShapeDtypeStruct((total, slots, 2 * length), jnp.bfloat16),)
        if from_waves:
            out_shape += (jax.ShapeDtypeStruct((events * pad, 2 * length), jnp.bfloat16),)
    if prev is not None:
        inputs.append(prev)
    scratch = [
        pltpu.VMEM((events * chans, length), jnp.float32),
        pltpu.VMEM((events * pad, length), jnp.float32),
        pltpu.VMEM((events * pad, 2 * length), jnp.float32),
        pltpu.VMEM((events * pad, 2 * length), jnp.float32),
        pltpu.VMEM((slots, 2 * length), jnp.float32),
    ]
    if final:
        scratch.append(pltpu.VMEM((total * slots, 2 * length), jnp.bfloat16))
    return pl.pallas_call(
        kernel,
        out_shape=out_shape,
        in_specs=[smem, smem, smem] + [vmem] * (len(inputs) - 3),
        out_specs=tuple(vmem for _ in out_shape),
        scratch_shapes=scratch,
    )(*inputs)


def station_sum(keep, send, groups):
    total = keep
    for j in range(1, groups):
        perm = [(s, s ^ j) for s in range(groups)]
        total = total + lax.ppermute(send[j - 1], "station", perm).astype(jnp.float32)
    return total


def shards(waveforms, pair_lists, pair_counts):
    events, stations, comps, length = waveforms.shape
    groups = lax.axis_size("station")
    rounds, slots, _ = pair_lists.shape
    chans = stations * comps
    fwd_np, inv_np = half_tables(length, stations * groups * comps, LAGS)
    fwd = jnp.asarray(fwd_np)
    inv = jnp.asarray(inv_np)
    flat = waveforms.reshape(events * chans, length)
    sid = lax.axis_index("station").astype(jnp.int32).reshape(1)
    pairs = jnp.transpose(pair_lists, (0, 2, 1))
    counts = pair_counts.reshape(-1)
    partners = {q: swapped(flat, "region", q) for q in reversed(range(rounds))}
    crosses, spec = rounds_call(pairs, counts, sid, flat, [partners[0]], fwd, inv,
                                [0], events, chans, slots, groups)
    rest = list(range(1, rounds))
    keep, send = rounds_call(pairs, counts, sid, spec, [partners[q] for q in rest], fwd, inv,
                             rest, events, chans, slots, groups, prev=crosses, final=True)
    return station_sum(keep, send, groups)


def solution(mesh):
    return jax.shard_map(
        shards,
        mesh=mesh,
        in_specs=(P("region", "station", None, None), P(None, "region", None), P(None, "region")),
        out_specs=P(None, ("region", "station"), None),
        check_vma=False,
    )
```

```python
import math

import ml_dtypes
import numpy as np

import jax
import jax.numpy as jnp
from jax import lax
from jax.experimental import pallas as pl
from jax.experimental.pallas import tpu as pltpu
from jax.sharding import PartitionSpec as P

EPS = 1e-06
LAGS = 256


def swapped(block, axis, bit):
    count = lax.axis_size(axis)
    route = []
    for low in range(count):
        high = low | 1 << bit
        if high != low and high < count:
            route += [(low, high), (high, low)]
    return lax.ppermute(block, axis, route)


def half_tables(length, channels, lags):
    period = 2 * length
    half = period // 2
    step = np.float32(2.0 * math.pi / period)
    times = np.arange(length, dtype=np.int64)[:, None]
    freqs = np.arange(half, dtype=np.int64)[None, :]
    angle = step * ((times * freqs) % period).astype(np.float32)
    fwd = np.concatenate([np.cos(angle), -np.sin(angle)], axis=1).astype(np.float32)
    fwd[:, half] = np.where(times[:, 0] % 2 == 0, 1.0, -1.0)
    fwd = fwd.astype(ml_dtypes.bfloat16)

    factor = np.float32(1.0 / (period * math.sqrt(channels * length)))
    rows = np.arange(half, dtype=np.int64)[:, None]
    lagged = np.arange(lags, dtype=np.int64)[None, :] - lags // 2
    angle = step * ((rows * lagged) % period).astype(np.float32)
    cos_t = (np.cos(angle).astype(np.float32) * factor).astype(ml_dtypes.bfloat16).astype(np.float32)
    sin_t = ((-np.sin(angle)).astype(np.float32) * factor).astype(ml_dtypes.bfloat16).astype(np.float32)
    inv = np.zeros((period, lags), np.float32)
    inv[0] = cos_t[0]
    inv[1:half] = 2.0 * cos_t[1:]
    nyq_angle = step * ((half * lagged[0]) % period).astype(np.float32)
    inv[half] = (np.cos(nyq_angle).astype(np.float32) * factor).astype(ml_dtypes.bfloat16).astype(np.float32)
    inv[half + 1:] = 2.0 * sin_t[1:]
    return fwd, inv.astype(ml_dtypes.bfloat16)


def make_kernel(events, chans, pad, length, slots, groups, share, rounds, n_prev, from_waves, final):
    half = length
    n_part = len(rounds)
    total_rounds = n_prev + n_part

    def kernel(*refs):
        pl_ref, cnt_ref, sid_ref, own_ref = refs[:4]
        part_refs = refs[4:4 + n_part]
        rest = list(refs[4 + n_part:])
        f_ref = rest.pop(0)
        g_ref = rest.pop(0) if final else None
        prev_ref = rest.pop(0) if n_prev else None
        if final:
            keep_ref, send_ref = rest.pop(0), rest.pop(0)
        else:
            xout = rest.pop(0)
            spec_out = rest.pop(0) if from_waves else None
        nscr, xpad, specl, specall, cross = rest[:5]
        allx = rest[5] if final else None
        sources = ([own_ref] if from_waves else []) + list(part_refs)
        block = events * pad

        xpad[...] = jnp.zeros(xpad.shape, jnp.float32)
        for m, w_ref in enumerate(sources):
            x = w_ref[...].astype(jnp.float32)
            x = x - jnp.mean(x, axis=-1, keepdims=True)
            x = x * lax.rsqrt(jnp.mean(x * x, axis=-1, keepdims=True) + EPS)
            nscr[...] = x
            for e in range(events):
                row = m * block + e * pad
                xpad[row:row + chans, :] = nscr[e * chans:(e + 1) * chans, :]
        xb = xpad[...].astype(jnp.bfloat16)
        spec = jnp.dot(xb, f_ref[...], preferred_element_type=jnp.float32)
        specall[...] = spec.astype(jnp.bfloat16).astype(jnp.float32)

        if from_waves:
            left_ref = specall
            spec_out[...] = specall[0:block, :].astype(jnp.bfloat16)
        else:
            left_ref = specl
            specl[...] = own_ref[...].astype(jnp.float32)
            for n in range(n_prev):
                if final:
                    allx[n * slots:(n + 1) * slots, :] = prev_ref[n]
                else:
                    xout[n] = prev_ref[n]

        sid = sid_ref[0]
        lane = lax.broadcasted_iota(jnp.int32, (1, 128), 1)
        for n, q in enumerate(rounds):
            off = (n + int(from_waves)) * block
            for r in range(slots):
                slot = (sid ^ (r // share)) * share + r % share
                a = jnp.minimum(jnp.maximum(pl_ref[q, 0, slot], 0), events - 1)
                b = jnp.minimum(jnp.maximum(pl_ref[q, 1, slot], 0), events - 1)
                left = left_ref[pl.ds(pl.multiple_of(a * pad, pad), pad), :]
                right = specall[pl.ds(pl.multiple_of(off + b * pad, pad), pad), :]
                lr, li = left[:, :half], left[:, half:]
                rr, ri = right[:, :half], right[:, half:]
                pp = lr * rr
                qq = li * ri
                re = jnp.sum(pp + qq, axis=0, keepdims=True)
                im = jnp.sum(lr * ri - li * rr, axis=0, keepdims=True)
                p0 = jnp.sum(pp[:, :128], axis=0, keepdims=True)
                q0 = jnp.sum(qq[:, :128], axis=0, keepdims=True)
                cross[r:r + 1, 0:128] = jnp.where(lane == 0, p0, re[:, :128])
                cross[r:r + 1, 128:half] = re[:, 128:]
                cross[r:r + 1, half:half + 128] = jnp.where(lane == 0, q0, im[:, :128])
                cross[r:r + 1, half + 128:] = im[:, 128:]
            cb = cross[...].astype(jnp.bfloat16)
            if final:
                allx[(n_prev + n) * slots:(n_prev + n + 1) * slots, :] = cb
            else:
                xout[n_prev + n] = cb

        if final:
            corr = jnp.dot(allx[...], g_ref[...], preferred_element_type=jnp.float32)
            rows = lax.broadcasted_iota(jnp.int32, corr.shape, 0)
            rnd = rows // slots
            rr_ = rows % slots
            slot_of = (sid ^ (rr_ // share)) * share + rr_ % share
            limit = jnp.zeros(corr.shape, jnp.int32)
            for q in range(total_rounds):
                limit = jnp.where(rnd == q, cnt_ref[q], limit)
            corr = jnp.where(slot_of < limit, corr, 0.0)
            for q in range(total_rounds):
                keep_ref[q] = corr[q * slots:q * slots + share]
                for j in range(1, groups):
                    lo = q * slots + j * share
                    send_ref[j - 1, q] = corr[lo:lo + share].astype(jnp.bfloat16)

    return kernel


def rounds_call(pairs, counts, sid, own, partners, fwd, inv, rounds, events, chans, slots, groups,
                prev=None, final=False):
    length = fwd.shape[0]
    lags = inv.shape[1]
    pad = 16
    share = slots // groups
    from_waves = prev is None and own.shape[0] == events * chans
    n_prev = 0 if prev is None else prev.shape[0]
    total = n_prev + len(rounds)
    kernel = make_kernel(events, chans, pad, length, slots, groups, share, rounds, n_prev, from_waves, final)
    smem = pl.BlockSpec(memory_space=pltpu.SMEM)
    vmem = pl.BlockSpec(memory_space=pltpu.VMEM)
    inputs = [pairs, counts, sid, own, *partners, fwd]
    if final:
        inputs.append(inv)
        out_shape = (jax.ShapeDtypeStruct((total, share, lags), jnp.float32),
                     jax.ShapeDtypeStruct((groups - 1, total, share, lags), jnp.bfloat16))
    else:
        out_shape = (jax.ShapeDtypeStruct((total, slots, 2 * length), jnp.bfloat16),)
        if from_waves:
            out_shape += (jax.ShapeDtypeStruct((events * pad, 2 * length), jnp.bfloat16),)
    if prev is not None:
        inputs.append(prev)
    n_src = len(partners) + int(from_waves)
    scratch = [
        pltpu.VMEM((events * chans, length), jnp.float32),
        pltpu.VMEM((n_src * events * pad, length), jnp.float32),
        pltpu.VMEM((events * pad, 2 * length), jnp.float32),
        pltpu.VMEM((n_src * events * pad, 2 * length), jnp.float32),
        pltpu.VMEM((slots, 2 * length), jnp.float32),
    ]
    if final:
        scratch.append(pltpu.VMEM((total * slots, 2 * length), jnp.bfloat16))
    return pl.pallas_call(
        kernel,
        out_shape=out_shape,
        in_specs=[smem, smem, smem] + [vmem] * (len(inputs) - 3),
        out_specs=tuple(vmem for _ in out_shape),
        scratch_shapes=scratch,
    )(*inputs)


def station_sum(keep, send, groups):
    total = keep
    for j in range(1, groups):
        perm = [(s, s ^ j) for s in range(groups)]
        total = total + lax.ppermute(send[j - 1], "station", perm).astype(jnp.float32)
    return total


def shards(waveforms, pair_lists, pair_counts):
    events, stations, comps, length = waveforms.shape
    groups = lax.axis_size("station")
    rounds, slots, _ = pair_lists.shape
    chans = stations * comps
    fwd_np, inv_np = half_tables(length, stations * groups * comps, LAGS)
    fwd = jnp.asarray(fwd_np)
    inv = jnp.asarray(inv_np)
    flat = waveforms.reshape(events * chans, length)
    sid = lax.axis_index("station").astype(jnp.int32).reshape(1)
    pairs = jnp.transpose(pair_lists, (0, 2, 1))
    counts = pair_counts.reshape(-1)
    partners = {q: swapped(flat, "region", q) for q in reversed(range(rounds))}
    crosses, spec = rounds_call(pairs, counts, sid, flat, [partners[0]], fwd, inv,
                                [0], events, chans, slots, groups)
    rest = list(range(1, rounds))
    keep, send = rounds_call(pairs, counts, sid, spec, [partners[q] for q in rest], fwd, inv,
                             rest, events, chans, slots, groups, prev=crosses, final=True)
    return station_sum(keep, send, groups)


def solution(mesh):
    return jax.shard_map(
        shards,
        mesh=mesh,
        in_specs=(P("region", "station", None, None), P(None, "region", None), P(None, "region")),
        out_specs=P(None, ("region", "station"), None),
        check_vma=False,
    )
```

```python
import math

import ml_dtypes
import numpy as np

import jax
import jax.numpy as jnp
from jax import lax
from jax.experimental import pallas as pl
from jax.experimental.pallas import tpu as pltpu
from jax.sharding import PartitionSpec as P

EPS = 1e-06
LAGS = 256


def swapped(block, axis, bit):
    count = lax.axis_size(axis)
    route = []
    for low in range(count):
        high = low | 1 << bit
        if high != low and high < count:
            route += [(low, high), (high, low)]
    return lax.ppermute(block, axis, route)


def half_tables(length, channels, lags):
    period = 2 * length
    half = period // 2
    step = np.float32(2.0 * math.pi / period)
    times = np.arange(length, dtype=np.int64)[:, None]
    freqs = np.arange(half, dtype=np.int64)[None, :]
    angle = step * ((times * freqs) % period).astype(np.float32)
    fwd = np.concatenate([np.cos(angle), -np.sin(angle)], axis=1).astype(np.float32)
    fwd[:, half] = np.where(times[:, 0] % 2 == 0, 1.0, -1.0)
    fwd = fwd.astype(ml_dtypes.bfloat16)

    factor = np.float32(1.0 / (period * math.sqrt(channels * length)))
    rows = np.arange(half, dtype=np.int64)[:, None]
    lagged = np.arange(lags, dtype=np.int64)[None, :] - lags // 2
    angle = step * ((rows * lagged) % period).astype(np.float32)
    cos_t = (np.cos(angle).astype(np.float32) * factor).astype(ml_dtypes.bfloat16).astype(np.float32)
    sin_t = ((-np.sin(angle)).astype(np.float32) * factor).astype(ml_dtypes.bfloat16).astype(np.float32)
    inv = np.zeros((period, lags), np.float32)
    inv[0] = cos_t[0]
    inv[1:half] = 2.0 * cos_t[1:]
    nyq_angle = step * ((half * lagged[0]) % period).astype(np.float32)
    inv[half] = (np.cos(nyq_angle).astype(np.float32) * factor).astype(ml_dtypes.bfloat16).astype(np.float32)
    inv[half + 1:] = 2.0 * sin_t[1:]
    return fwd, inv.astype(ml_dtypes.bfloat16)


def make_kernel(events, chans, pad, length, slots, groups, share, rounds, prev_rounds, from_waves, final):
    half = length
    n_part = len(rounds)
    n_prev = len(prev_rounds)
    total_rounds = n_prev + n_part

    def kernel(*refs):
        pl_ref, cnt_ref, sid_ref, own_ref = refs[:4]
        part_refs = refs[4:4 + n_part]
        rest = list(refs[4 + n_part:])
        f_ref = rest.pop(0)
        g_ref = rest.pop(0) if final else None
        prev_ref = rest.pop(0) if n_prev else None
        if final:
            keep_ref, send_ref = rest.pop(0), rest.pop(0)
        else:
            xout = rest.pop(0)
            spec_out = rest.pop(0) if from_waves else None
        nscr, xpad, specl, specp, cross = rest[:5]
        allx = rest[5] if final else None

        def spectra(w_ref, spec_ref):
            x = w_ref[...].astype(jnp.float32)
            x = x - jnp.mean(x, axis=-1, keepdims=True)
            x = x * lax.rsqrt(jnp.mean(x * x, axis=-1, keepdims=True) + EPS)
            nscr[...] = x
            for e in range(events):
                xpad[e * pad:e * pad + chans, :] = nscr[e * chans:(e + 1) * chans, :]
            xb = xpad[...].astype(jnp.bfloat16)
            spec = jnp.dot(xb, f_ref[...], preferred_element_type=jnp.float32)
            spec_ref[...] = spec.astype(jnp.bfloat16).astype(jnp.float32)

        xpad[...] = jnp.zeros(xpad.shape, jnp.float32)
        if from_waves:
            spectra(own_ref, specl)
            spec_out[...] = specl[...].astype(jnp.bfloat16)
        else:
            specl[...] = own_ref[...].astype(jnp.float32)
            for n, q in enumerate(prev_rounds):
                if final:
                    allx[q * slots:(q + 1) * slots, :] = prev_ref[n]
                else:
                    xout[n] = prev_ref[n]

        sid = sid_ref[0]
        lane = lax.broadcasted_iota(jnp.int32, (1, 128), 1)
        for n, q in enumerate(rounds):
            spectra(part_refs[n], specp)
            for r in range(slots):
                slot = (sid ^ (r // share)) * share + r % share
                a = jnp.minimum(jnp.maximum(pl_ref[q, 0, slot], 0), events - 1)
                b = jnp.minimum(jnp.maximum(pl_ref[q, 1, slot], 0), events - 1)
                left = specl[pl.ds(pl.multiple_of(a * pad, pad), pad), :]
                right = specp[pl.ds(pl.multiple_of(b * pad, pad), pad), :]
                lr, li = left[:, :half], left[:, half:]
                rr, ri = right[:, :half], right[:, half:]
                pp = lr * rr
                qq = li * ri
                re = jnp.sum(pp + qq, axis=0, keepdims=True)
                im = jnp.sum(lr * ri - li * rr, axis=0, keepdims=True)
                p0 = jnp.sum(pp[:, :128], axis=0, keepdims=True)
                q0 = jnp.sum(qq[:, :128], axis=0, keepdims=True)
                cross[r:r + 1, 0:128] = jnp.where(lane == 0, p0, re[:, :128])
                cross[r:r + 1, 128:half] = re[:, 128:]
                cross[r:r + 1, half:half + 128] = jnp.where(lane == 0, q0, im[:, :128])
                cross[r:r + 1, half + 128:] = im[:, 128:]
            cb = cross[...].astype(jnp.bfloat16)
            if final:
                allx[q * slots:(q + 1) * slots, :] = cb
            else:
                xout[n_prev + n] = cb

        if final:
            corr = jnp.dot(allx[...], g_ref[...], preferred_element_type=jnp.float32)
            rows = lax.broadcasted_iota(jnp.int32, corr.shape, 0)
            rnd = rows // slots
            rr_ = rows % slots
            slot_of = (sid ^ (rr_ // share)) * share + rr_ % share
            limit = jnp.zeros(corr.shape, jnp.int32)
            for q in range(total_rounds):
                limit = jnp.where(rnd == q, cnt_ref[q], limit)
            corr = jnp.where(slot_of < limit, corr, 0.0)
            for q in range(total_rounds):
                keep_ref[q] = corr[q * slots:q * slots + share]
                for j in range(1, groups):
                    lo = q * slots + j * share
                    send_ref[j - 1, q] = corr[lo:lo + share].astype(jnp.bfloat16)

    return kernel


def rounds_call(pairs, counts, sid, own, partners, fwd, inv, rounds, events, chans, slots, groups,
                prev=None, prev_rounds=(), final=False):
    length = fwd.shape[0]
    lags = inv.shape[1]
    pad = 16
    share = slots // groups
    from_waves = prev is None and own.shape[0] == events * chans
    n_prev = 0 if prev is None else prev.shape[0]
    total = n_prev + len(rounds)
    kernel = make_kernel(events, chans, pad, length, slots, groups, share, rounds, list(prev_rounds),
                         from_waves, final)
    smem = pl.BlockSpec(memory_space=pltpu.SMEM)
    vmem = pl.BlockSpec(memory_space=pltpu.VMEM)
    inputs = [pairs, counts, sid, own, *partners, fwd]
    if final:
        inputs.append(inv)
        out_shape = (jax.ShapeDtypeStruct((total, share, lags), jnp.float32),
                     jax.ShapeDtypeStruct((groups - 1, total, share, lags), jnp.bfloat16))
    else:
        out_shape = (jax.ShapeDtypeStruct((total, slots, 2 * length), jnp.bfloat16),)
        if from_waves:
            out_shape += (jax.ShapeDtypeStruct((events * pad, 2 * length), jnp.bfloat16),)
    if prev is not None:
        inputs.append(prev)
    scratch = [
        pltpu.VMEM((events * chans, length), jnp.float32),
        pltpu.VMEM((events * pad, length), jnp.float32),
        pltpu.VMEM((events * pad, 2 * length), jnp.float32),
        pltpu.VMEM((events * pad, 2 * length), jnp.float32),
        pltpu.VMEM((slots, 2 * length), jnp.float32),
    ]
    if final:
        scratch.append(pltpu.VMEM((total * slots, 2 * length), jnp.bfloat16))
    return pl.pallas_call(
        kernel,
        out_shape=out_shape,
        in_specs=[smem, smem, smem] + [vmem] * (len(inputs) - 3),
        out_specs=tuple(vmem for _ in out_shape),
        scratch_shapes=scratch,
    )(*inputs)


def station_sum(keep, send, groups):
    total = keep
    for j in range(1, groups):
        perm = [(s, s ^ j) for s in range(groups)]
        total = total + lax.ppermute(send[j - 1], "station", perm).astype(jnp.float32)
    return total


def shards(waveforms, pair_lists, pair_counts):
    events, stations, comps, length = waveforms.shape
    groups = lax.axis_size("station")
    rounds, slots, _ = pair_lists.shape
    chans = stations * comps
    fwd_np, inv_np = half_tables(length, stations * groups * comps, LAGS)
    fwd = jnp.asarray(fwd_np)
    inv = jnp.asarray(inv_np)
    flat = waveforms.reshape(events * chans, length)
    sid = lax.axis_index("station").astype(jnp.int32).reshape(1)
    pairs = jnp.transpose(pair_lists, (0, 2, 1))
    counts = pair_counts.reshape(-1)
    partners = {q: swapped(flat, "region", q) for q in reversed(range(rounds))}
    first = [1 % rounds]
    rest = [q for q in reversed(range(rounds)) if q not in first]
    crosses, spec = rounds_call(pairs, counts, sid, flat, [partners[q] for q in first], fwd, inv,
                                first, events, chans, slots, groups)
    keep, send = rounds_call(pairs, counts, sid, spec, [partners[q] for q in rest], fwd, inv,
                             rest, events, chans, slots, groups, prev=crosses, prev_rounds=first,
                             final=True)
    return station_sum(keep, send, groups)


def solution(mesh):
    return jax.shard_map(
        shards,
        mesh=mesh,
        in_specs=(P("region", "station", None, None), P(None, "region", None), P(None, "region")),
        out_specs=P(None, ("region", "station"), None),
        check_vma=False,
    )
```

```python
import math

import ml_dtypes
import numpy as np

import jax
import jax.numpy as jnp
from jax import lax
from jax.experimental import pallas as pl
from jax.experimental.pallas import tpu as pltpu
from jax.sharding import PartitionSpec as P

EPS = 1e-06
LAGS = 256


def swapped(block, axis, bit):
    count = lax.axis_size(axis)
    route = []
    for low in range(count):
        high = low | 1 << bit
        if high != low and high < count:
            route += [(low, high), (high, low)]
    return lax.ppermute(block, axis, route)


def half_tables(length, channels, lags):
    period = 2 * length
    half = period // 2
    step = np.float32(2.0 * math.pi / period)
    times = np.arange(length, dtype=np.int64)[:, None]
    freqs = np.arange(half, dtype=np.int64)[None, :]
    angle = step * ((times * freqs) % period).astype(np.float32)
    fwd = np.concatenate([np.cos(angle), -np.sin(angle)], axis=1).astype(np.float32)
    fwd[:, half] = np.where(times[:, 0] % 2 == 0, 1.0, -1.0)
    fwd = fwd.astype(ml_dtypes.bfloat16)

    factor = np.float32(1.0 / (period * math.sqrt(channels * length)))
    rows = np.arange(half, dtype=np.int64)[:, None]
    lagged = np.arange(lags, dtype=np.int64)[None, :] - lags // 2
    angle = step * ((rows * lagged) % period).astype(np.float32)
    cos_t = (np.cos(angle).astype(np.float32) * factor).astype(ml_dtypes.bfloat16).astype(np.float32)
    sin_t = ((-np.sin(angle)).astype(np.float32) * factor).astype(ml_dtypes.bfloat16).astype(np.float32)
    inv = np.zeros((period, lags), np.float32)
    inv[0] = cos_t[0]
    inv[1:half] = 2.0 * cos_t[1:]
    nyq_angle = step * ((half * lagged[0]) % period).astype(np.float32)
    inv[half] = (np.cos(nyq_angle).astype(np.float32) * factor).astype(ml_dtypes.bfloat16).astype(np.float32)
    inv[half + 1:] = 2.0 * sin_t[1:]
    return fwd, inv.astype(ml_dtypes.bfloat16)


def make_kernel(events, chans, pad, length, slots, groups, share, rounds, n_prev, from_waves, final):
    half = length
    n_part = len(rounds)
    total_rounds = n_prev + n_part

    def kernel(*refs):
        pl_ref, cnt_ref, sid_ref, own_ref = refs[:4]
        part_refs = refs[4:4 + n_part]
        rest = list(refs[4 + n_part:])
        f_ref = rest.pop(0)
        g_ref = rest.pop(0) if final else None
        prev_ref = rest.pop(0) if n_prev else None
        if final:
            keep_ref, send_ref = rest.pop(0), rest.pop(0)
        else:
            xout = rest.pop(0)
            spec_out = rest.pop(0) if from_waves else None
        nscr, xpad, specl, specp, cross = rest[:5]
        allx = rest[5] if final else None

        def spectra(w_ref, spec_ref):
            x = w_ref[...].astype(jnp.float32)
            x = x - jnp.mean(x, axis=-1, keepdims=True)
            x = x * lax.rsqrt(jnp.mean(x * x, axis=-1, keepdims=True) + EPS)
            nscr[...] = x
            for e in range(events):
                xpad[e * pad:e * pad + chans, :] = nscr[e * chans:(e + 1) * chans, :]
            xb = xpad[...].astype(jnp.bfloat16)
            spec = jnp.dot(xb, f_ref[...], preferred_element_type=jnp.float32)
            spec_ref[...] = spec.astype(jnp.bfloat16).astype(jnp.float32)

        for e in range(events):
            xpad[e * pad + chans:(e + 1) * pad, :] = jnp.zeros((pad - chans, length), jnp.float32)
        if from_waves:
            spectra(own_ref, specl)
            spec_out[...] = specl[...].astype(jnp.bfloat16)
        else:
            specl[...] = own_ref[...].astype(jnp.float32)
            for n in range(n_prev):
                if final:
                    allx[n * slots:(n + 1) * slots, :] = prev_ref[n]
                else:
                    xout[n] = prev_ref[n]

        sid = sid_ref[0]
        lane = lax.broadcasted_iota(jnp.int32, (1, 128), 1)
        for n, q in enumerate(rounds):
            spectra(part_refs[n], specp)
            for r in range(slots):
                slot = (sid ^ (r // share)) * share + r % share
                a = jnp.minimum(jnp.maximum(pl_ref[q, 0, slot], 0), events - 1)
                b = jnp.minimum(jnp.maximum(pl_ref[q, 1, slot], 0), events - 1)
                left = specl[pl.ds(pl.multiple_of(a * pad, pad), pad), :]
                right = specp[pl.ds(pl.multiple_of(b * pad, pad), pad), :]
                lr, li = left[:, :half], left[:, half:]
                rr, ri = right[:, :half], right[:, half:]
                pp = lr * rr
                qq = li * ri
                re = jnp.sum(pp + qq, axis=0, keepdims=True)
                im = jnp.sum(lr * ri - li * rr, axis=0, keepdims=True)
                q0 = jnp.sum(qq[:, :128], axis=0, keepdims=True)
                p0 = jnp.sum(pp[:, :128], axis=0, keepdims=True)
                cross[r:r + 1, 0:128] = jnp.where(lane == 0, p0, re[:, :128])
                cross[r:r + 1, 128:half] = re[:, 128:]
                cross[r:r + 1, half:half + 128] = jnp.where(lane == 0, q0, im[:, :128])
                cross[r:r + 1, half + 128:] = im[:, 128:]
            cb = cross[...].astype(jnp.bfloat16)
            if final:
                allx[(n_prev + n) * slots:(n_prev + n + 1) * slots, :] = cb
            else:
                xout[n_prev + n] = cb

        if final:
            corr = jnp.dot(allx[...], g_ref[...], preferred_element_type=jnp.float32)
            rows = lax.broadcasted_iota(jnp.int32, corr.shape, 0)
            rnd = rows // slots
            rr_ = rows % slots
            slot_of = (sid ^ (rr_ // share)) * share + rr_ % share
            limit = jnp.zeros(corr.shape, jnp.int32)
            for q in range(total_rounds):
                limit = jnp.where(rnd == q, cnt_ref[q], limit)
            corr = jnp.where(slot_of < limit, corr, 0.0)
            for q in range(total_rounds):
                keep_ref[q] = corr[q * slots:q * slots + share]
                for j in range(1, groups):
                    lo = q * slots + j * share
                    send_ref[j - 1, q] = corr[lo:lo + share].astype(jnp.bfloat16)

    return kernel


def rounds_call(pairs, counts, sid, own, partners, fwd, inv, rounds, events, chans, slots, groups,
                prev=None, final=False):
    length = fwd.shape[0]
    lags = inv.shape[1]
    pad = 16
    share = slots // groups
    from_waves = prev is None and own.shape[0] == events * chans
    n_prev = 0 if prev is None else prev.shape[0]
    total = n_prev + len(rounds)
    kernel = make_kernel(events, chans, pad, length, slots, groups, share, rounds, n_prev, from_waves, final)
    smem = pl.BlockSpec(memory_space=pltpu.SMEM)
    vmem = pl.BlockSpec(memory_space=pltpu.VMEM)
    inputs = [pairs, counts, sid, own, *partners, fwd]
    if final:
        inputs.append(inv)
        out_shape = (jax.ShapeDtypeStruct((total, share, lags), jnp.float32),
                     jax.ShapeDtypeStruct((groups - 1, total, share, lags), jnp.bfloat16))
    else:
        out_shape = (jax.ShapeDtypeStruct((total, slots, 2 * length), jnp.bfloat16),)
        if from_waves:
            out_shape += (jax.ShapeDtypeStruct((events * pad, 2 * length), jnp.bfloat16),)
    if prev is not None:
        inputs.append(prev)
    scratch = [
        pltpu.VMEM((events * chans, length), jnp.float32),
        pltpu.VMEM((events * pad, length), jnp.float32),
        pltpu.VMEM((events * pad, 2 * length), jnp.float32),
        pltpu.VMEM((events * pad, 2 * length), jnp.float32),
        pltpu.VMEM((slots, 2 * length), jnp.float32),
    ]
    if final:
        scratch.append(pltpu.VMEM((total * slots, 2 * length), jnp.bfloat16))
    return pl.pallas_call(
        kernel,
        out_shape=out_shape,
        in_specs=[smem, smem, smem] + [vmem] * (len(inputs) - 3),
        out_specs=tuple(vmem for _ in out_shape),
        scratch_shapes=scratch,
        compiler_params=pltpu.CompilerParams(),
    )(*inputs)


def station_sum(keep, send, groups):
    total = keep
    for j in range(1, groups):
        perm = [(s, s ^ j) for s in range(groups)]
        total = total + lax.ppermute(send[j - 1], "station", perm).astype(jnp.float32)
    return total


def shards(waveforms, pair_lists, pair_counts):
    events, stations, comps, length = waveforms.shape
    groups = lax.axis_size("station")
    rounds, slots, _ = pair_lists.shape
    chans = stations * comps
    fwd_np, inv_np = half_tables(length, stations * groups * comps, LAGS)
    fwd = jnp.asarray(fwd_np)
    inv = jnp.asarray(inv_np)
    flat = waveforms.reshape(events * chans, length)
    sid = lax.axis_index("station").astype(jnp.int32).reshape(1)
    pairs = jnp.transpose(pair_lists, (0, 2, 1))
    counts = pair_counts.reshape(-1)
    partners = {q: swapped(flat, "region", q) for q in reversed(range(rounds))}
    crosses, spec = rounds_call(pairs, counts, sid, flat, [partners[0]], fwd, inv,
                                [0], events, chans, slots, groups)
    rest = list(range(1, rounds))
    keep, send = rounds_call(pairs, counts, sid, spec, [partners[q] for q in rest], fwd, inv,
                             rest, events, chans, slots, groups, prev=crosses, final=True)
    return station_sum(keep, send, groups)


def solution(mesh):
    return jax.shard_map(
        shards,
        mesh=mesh,
        in_specs=(P("region", "station", None, None), P(None, "region", None), P(None, "region")),
        out_specs=P(None, ("region", "station"), None),
        check_vma=False,
    )
```

```python
import math

import ml_dtypes
import numpy as np

import jax
import jax.numpy as jnp
from jax import lax
from jax.experimental import pallas as pl
from jax.experimental.pallas import tpu as pltpu
from jax.sharding import PartitionSpec as P

EPS = 1e-06
LAGS = 256


def swapped(block, axis, bit):
    count = lax.axis_size(axis)
    route = []
    for low in range(count):
        high = low | 1 << bit
        if high != low and high < count:
            route += [(low, high), (high, low)]
    return lax.ppermute(block, axis, route)


def half_tables(length, channels, lags):
    period = 2 * length
    half = period // 2
    step = np.float32(2.0 * math.pi / period)
    times = np.arange(length, dtype=np.int64)[:, None]
    freqs = np.arange(half, dtype=np.int64)[None, :]
    angle = step * ((times * freqs) % period).astype(np.float32)
    fwd = np.concatenate([np.cos(angle), -np.sin(angle)], axis=1).astype(np.float32)
    fwd[:, half] = np.where(times[:, 0] % 2 == 0, 1.0, -1.0)
    fwd = fwd.astype(ml_dtypes.bfloat16)

    factor = np.float32(1.0 / (period * math.sqrt(channels * length)))
    rows = np.arange(half, dtype=np.int64)[:, None]
    lagged = np.arange(lags, dtype=np.int64)[None, :] - lags // 2
    angle = step * ((rows * lagged) % period).astype(np.float32)
    cos_t = (np.cos(angle).astype(np.float32) * factor).astype(ml_dtypes.bfloat16).astype(np.float32)
    sin_t = ((-np.sin(angle)).astype(np.float32) * factor).astype(ml_dtypes.bfloat16).astype(np.float32)
    inv = np.zeros((period, lags), np.float32)
    inv[0] = cos_t[0]
    inv[1:half] = 2.0 * cos_t[1:]
    nyq_angle = step * ((half * lagged[0]) % period).astype(np.float32)
    inv[half] = (np.cos(nyq_angle).astype(np.float32) * factor).astype(ml_dtypes.bfloat16).astype(np.float32)
    inv[half + 1:] = 2.0 * sin_t[1:]
    return fwd, inv.astype(ml_dtypes.bfloat16)


def make_kernel(events, chans, pad, length, slots, groups, share, rounds, n_prev, from_waves, final):
    half = length
    n_part = len(rounds)
    total_rounds = n_prev + n_part

    def kernel(*refs):
        pl_ref, cnt_ref, sid_ref, own_ref = refs[:4]
        part_refs = refs[4:4 + n_part]
        rest = list(refs[4 + n_part:])
        f_ref = rest.pop(0)
        g_ref = rest.pop(0) if final else None
        prev_ref = rest.pop(0) if n_prev else None
        if final:
            keep_ref = rest.pop(0)
            send_refs = [rest.pop(0) for _ in range(groups - 1)]
        else:
            xout = rest.pop(0)
            spec_out = rest.pop(0) if from_waves else None
        nscr, xpad, specl, specp, cross = rest[:5]
        allx = rest[5] if final else None

        def spectra(w_ref, spec_ref):
            x = w_ref[...].astype(jnp.float32)
            x = x - jnp.mean(x, axis=-1, keepdims=True)
            x = x * lax.rsqrt(jnp.mean(x * x, axis=-1, keepdims=True) + EPS)
            nscr[...] = x
            for e in range(events):
                xpad[e * pad:e * pad + chans, :] = nscr[e * chans:(e + 1) * chans, :]
            xb = xpad[...].astype(jnp.bfloat16)
            spec = jnp.dot(xb, f_ref[...], preferred_element_type=jnp.float32)
            spec_ref[...] = spec.astype(jnp.bfloat16).astype(jnp.float32)

        xpad[...] = jnp.zeros(xpad.shape, jnp.float32)
        if from_waves:
            spectra(own_ref, specl)
            spec_out[...] = specl[...].astype(jnp.bfloat16)
        else:
            specl[...] = own_ref[...].astype(jnp.float32)
            for n in range(n_prev):
                if final:
                    allx[n * slots:(n + 1) * slots, :] = prev_ref[n]
                else:
                    xout[n] = prev_ref[n]

        sid = sid_ref[0]
        lane = lax.broadcasted_iota(jnp.int32, (1, 128), 1)
        for n, q in enumerate(rounds):
            spectra(part_refs[n], specp)
            for r in range(slots):
                slot = (sid ^ (r // share)) * share + r % share
                a = jnp.minimum(jnp.maximum(pl_ref[q, 0, slot], 0), events - 1)
                b = jnp.minimum(jnp.maximum(pl_ref[q, 1, slot], 0), events - 1)
                left = specl[pl.ds(pl.multiple_of(a * pad, pad), pad), :]
                right = specp[pl.ds(pl.multiple_of(b * pad, pad), pad), :]
                lr, li = left[:, :half], left[:, half:]
                rr, ri = right[:, :half], right[:, half:]
                pp = lr * rr
                qq = li * ri
                re = jnp.sum(pp + qq, axis=0, keepdims=True)
                im = jnp.sum(lr * ri - li * rr, axis=0, keepdims=True)
                p0 = jnp.sum(pp[:, :128], axis=0, keepdims=True)
                q0 = jnp.sum(qq[:, :128], axis=0, keepdims=True)
                cross[r:r + 1, 0:128] = jnp.where(lane == 0, p0, re[:, :128])
                cross[r:r + 1, 128:half] = re[:, 128:]
                cross[r:r + 1, half:half + 128] = jnp.where(lane == 0, q0, im[:, :128])
                cross[r:r + 1, half + 128:] = im[:, 128:]
            cb = cross[...].astype(jnp.bfloat16)
            if final:
                allx[(n_prev + n) * slots:(n_prev + n + 1) * slots, :] = cb
            else:
                xout[n_prev + n] = cb

        if final:
            corr = jnp.dot(allx[...], g_ref[...], preferred_element_type=jnp.float32)
            rows = lax.broadcasted_iota(jnp.int32, corr.shape, 0)
            rnd = rows // slots
            rr_ = rows % slots
            slot_of = (sid ^ (rr_ // share)) * share + rr_ % share
            limit = jnp.zeros(corr.shape, jnp.int32)
            for q in range(total_rounds):
                limit = jnp.where(rnd == q, cnt_ref[q], limit)
            corr = jnp.where(slot_of < limit, corr, 0.0)
            for q in range(total_rounds):
                keep_ref[q] = corr[q * slots:q * slots + share]
                for j in range(1, groups):
                    lo = q * slots + j * share
                    send_refs[j - 1][q] = corr[lo:lo + share]

    return kernel


def rounds_call(pairs, counts, sid, own, partners, fwd, inv, rounds, events, chans, slots, groups,
                prev=None, final=False):
    length = fwd.shape[0]
    lags = inv.shape[1]
    pad = 16
    share = slots // groups
    from_waves = prev is None and own.shape[0] == events * chans
    n_prev = 0 if prev is None else prev.shape[0]
    total = n_prev + len(rounds)
    kernel = make_kernel(events, chans, pad, length, slots, groups, share, rounds, n_prev, from_waves, final)
    smem = pl.BlockSpec(memory_space=pltpu.SMEM)
    vmem = pl.BlockSpec(memory_space=pltpu.VMEM)
    inputs = [pairs, counts, sid, own, *partners, fwd]
    if final:
        inputs.append(inv)
        out_shape = tuple(jax.ShapeDtypeStruct((total, share, lags), jnp.float32) for _ in range(groups))
    else:
        out_shape = (jax.ShapeDtypeStruct((total, slots, 2 * length), jnp.bfloat16),)
        if from_waves:
            out_shape += (jax.ShapeDtypeStruct((events * pad, 2 * length), jnp.bfloat16),)
    if prev is not None:
        inputs.append(prev)
    scratch = [
        pltpu.VMEM((events * chans, length), jnp.float32),
        pltpu.VMEM((events * pad, length), jnp.float32),
        pltpu.VMEM((events * pad, 2 * length), jnp.float32),
        pltpu.VMEM((events * pad, 2 * length), jnp.float32),
        pltpu.VMEM((slots, 2 * length), jnp.float32),
    ]
    if final:
        scratch.append(pltpu.VMEM((total * slots, 2 * length), jnp.bfloat16))
    return pl.pallas_call(
        kernel,
        out_shape=out_shape,
        in_specs=[smem, smem, smem] + [vmem] * (len(inputs) - 3),
        out_specs=tuple(vmem for _ in out_shape),
        scratch_shapes=scratch,
    )(*inputs)


def station_sum(keep, send, groups):
    total = keep
    for j in range(1, groups):
        perm = [(s, s ^ j) for s in range(groups)]
        total = total + lax.ppermute(send[j - 1], "station", perm).astype(jnp.float32)
    return total


def shards(waveforms, pair_lists, pair_counts):
    events, stations, comps, length = waveforms.shape
    groups = lax.axis_size("station")
    rounds, slots, _ = pair_lists.shape
    chans = stations * comps
    fwd_np, inv_np = half_tables(length, stations * groups * comps, LAGS)
    fwd = jnp.asarray(fwd_np)
    inv = jnp.asarray(inv_np)
    flat = waveforms.reshape(events * chans, length)
    sid = lax.axis_index("station").astype(jnp.int32).reshape(1)
    pairs = jnp.transpose(pair_lists, (0, 2, 1))
    counts = pair_counts.reshape(-1)
    partners = {q: swapped(flat, "region", q) for q in reversed(range(rounds))}
    crosses, spec = rounds_call(pairs, counts, sid, flat, [partners[0]], fwd, inv,
                                [0], events, chans, slots, groups)
    rest = list(range(1, rounds))
    keep, *send = rounds_call(pairs, counts, sid, spec, [partners[q] for q in rest], fwd, inv,
                             rest, events, chans, slots, groups, prev=crosses, final=True)
    return station_sum(keep, send, groups)


def solution(mesh):
    return jax.shard_map(
        shards,
        mesh=mesh,
        in_specs=(P("region", "station", None, None), P(None, "region", None), P(None, "region")),
        out_specs=P(None, ("region", "station"), None),
        check_vma=False,
    )
```

```python
import math

import ml_dtypes
import numpy as np

import jax
import jax.numpy as jnp
from jax import lax
from jax.experimental import pallas as pl
from jax.experimental.pallas import tpu as pltpu
from jax.sharding import PartitionSpec as P

EPS = 1e-06
LAGS = 256


def swapped(block, axis, bit):
    count = lax.axis_size(axis)
    route = []
    for low in range(count):
        high = low | 1 << bit
        if high != low and high < count:
            route += [(low, high), (high, low)]
    return lax.ppermute(block, axis, route)


def half_tables(length, channels, lags):
    period = 2 * length
    half = period // 2
    step = np.float32(2.0 * math.pi / period)
    times = np.arange(length, dtype=np.int64)[:, None]
    freqs = np.arange(half, dtype=np.int64)[None, :]
    angle = step * ((times * freqs) % period).astype(np.float32)
    fwd = np.concatenate([np.cos(angle), -np.sin(angle)], axis=1).astype(np.float32)
    fwd[:, half] = np.where(times[:, 0] % 2 == 0, 1.0, -1.0)
    fwd = fwd.astype(ml_dtypes.bfloat16)

    factor = np.float32(1.0 / (period * math.sqrt(channels * length)))
    rows = np.arange(half, dtype=np.int64)[:, None]
    lagged = np.arange(lags, dtype=np.int64)[None, :] - lags // 2
    angle = step * ((rows * lagged) % period).astype(np.float32)
    cos_t = (np.cos(angle).astype(np.float32) * factor).astype(ml_dtypes.bfloat16).astype(np.float32)
    sin_t = ((-np.sin(angle)).astype(np.float32) * factor).astype(ml_dtypes.bfloat16).astype(np.float32)
    inv = np.zeros((period, lags), np.float32)
    inv[0] = cos_t[0]
    inv[1:half] = 2.0 * cos_t[1:]
    nyq_angle = step * ((half * lagged[0]) % period).astype(np.float32)
    inv[half] = (np.cos(nyq_angle).astype(np.float32) * factor).astype(ml_dtypes.bfloat16).astype(np.float32)
    inv[half + 1:] = 2.0 * sin_t[1:]
    return fwd, inv.astype(ml_dtypes.bfloat16)


def make_kernel(events, chans, pad, length, slots, groups, share, rounds, n_prev, from_waves, final):
    half = length
    n_part = len(rounds)
    total_rounds = n_prev + n_part

    def kernel(*refs):
        pl_ref, cnt_ref, sid_ref, own_ref = refs[:4]
        part_refs = refs[4:4 + n_part]
        rest = list(refs[4 + n_part:])
        f_ref = rest.pop(0)
        g_ref = rest.pop(0) if final else None
        prev_ref = rest.pop(0) if n_prev else None
        if final:
            keep_ref, send_ref = rest.pop(0), rest.pop(0)
        else:
            xout = rest.pop(0)
            spec_out = rest.pop(0) if from_waves else None
        nscr, xpad, specl, specp, cross = rest[:5]
        allx = rest[5] if final else None

        def spectra(w_ref, spec_ref):
            x = w_ref[...].astype(jnp.float32)
            x = x - jnp.mean(x, axis=-1, keepdims=True)
            x = x * lax.rsqrt(jnp.mean(x * x, axis=-1, keepdims=True) + EPS)
            nscr[...] = x
            for e in range(events):
                xpad[e * pad:e * pad + chans, :] = nscr[e * chans:(e + 1) * chans, :]
            xb = xpad[...].astype(jnp.bfloat16)
            spec = jnp.dot(xb, f_ref[...], preferred_element_type=jnp.float32)
            spec_ref[...] = spec.astype(jnp.bfloat16).astype(jnp.float32)

        xpad[...] = jnp.zeros(xpad.shape, jnp.float32)
        if from_waves:
            spectra(own_ref, specl)
            spec_out[...] = specl[...].astype(jnp.bfloat16)
        else:
            specl[...] = own_ref[...].astype(jnp.float32)
            for n in range(n_prev):
                if final:
                    allx[n * slots:(n + 1) * slots, :] = prev_ref[n]
                else:
                    xout[n] = prev_ref[n]

        sid = sid_ref[0]
        lane = lax.broadcasted_iota(jnp.int32, (1, 128), 1)
        for n, q in enumerate(rounds):
            spectra(part_refs[n], specp)
            for r in range(slots):
                slot = (sid ^ (r // share)) * share + r % share
                a = jnp.minimum(jnp.maximum(pl_ref[q, 0, slot], 0), events - 1)
                b = jnp.minimum(jnp.maximum(pl_ref[q, 1, slot], 0), events - 1)
                left = specl[pl.ds(pl.multiple_of(a * pad, pad), pad), :]
                right = specp[pl.ds(pl.multiple_of(b * pad, pad), pad), :]
                lr, li = left[:, :half], left[:, half:]
                rr, ri = right[:, :half], right[:, half:]
                pp = lr * rr
                qq = li * ri
                re = jnp.sum(pp + qq, axis=0, keepdims=True)
                im = jnp.sum(lr * ri - li * rr, axis=0, keepdims=True)
                p0 = jnp.sum(pp[:, :128], axis=0, keepdims=True)
                q0 = jnp.sum(qq[:, :128], axis=0, keepdims=True)
                cross[r:r + 1, 0:128] = jnp.where(lane == 0, p0, re[:, :128])
                cross[r:r + 1, 128:half] = re[:, 128:]
                cross[r:r + 1, half:half + 128] = jnp.where(lane == 0, q0, im[:, :128])
                cross[r:r + 1, half + 128:] = im[:, 128:]
            cb = cross[...].astype(jnp.bfloat16)
            if final:
                allx[(n_prev + n) * slots:(n_prev + n + 1) * slots, :] = cb
            else:
                xout[n_prev + n] = cb

        if final:
            corr = jnp.dot(allx[...], g_ref[...], preferred_element_type=jnp.float32)
            rows = lax.broadcasted_iota(jnp.int32, corr.shape, 0)
            rnd = rows // slots
            rr_ = rows % slots
            slot_of = (sid ^ (rr_ // share)) * share + rr_ % share
            limit = jnp.zeros(corr.shape, jnp.int32)
            for q in range(total_rounds):
                limit = jnp.where(rnd == q, cnt_ref[q], limit)
            corr = jnp.where(slot_of < limit, corr, 0.0)
            for q in range(total_rounds):
                keep_ref[q] = corr[q * slots:q * slots + share]
                for j in range(1, groups):
                    lo = q * slots + j * share
                    send_ref[j - 1, q] = corr[lo:lo + share].astype(jnp.bfloat16)

    return kernel


def rounds_call(pairs, counts, sid, own, partners, fwd, inv, rounds, events, chans, slots, groups,
                prev=None, final=False):
    length = fwd.shape[0]
    lags = inv.shape[1]
    pad = 16
    share = slots // groups
    from_waves = prev is None and own.shape[0] == events * chans
    n_prev = 0 if prev is None else prev.shape[0]
    total = n_prev + len(rounds)
    kernel = make_kernel(events, chans, pad, length, slots, groups, share, rounds, n_prev, from_waves, final)
    smem = pl.BlockSpec(memory_space=pltpu.SMEM)
    vmem = pl.BlockSpec(memory_space=pltpu.VMEM)
    inputs = [pairs, counts, sid, own, *partners, fwd]
    if final:
        inputs.append(inv)
        out_shape = (jax.ShapeDtypeStruct((total, share, lags), jnp.float32),
                     jax.ShapeDtypeStruct((groups - 1, total, share, lags), jnp.bfloat16))
    else:
        out_shape = (jax.ShapeDtypeStruct((total, slots, 2 * length), jnp.bfloat16),)
        if from_waves:
            out_shape += (jax.ShapeDtypeStruct((events * pad, 2 * length), jnp.bfloat16),)
    if prev is not None:
        inputs.append(prev)
    scratch = [
        pltpu.VMEM((events * chans, length), jnp.float32),
        pltpu.VMEM((events * pad, length), jnp.float32),
        pltpu.VMEM((events * pad, 2 * length), jnp.float32),
        pltpu.VMEM((events * pad, 2 * length), jnp.float32),
        pltpu.VMEM((slots, 2 * length), jnp.float32),
    ]
    if final:
        scratch.append(pltpu.VMEM((total * slots, 2 * length), jnp.bfloat16))
    return pl.pallas_call(
        kernel,
        out_shape=out_shape,
        in_specs=[smem, smem, smem] + [vmem] * (len(inputs) - 3),
        out_specs=tuple(vmem for _ in out_shape),
        scratch_shapes=scratch,
    )(*inputs)


def station_sum(keep, send, groups):
    total = keep
    for j in range(1, groups):
        perm = [(s, s ^ j) for s in range(groups)]
        total = total + lax.ppermute(send[j - 1], "station", perm).astype(jnp.float32)
    return total


def shards(waveforms, pair_lists, pair_counts):
    events, stations, comps, length = waveforms.shape
    groups = lax.axis_size("station")
    rounds, slots, _ = pair_lists.shape
    chans = stations * comps
    fwd_np, inv_np = half_tables(length, stations * groups * comps, LAGS)
    fwd = jnp.asarray(fwd_np)
    inv = jnp.asarray(inv_np)
    flat = jnp.transpose(waveforms, (0, 2, 1, 3)).reshape(events * chans, length)
    sid = lax.axis_index("station").astype(jnp.int32).reshape(1)
    pairs = jnp.transpose(pair_lists, (0, 2, 1))
    counts = pair_counts.reshape(-1)
    partners = {q: swapped(flat, "region", q) for q in reversed(range(rounds))}
    crosses, spec = rounds_call(pairs, counts, sid, flat, [partners[0]], fwd, inv,
                                [0], events, chans, slots, groups)
    rest = list(range(1, rounds))
    keep, send = rounds_call(pairs, counts, sid, spec, [partners[q] for q in rest], fwd, inv,
                             rest, events, chans, slots, groups, prev=crosses, final=True)
    return station_sum(keep, send, groups)


def solution(mesh):
    return jax.shard_map(
        shards,
        mesh=mesh,
        in_specs=(P("region", "station", None, None), P(None, "region", None), P(None, "region")),
        out_specs=P(None, ("region", "station"), None),
        check_vma=False,
    )
```

```python
import math

import ml_dtypes
import numpy as np

import jax
import jax.numpy as jnp
from jax import lax
from jax.experimental import pallas as pl
from jax.experimental.pallas import tpu as pltpu
from jax.sharding import PartitionSpec as P

EPS = 1e-06
LAGS = 256


def swapped(block, axis, bit):
    count = lax.axis_size(axis)
    route = []
    for low in range(count):
        high = low | 1 << bit
        if high != low and high < count:
            route += [(low, high), (high, low)]
    return lax.ppermute(block, axis, route)


def half_tables(length, channels, lags):
    period = 2 * length
    half = period // 2
    step = np.float32(2.0 * math.pi / period)
    times = np.arange(length, dtype=np.int64)[:, None]
    freqs = np.arange(half, dtype=np.int64)[None, :]
    angle = step * ((times * freqs) % period).astype(np.float32)
    fwd = np.concatenate([np.cos(angle), -np.sin(angle)], axis=1).astype(np.float32)
    fwd[:, half] = np.where(times[:, 0] % 2 == 0, 1.0, -1.0)
    fwd = fwd.astype(ml_dtypes.bfloat16)

    factor = np.float32(1.0 / (period * math.sqrt(channels * length)))
    rows = np.arange(half, dtype=np.int64)[:, None]
    lagged = np.arange(lags, dtype=np.int64)[None, :] - lags // 2
    angle = step * ((rows * lagged) % period).astype(np.float32)
    cos_t = (np.cos(angle).astype(np.float32) * factor).astype(ml_dtypes.bfloat16).astype(np.float32)
    sin_t = ((-np.sin(angle)).astype(np.float32) * factor).astype(ml_dtypes.bfloat16).astype(np.float32)
    inv = np.zeros((period, lags), np.float32)
    inv[0] = cos_t[0]
    inv[1:half] = 2.0 * cos_t[1:]
    nyq_angle = step * ((half * lagged[0]) % period).astype(np.float32)
    inv[half] = (np.cos(nyq_angle).astype(np.float32) * factor).astype(ml_dtypes.bfloat16).astype(np.float32)
    inv[half + 1:] = 2.0 * sin_t[1:]
    return fwd, inv.astype(ml_dtypes.bfloat16)


def make_kernel(events, chans, pad, length, slots, groups, share, rounds, n_prev, from_waves, final):
    half = length
    n_part = len(rounds)
    total_rounds = n_prev + n_part

    def kernel(*refs):
        pl_ref, cnt_ref, sid_ref, own_ref = refs[:4]
        part_refs = refs[4:4 + n_part]
        rest = list(refs[4 + n_part:])
        f_ref = rest.pop(0)
        g_ref = rest.pop(0) if final else None
        prev_ref = rest.pop(0) if n_prev else None
        if final:
            keep_ref, send_ref = rest.pop(0), rest.pop(0)
        else:
            xout = rest.pop(0)
            spec_out = rest.pop(0) if from_waves else None
        nscr, xpad, specl, specp, cross = rest[:5]
        allx = rest[5] if final else None

        def spectra(w_ref, spec_ref):
            x = w_ref[...].astype(jnp.float32)
            x = x - jnp.mean(x, axis=-1, keepdims=True)
            x = x * lax.rsqrt(jnp.mean(x * x, axis=-1, keepdims=True) + EPS)
            nscr[...] = x
            for e in range(events):
                xpad[e * pad:e * pad + chans, :] = nscr[e * chans:(e + 1) * chans, :]
            xb = xpad[...].astype(jnp.bfloat16)
            spec = jnp.dot(xb, f_ref[...], preferred_element_type=jnp.float32)
            spec_ref[...] = spec.astype(jnp.bfloat16).astype(jnp.float32)

        xpad[...] = jnp.zeros(xpad.shape, jnp.float32)
        if from_waves:
            spectra(own_ref, specl)
            spec_out[...] = specl[...].astype(jnp.bfloat16)
        else:
            specl[...] = own_ref[...].astype(jnp.float32)
            for n in range(n_prev):
                if final:
                    allx[n * slots:(n + 1) * slots, :] = prev_ref[n]
                else:
                    xout[n] = prev_ref[n]

        sid = sid_ref[0]
        lane = lax.broadcasted_iota(jnp.int32, (1, 128), 1)
        for n, q in enumerate(rounds):
            spectra(part_refs[n], specp)
            for r in range(slots):
                slot = (sid ^ (r // share)) * share + r % share
                a = jnp.minimum(jnp.maximum(pl_ref[q, 0, slot], 0), events - 1)
                b = jnp.minimum(jnp.maximum(pl_ref[q, 1, slot], 0), events - 1)
                left = specl[pl.ds(pl.multiple_of(a * pad, pad), pad), :]
                right = specp[pl.ds(pl.multiple_of(b * pad, pad), pad), :]
                lr, li = left[:, :half], left[:, half:]
                rr, ri = right[:, :half], right[:, half:]
                pp = lr * rr
                qq = li * ri
                re = jnp.sum(pp + qq, axis=0, keepdims=True)
                im = jnp.sum(lr * ri - li * rr, axis=0, keepdims=True)
                p0 = jnp.sum(pp[:, :128], axis=0, keepdims=True)
                q0 = jnp.sum(qq[:, :128], axis=0, keepdims=True)
                cross[r:r + 1, 0:128] = jnp.where(lane == 0, p0, re[:, :128])
                cross[r:r + 1, 128:half] = re[:, 128:]
                cross[r:r + 1, half:half + 128] = jnp.where(lane == 0, q0, im[:, :128])
                cross[r:r + 1, half + 128:] = im[:, 128:]
            cb = cross[...].astype(jnp.bfloat16)
            if final:
                allx[(n_prev + n) * slots:(n_prev + n + 1) * slots, :] = cb
            else:
                xout[n_prev + n] = cb

        if final:
            corr = jnp.dot(allx[...], g_ref[...], preferred_element_type=jnp.float32)
            rows = lax.broadcasted_iota(jnp.int32, corr.shape, 0)
            rnd = rows // slots
            rr_ = rows % slots
            slot_of = (sid ^ (rr_ // share)) * share + rr_ % share
            limit = jnp.zeros(corr.shape, jnp.int32)
            for q in range(total_rounds):
                limit = jnp.where(rnd == q, cnt_ref[q], limit)
            corr = jnp.where(slot_of < limit, corr, 0.0)
            for q in range(total_rounds):
                keep_ref[q] = corr[q * slots:q * slots + share]
                for j in range(1, groups):
                    lo = q * slots + j * share
                    send_ref[j - 1, q] = corr[lo:lo + share].astype(jnp.bfloat16)

    return kernel


def rounds_call(pairs, counts, sid, own, partners, fwd, inv, rounds, events, chans, slots, groups,
                prev=None, final=False):
    length = fwd.shape[0]
    lags = inv.shape[1]
    pad = 16
    share = slots // groups
    from_waves = prev is None and own.shape[0] == events * chans
    n_prev = 0 if prev is None else prev.shape[0]
    total = n_prev + len(rounds)
    kernel = make_kernel(events, chans, pad, length, slots, groups, share, rounds, n_prev, from_waves, final)
    smem = pl.BlockSpec(memory_space=pltpu.SMEM)
    vmem = pl.BlockSpec(memory_space=pltpu.VMEM)
    inputs = [pairs, counts, sid, own, *partners, fwd]
    if final:
        inputs.append(inv)
        out_shape = (jax.ShapeDtypeStruct((total, share, lags), jnp.float32),
                     jax.ShapeDtypeStruct((groups - 1, total, share, lags), jnp.bfloat16))
    else:
        out_shape = (jax.ShapeDtypeStruct((total, slots, 2 * length), jnp.bfloat16),)
        if from_waves:
            out_shape += (jax.ShapeDtypeStruct((events * pad, 2 * length), jnp.bfloat16),)
    if prev is not None:
        inputs.append(prev)
    scratch = [
        pltpu.VMEM((events * chans, length), jnp.float32),
        pltpu.VMEM((events * pad, length), jnp.float32),
        pltpu.VMEM((events * pad, 2 * length), jnp.float32),
        pltpu.VMEM((events * pad, 2 * length), jnp.float32),
        pltpu.VMEM((slots, 2 * length), jnp.float32),
    ]
    if final:
        scratch.append(pltpu.VMEM((total * slots, 2 * length), jnp.bfloat16))
    return pl.pallas_call(
        kernel,
        out_shape=out_shape,
        in_specs=[smem, smem, smem] + [vmem] * (len(inputs) - 3),
        out_specs=tuple(vmem for _ in out_shape),
        scratch_shapes=scratch,
    )(*inputs)


def station_sum(keep, send, groups):
    total = keep
    for j in range(1, groups):
        perm = [(s, s ^ j) for s in range(groups)]
        total = total + lax.ppermute(send[j - 1], "station", perm).astype(jnp.float32)
    return total


def shards(waveforms, pair_lists, pair_counts):
    events, stations, comps, length = waveforms.shape
    groups = lax.axis_size("station")
    rounds, slots, _ = pair_lists.shape
    chans = stations * comps
    fwd_np, inv_np = half_tables(length, stations * groups * comps, LAGS)
    fwd = jnp.asarray(fwd_np)
    inv = jnp.asarray(inv_np)
    stored = jnp.transpose(waveforms, (0, 2, 1, 3))
    flat = stored.reshape(events * chans, length)
    sid = lax.axis_index("station").astype(jnp.int32).reshape(1)
    pairs = jnp.transpose(pair_lists, (0, 2, 1))
    counts = pair_counts.reshape(-1)
    partners = {q: swapped(stored, "region", q).reshape(events * chans, length)
                for q in reversed(range(rounds))}
    crosses, spec = rounds_call(pairs, counts, sid, flat, [partners[0]], fwd, inv,
                                [0], events, chans, slots, groups)
    rest = list(range(1, rounds))
    keep, send = rounds_call(pairs, counts, sid, spec, [partners[q] for q in rest], fwd, inv,
                             rest, events, chans, slots, groups, prev=crosses, final=True)
    return station_sum(keep, send, groups)


def solution(mesh):
    return jax.shard_map(
        shards,
        mesh=mesh,
        in_specs=(P("region", "station", None, None), P(None, "region", None), P(None, "region")),
        out_specs=P(None, ("region", "station"), None),
        check_vma=False,
    )
```

```python
import math

import ml_dtypes
import numpy as np

import jax
import jax.numpy as jnp
from jax import lax
from jax.experimental import pallas as pl
from jax.experimental.pallas import tpu as pltpu
from jax.sharding import PartitionSpec as P

EPS = 1e-06
LAGS = 256


def swapped(block, axis, bit):
    count = lax.axis_size(axis)
    route = []
    for low in range(count):
        high = low | 1 << bit
        if high != low and high < count:
            route += [(low, high), (high, low)]
    return lax.ppermute(block, axis, route)


def half_tables(length, channels, lags):
    period = 2 * length
    half = period // 2
    step = np.float32(2.0 * math.pi / period)
    times = np.arange(length, dtype=np.int64)[:, None]
    freqs = np.arange(half, dtype=np.int64)[None, :]
    angle = step * ((times * freqs) % period).astype(np.float32)
    fwd = np.concatenate([np.cos(angle), -np.sin(angle)], axis=1).astype(np.float32)
    fwd[:, half] = np.where(times[:, 0] % 2 == 0, 1.0, -1.0)
    fwd = fwd.astype(ml_dtypes.bfloat16)

    factor = np.float32(1.0 / (period * math.sqrt(channels * length)))
    rows = np.arange(half, dtype=np.int64)[:, None]
    lagged = np.arange(lags, dtype=np.int64)[None, :] - lags // 2
    angle = step * ((rows * lagged) % period).astype(np.float32)
    cos_t = (np.cos(angle).astype(np.float32) * factor).astype(ml_dtypes.bfloat16).astype(np.float32)
    sin_t = ((-np.sin(angle)).astype(np.float32) * factor).astype(ml_dtypes.bfloat16).astype(np.float32)
    inv = np.zeros((period, lags), np.float32)
    inv[0] = cos_t[0]
    inv[1:half] = 2.0 * cos_t[1:]
    nyq_angle = step * ((half * lagged[0]) % period).astype(np.float32)
    inv[half] = (np.cos(nyq_angle).astype(np.float32) * factor).astype(ml_dtypes.bfloat16).astype(np.float32)
    inv[half + 1:] = 2.0 * sin_t[1:]
    return fwd, inv.astype(ml_dtypes.bfloat16)


def make_kernel(events, chans, pad, length, slots, groups, share, rounds, n_prev, from_waves, final):
    half = length
    n_part = len(rounds)
    total_rounds = n_prev + n_part

    def kernel(*refs):
        pl_ref, cnt_ref, sid_ref, own_ref = refs[:4]
        part_refs = refs[4:4 + n_part]
        rest = list(refs[4 + n_part:])
        f_ref = rest.pop(0)
        g_ref = rest.pop(0) if final else None
        prev_ref = rest.pop(0) if n_prev else None
        if final:
            keep_ref, send_ref = rest.pop(0), rest.pop(0)
        else:
            xout = rest.pop(0)
            spec_out = rest.pop(0) if from_waves else None
        nscr, xpad, specl, specp, cross = rest[:5]
        allx = rest[5] if final else None

        def spectra(w_ref, spec_ref):
            x = w_ref[...].astype(jnp.float32)
            x = x - jnp.mean(x, axis=-1, keepdims=True)
            x = x * lax.rsqrt(jnp.mean(x * x, axis=-1, keepdims=True) + EPS)
            nscr[...] = x
            for e in range(events):
                xpad[e * pad:e * pad + chans, :] = nscr[e * chans:(e + 1) * chans, :]
            xb = xpad[...].astype(jnp.bfloat16)
            spec = jnp.dot(xb, f_ref[...], preferred_element_type=jnp.float32)
            spec_ref[...] = spec.astype(jnp.bfloat16).astype(jnp.float32)

        xpad[...] = jnp.zeros(xpad.shape, jnp.float32)
        if from_waves:
            spectra(own_ref, specl)
            spec_out[...] = specl[...].astype(jnp.bfloat16)
        else:
            specl[...] = own_ref[...].astype(jnp.float32)
            for n in range(n_prev):
                if final:
                    allx[n * slots:(n + 1) * slots, :] = prev_ref[n]
                else:
                    xout[n] = prev_ref[n]

        sid = sid_ref[0]
        lane = lax.broadcasted_iota(jnp.int32, (1, 128), 1)
        for n, q in enumerate(rounds):
            spectra(part_refs[n], specp)
            for r in range(slots):
                slot = (sid ^ (r // share)) * share + r % share
                a = jnp.minimum(jnp.maximum(pl_ref[q, 0, slot], 0), events - 1)
                b = jnp.minimum(jnp.maximum(pl_ref[q, 1, slot], 0), events - 1)
                left = specl[pl.ds(pl.multiple_of(a * pad, pad), pad), :]
                right = specp[pl.ds(pl.multiple_of(b * pad, pad), pad), :]
                lr, li = left[:, :half], left[:, half:]
                rr, ri = right[:, :half], right[:, half:]
                pp = lr * rr
                qq = li * ri
                re = jnp.sum(pp + qq, axis=0, keepdims=True)
                im = jnp.sum(lr * ri - li * rr, axis=0, keepdims=True)
                p0 = jnp.sum(pp[:, :128], axis=0, keepdims=True)
                q0 = jnp.sum(qq[:, :128], axis=0, keepdims=True)
                cross[r:r + 1, 0:128] = jnp.where(lane == 0, p0, re[:, :128])
                cross[r:r + 1, 128:half] = re[:, 128:]
                cross[r:r + 1, half:half + 128] = jnp.where(lane == 0, q0, im[:, :128])
                cross[r:r + 1, half + 128:] = im[:, 128:]
            cb = cross[...].astype(jnp.bfloat16)
            if final:
                allx[(n_prev + n) * slots:(n_prev + n + 1) * slots, :] = cb
            else:
                xout[n_prev + n] = cb

        if final:
            corr = jnp.dot(allx[...], g_ref[...], preferred_element_type=jnp.float32)
            rows = lax.broadcasted_iota(jnp.int32, corr.shape, 0)
            rnd = rows // slots
            rr_ = rows % slots
            slot_of = (sid ^ (rr_ // share)) * share + rr_ % share
            limit = jnp.zeros(corr.shape, jnp.int32)
            for q in range(total_rounds):
                limit = jnp.where(rnd == q, cnt_ref[q], limit)
            corr = jnp.where(slot_of < limit, corr, 0.0)
            for q in range(total_rounds):
                keep_ref[q] = corr[q * slots:q * slots + share]
                for j in range(1, groups):
                    lo = q * slots + j * share
                    send_ref[j - 1, q] = corr[lo:lo + share].astype(jnp.bfloat16)

    return kernel


def rounds_call(pairs, counts, sid, own, partners, fwd, inv, rounds, events, chans, slots, groups,
                prev=None, final=False):
    length = fwd.shape[0]
    lags = inv.shape[1]
    pad = 16
    share = slots // groups
    from_waves = prev is None and own.shape[0] == events * chans
    n_prev = 0 if prev is None else prev.shape[0]
    total = n_prev + len(rounds)
    kernel = make_kernel(events, chans, pad, length, slots, groups, share, rounds, n_prev, from_waves, final)
    smem = pl.BlockSpec(memory_space=pltpu.SMEM)
    vmem = pl.BlockSpec(memory_space=pltpu.VMEM)
    inputs = [pairs, counts, sid, own, *partners, fwd]
    if final:
        inputs.append(inv)
        out_shape = (jax.ShapeDtypeStruct((total, share, lags), jnp.float32),
                     jax.ShapeDtypeStruct((groups - 1, total, share, lags), jnp.bfloat16))
    else:
        out_shape = (jax.ShapeDtypeStruct((total, slots, 2 * length), jnp.bfloat16),)
        if from_waves:
            out_shape += (jax.ShapeDtypeStruct((events * pad, 2 * length), jnp.bfloat16),)
    if prev is not None:
        inputs.append(prev)
    scratch = [
        pltpu.VMEM((events * chans, length), jnp.float32),
        pltpu.VMEM((events * pad, length), jnp.float32),
        pltpu.VMEM((events * pad, 2 * length), jnp.float32),
        pltpu.VMEM((events * pad, 2 * length), jnp.float32),
        pltpu.VMEM((slots, 2 * length), jnp.float32),
    ]
    if final:
        scratch.append(pltpu.VMEM((total * slots, 2 * length), jnp.bfloat16))
    return pl.pallas_call(
        kernel,
        out_shape=out_shape,
        in_specs=[smem, smem, smem] + [vmem] * (len(inputs) - 3),
        out_specs=tuple(vmem for _ in out_shape),
        scratch_shapes=scratch,
    )(*inputs)


def station_sum(keep, send, groups):
    total = keep
    order = [j for j in range(1, groups) if j & (groups // 2)] + [j for j in range(1, groups) if not j & (groups // 2)]
    for j in order:
        perm = [(s, s ^ j) for s in range(groups)]
        total = total + lax.ppermute(send[j - 1], "station", perm).astype(jnp.float32)
    return total


def shards(waveforms, pair_lists, pair_counts):
    events, stations, comps, length = waveforms.shape
    groups = lax.axis_size("station")
    rounds, slots, _ = pair_lists.shape
    chans = stations * comps
    fwd_np, inv_np = half_tables(length, stations * groups * comps, LAGS)
    fwd = jnp.asarray(fwd_np)
    inv = jnp.asarray(inv_np)
    stored = jnp.transpose(waveforms, (0, 2, 1, 3))
    flat = stored.reshape(events * chans, length)
    sid = lax.axis_index("station").astype(jnp.int32).reshape(1)
    pairs = jnp.transpose(pair_lists, (0, 2, 1))
    counts = pair_counts.reshape(-1)
    partners = {q: swapped(stored, "region", q).reshape(events * chans, length)
                for q in reversed(range(rounds))}
    crosses, spec = rounds_call(pairs, counts, sid, flat, [partners[0]], fwd, inv,
                                [0], events, chans, slots, groups)
    rest = list(range(1, rounds))
    keep, send = rounds_call(pairs, counts, sid, spec, [partners[q] for q in rest], fwd, inv,
                             rest, events, chans, slots, groups, prev=crosses, final=True)
    return station_sum(keep, send, groups)


def solution(mesh):
    return jax.shard_map(
        shards,
        mesh=mesh,
        in_specs=(P("region", "station", None, None), P(None, "region", None), P(None, "region")),
        out_specs=P(None, ("region", "station"), None),
        check_vma=False,
    )
```
